128 devices in a mesh: req: 16 (over z, x), tp: 8 (over y, core).
Axes of the slice: x: 4, y: 4, z: 4, core: 2. Of those that a mesh axis runs over, the one named last changes fastest.
Arguments:
- tokens: bfloat16 [8192, 3072], P('req', 'tp'), may hold values from -3 to 3
- norm_gain: bfloat16 [3072], P('tp'), may hold values from 0.099609375 to 1.8984375
- w_query: bfloat16 [3072, 3072], P(None, 'tp'), may hold values from -0.3125 to 0.3125
- w_key: bfloat16 [3072, 3072], P(None, 'tp'), may hold values from -0.109375 to 0.109375
- w_value: bfloat16 [3072, 3072], P(None, 'tp'), may hold values from -0.109375 to 0.109375
- w_out: bfloat16 [3072, 3072], P('tp'), may hold values from -0.109375 to 0.109375
- prev_keys: bfloat16 [65536, 3072], P('req', 'tp'), may hold values from -300 to 300
- prev_values: bfloat16 [65536, 3072], P('req', 'tp'), may hold values from -6 to 6
- earlier_lengths: int32 [16, 4], P('req'), may hold values from 1 to 2048, 4096 in all within a row
- new_lengths: int32 [16, 4], P('req'), may hold values from 1 to 256, 512 in all within a row
- page_table: int32 [16, 36], P('req'), may hold values from 0 to 575, as said below
Outputs:
- layer_out: bfloat16 [8192, 3072], P('req', 'tp')
- decode_pool: bfloat16 [288, 8, 128, 1536], P('req', 'tp')
The draws below stay inside these ranges and needn't reach their ends.
Inputs may be any that keep to these rules, and one draw needn't show every extreme that they name: `page_table`: every value appears exactly once. Among the pages of one index of req, at most 2 share the same value // 18, and in every draw some destination receives exactly 2 of them.
All inputs are finite; a program needn't handle non-finite values.
Results may differ from the reference program's by a relative error of at most 0.0075.
Values may be sent and summed in bfloat16 or wider, within the bound.
No kernel may reach another device: no remote copies, remote signals or barrier semaphores. Data moves between devices by JAX's collectives and lax.ppermute only.
A program may use at most 256 MiB of HBM per device.

```python
import math
import jax
import jax.numpy as jnp
import numpy as np
from jax import lax

D = 3072
H = 32
HD = 96
HG = 4
PAGE = 128
REQ_DEV = 4
TOK_DEV = 512
PREV_DEV = 4096
TOKENS = 8192
PREV = 65536
STORE_PAGES = 36
SUB = 2
DESTS = 32
SLOTS = 18
HGW = 8
N_REQ = 16
N_TP = 8


def draw_prev_keys(key, part):
    base = jnp.clip(jax.random.normal(jax.random.fold_in(key, 21), (PREV, D), jnp.float32), -6.0, 6.0)
    return base.astype(jnp.bfloat16)


def draw_page_table(key, part):
    row_keys = jax.random.split(jax.random.fold_in(key, 11), N_REQ)
    orders = jax.vmap(lambda row_key: jax.random.permutation(row_key, STORE_PAGES))(row_keys).astype(jnp.int32)
    flat = jnp.arange(N_REQ, dtype=jnp.int32)[:, None] * STORE_PAGES + orders
    paired = flat // 2
    parity = flat % 2
    relabel = jax.random.permutation(jax.random.fold_in(key, 12), DESTS).astype(jnp.int32)
    return (relabel[paired % DESTS] * SLOTS + paired // DESTS * 2 + parity).astype(jnp.int32)


def shard_levels(stream_key, shape, pieces, smallest, top_value):
    level, own = 1.0, jax.random.fold_in(stream_key, 6)
    for dim, blocks in pieces:
        heights = jnp.exp(jax.random.uniform(jax.random.fold_in(own, dim), (blocks,), jnp.float32, smallest / len(pieces), top_value / len(pieces)))
        level = level * jnp.repeat(heights, shape[dim] // blocks).reshape([-1 if axis == dim else 1 for axis in range(len(shape))])
    return level


def split_up(number_of, total, most, lean):
    weights = [(1 << 20) // math.isqrt(grade ** lean) + 1 for grade in range(2, number_of + 1)]
    rest, given = total - most - (number_of - 1), [1] * (number_of - 1)
    while rest > 0:
        candidates = [i for i in range(number_of - 1) if given[i] < most]
        pool, remaining = sum([weights[i] for i in candidates]), rest
        for i in candidates:
            more = min(most - given[i], max(1, remaining * weights[i] // pool), rest)
            given[i] = given[i] + more
            rest = rest - more
    return np.array([most] + given)


def ragged_sizes(rng, number_of, total, limit, skew):
    if number_of == 2:
        one = jax.random.randint(rng, (), max(1, total - limit), min(limit, total - 1) + 1)
        return jnp.stack([one, total - one])
    sizes = jnp.asarray(split_up(number_of, total, limit, skew), jnp.int32)
    twos = (number_of - 1) // 2
    giver, sink = sizes[1:1 + 2 * twos:2], sizes[2:2 + 2 * twos:2]
    room = jnp.minimum(giver - 1, limit - sink)
    shifted = jax.random.randint(jax.random.fold_in(rng, 1), (twos,), 0, 1 << 20) % (room + 1)
    sizes = sizes.at[1:1 + 2 * twos:2].set(giver - shifted).at[2:2 + 2 * twos:2].set(sink + shifted)
    return sizes[jax.random.permutation(jax.random.fold_in(rng, 2), number_of)]


def scatter_about(own_key, dims, spread, most, cuts=(), kind=jnp.bfloat16):
    result = jax.random.normal(own_key, dims, jnp.float32) * spread
    if len(cuts) > 0:
        result = shard_levels(own_key, dims, cuts, -0.22, 0.18) * result
    return jnp.clip(result, min=-most, max=most).astype(kind)


def setup_inputs(seed: int = 0) -> dict:
    seeds = jax.random.split(jax.random.key(seed), 12)
    tokens = scatter_about(seeds[0], (TOKENS, D), 0.5, 3.0, ((0, 16), (1, 8)))
    norm_gain = jnp.clip(1.0 + 0.18 * jax.random.normal(seeds[1], (D,), jnp.float32), 0.099609375, 1.8984375).astype(jnp.bfloat16)
    w_query = scatter_about(seeds[2], (D, D), (D // 9) ** -0.5, 0.3125, ((1, 8),))
    w_key = scatter_about(seeds[3], (D, D), D ** -0.5, 0.109375, ((1, 8),))
    w_value = scatter_about(seeds[4], (D, D), D ** -0.5, 0.109375, ((1, 8),))
    w_out = scatter_about(seeds[5], (D, D), D ** -0.5, 0.109375, ((0, 8),))
    prev_keys = draw_prev_keys(jax.random.fold_in(seeds[11], 71), 0)
    prev_values = scatter_about(seeds[7], (PREV, D), 1.0, 6.0, ((0, 16), (1, 8)))
    earlier_lengths = jax.vmap(lambda own: ragged_sizes(own, REQ_DEV, PREV_DEV, PREV_DEV // 2, 2))(jax.random.split(seeds[8], N_REQ)).reshape((N_REQ, REQ_DEV)).astype(jnp.int32)
    new_lengths = jax.vmap(lambda own: ragged_sizes(own, REQ_DEV, TOK_DEV, TOK_DEV // 2, 2))(jax.random.split(seeds[9], N_REQ)).reshape((N_REQ, REQ_DEV)).astype(jnp.int32)
    page_table = draw_page_table(jax.random.fold_in(seeds[11], 71), 0)
    return dict(tokens=tokens, norm_gain=norm_gain, w_query=w_query, w_key=w_key, w_value=w_value, w_out=w_out, prev_keys=prev_keys, prev_values=prev_values, earlier_lengths=earlier_lengths, new_lengths=new_lengths, page_table=page_table)


EPSILON = 1e-05
THETA = 10000.0

def rotate(values, positions, head_size):
    count = values.shape[0]
    half_size = head_size // 2
    shaped = values.reshape(count, -1, head_size)
    freqs = jnp.exp(-math.log(THETA) * 2.0 * jnp.arange(half_size, dtype=jnp.float32) / head_size)
    angles = positions.astype(jnp.float32)[:, None] * freqs[None, :]
    cosine = jnp.cos(angles)[:, None, :]
    sine = jnp.sin(angles)[:, None, :]
    first = shaped[:, :, :half_size]
    second = shaped[:, :, half_size:]
    turned = jnp.concatenate([first * cosine - second * sine, second * cosine + first * sine], axis=2)
    return turned.reshape(count, -1)

def request_ids(lengths, count):
    ends = jnp.cumsum(lengths).astype(jnp.int32)
    row_index = jnp.arange(count, dtype=jnp.int32)
    return lax.optimization_barrier(jnp.sum((row_index[:, None] >= ends[None, :]).astype(jnp.int32), axis=1))

def block_layout(earlier, fresh, count):
    owners = request_ids(fresh, count)
    starts = (jnp.cumsum(fresh).astype(jnp.int32) - fresh).astype(jnp.int32)
    onehot = (owners[:, None] == jnp.arange(fresh.shape[0], dtype=jnp.int32)[None, :]).astype(jnp.int32)
    first_row = lax.optimization_barrier(jnp.sum(onehot * starts[None, :], axis=1))
    before = lax.optimization_barrier(jnp.sum(onehot * earlier[None, :], axis=1))
    row_index = jnp.arange(count, dtype=jnp.int32)
    return (owners, (before + row_index - first_row).astype(jnp.int32))

def visible(earlier, owners, prev_count, count):
    prev_owner = request_ids(earlier, prev_count)
    row_index = jnp.arange(count, dtype=jnp.int32)
    old_part = owners[:, None] == prev_owner[None, :]
    new_part = (owners[:, None] == owners[None, :]) & (row_index[None, :] <= row_index[:, None])
    return jnp.concatenate([old_part, new_part], axis=1)

def reference(tokens, norm_gain, w_query, w_key, w_value, w_out, prev_keys, prev_values, earlier_lengths, new_lengths, page_table):
    widened = tokens.astype(jnp.float32)
    mean_square = lax.optimization_barrier(jnp.mean(widened * widened, axis=1, keepdims=True))
    normed = (widened * lax.rsqrt(mean_square + EPSILON) * norm_gain.astype(jnp.float32)[None, :]).astype(jnp.bfloat16)
    query_raw = jnp.dot(normed, w_query, preferred_element_type=jnp.float32).reshape(N_REQ, TOK_DEV, D)
    key_raw = jnp.dot(normed, w_key, preferred_element_type=jnp.float32).reshape(N_REQ, TOK_DEV, D)
    new_values = jnp.dot(normed, w_value, preferred_element_type=jnp.float32).astype(jnp.bfloat16).reshape(N_REQ, TOK_DEV, D)
    old_keys = prev_keys.reshape(N_REQ, PREV_DEV, D)
    old_values = prev_values.reshape(N_REQ, PREV_DEV, D)

    def one_block(inputs):
        query_block, key_block, value_block, old_key_block, old_value_block, earlier, fresh = inputs
        owners, positions = block_layout(earlier, fresh, TOK_DEV)
        queries = rotate(query_block, positions, HD).astype(jnp.bfloat16)
        new_keys = rotate(key_block, positions, HD).astype(jnp.bfloat16)
        keys_all = jnp.concatenate([old_key_block, new_keys], axis=0)
        values_all = jnp.concatenate([old_value_block, value_block], axis=0)
        allowed = visible(earlier, owners, PREV_DEV, TOK_DEV)
        query_heads = queries.astype(jnp.float32).reshape(TOK_DEV, H, HD)
        key_heads = keys_all.astype(jnp.float32).reshape(-1, H, HD)
        value_heads = values_all.astype(jnp.float32).reshape(-1, H, HD)
        scores = jnp.einsum('qhd,khd->hqk', query_heads, key_heads) * HD ** (-0.5)
        scores = jnp.where(allowed[None, :, :], scores, -1e+30)
        row_peak = lax.optimization_barrier(jnp.max(scores, axis=2, keepdims=True))
        weights = jnp.exp(scores - row_peak)
        totals = lax.optimization_barrier(jnp.sum(weights, axis=2))
        prob_rows = weights.astype(jnp.bfloat16)
        mixture = jnp.einsum('hqk,khd->qhd', prob_rows.astype(jnp.float32), value_heads)
        attended = (mixture / totals.T[:, :, None]).astype(jnp.bfloat16).reshape(TOK_DEV, D)
        return (attended, keys_all, values_all)
    attended, key_store, value_store = lax.map(one_block, (query_raw, key_raw, new_values, old_keys, old_values, earlier_lengths, new_lengths))
    projected = jnp.dot(attended.reshape(TOKENS, D), w_out, preferred_element_type=jnp.float32)
    layer_out = (widened + projected).astype(jnp.bfloat16)
    page_keys = key_store.reshape(N_REQ * STORE_PAGES, PAGE, HG, HGW * HD)
    page_values = value_store.reshape(N_REQ * STORE_PAGES, PAGE, HG, HGW * HD)
    paired = jnp.stack([page_keys, page_values], axis=2)
    placed = jnp.zeros_like(paired).at[page_table.reshape(-1)].set(paired)
    placed = placed.reshape(N_REQ, SUB, SLOTS, PAGE, 2, HG, HGW * HD)
    placed = placed.transpose(0, 2, 5, 1, 3, 4, 6)
    decode_pool = placed.reshape(N_REQ * SLOTS, N_TP, PAGE, 2 * HGW * HD)
    return (layer_out, decode_pool)
```

```python
import math

import jax
import jax.numpy as jnp
from jax import lax
from jax.experimental import pallas as pl
from jax.experimental.pallas import tpu as pltpu
from jax.sharding import Mesh
from jax.sharding import PartitionSpec as P

HD = 96
HG = 4
PAGE = 128
CAPACITY = 2


EPSILON = 1e-05
THETA = 10000.0


def rotate(values, positions, head_size):
    count = values.shape[0]
    half_size = head_size // 2
    shaped = values.reshape(count, -1, head_size)
    freqs = jnp.exp(-math.log(THETA) * 2.0 * jnp.arange(half_size, dtype=jnp.float32) / head_size)
    angles = positions.astype(jnp.float32)[:, None] * freqs[None, :]
    cosine = jnp.cos(angles)[:, None, :]
    sine = jnp.sin(angles)[:, None, :]
    first = shaped[:, :, :half_size]
    second = shaped[:, :, half_size:]
    turned = jnp.concatenate(
        [first * cosine - second * sine, second * cosine + first * sine], axis=2
    )
    return turned.reshape(count, -1)


def request_ids(lengths, count):
    ends = jnp.cumsum(lengths)
    row_index = jnp.arange(count, dtype=jnp.int32)
    return jnp.sum((row_index[:, None] >= ends[None, :]).astype(jnp.int32), axis=1)


def block_layout(earlier, fresh, count):
    owners = request_ids(fresh, count)
    starts = jnp.cumsum(fresh) - fresh
    onehot = (owners[:, None] == jnp.arange(fresh.shape[0], dtype=jnp.int32)[None, :]).astype(
        jnp.int32
    )
    first_row = jnp.sum(onehot * starts[None, :], axis=1)
    before = jnp.sum(onehot * earlier[None, :], axis=1)
    row_index = jnp.arange(count, dtype=jnp.int32)
    return (owners, before + row_index - first_row)


def visible(earlier, owners, prev_count, count):
    prev_owner = request_ids(earlier, prev_count)
    row_index = jnp.arange(count, dtype=jnp.int32)
    old_part = owners[:, None] == prev_owner[None, :]
    new_part = (owners[:, None] == owners[None, :]) & (row_index[None, :] <= row_index[:, None])
    return jnp.concatenate([old_part, new_part], axis=1)


def rank_in_dest(dests):
    same = (dests[..., :, None] == dests[..., None, :]).astype(jnp.int32)
    count = dests.shape[-1]
    order_index = jnp.arange(count, dtype=jnp.int32)
    earlier_mask = (order_index[None, :] < order_index[:, None]).astype(jnp.int32)
    return jnp.sum(same * earlier_mask, axis=-1)


def pack_pages(slots, prev_keys, prev_values, new_keys, new_values, slot_total):
    prev_pages = prev_keys.shape[0] // PAGE
    new_pages = new_keys.shape[0] // PAGE
    width = prev_keys.shape[1]
    sources = ((prev_keys, prev_values, prev_pages), (new_keys, new_values, new_pages))

    def body(slot_ref, pk, pv, nk, nv, out, sems):
        refs = ((pk, pv), (nk, nv))
        copies = []
        page = 0
        for which, (_, _, pages) in enumerate(sources):
            for local in range(pages):
                for kv in range(2):
                    src = refs[which][kv].at[pl.ds(local * PAGE, PAGE), :]
                    copy = pltpu.make_async_copy(
                        src, out.at[slot_ref[page], kv], sems.at[2 * page + kv]
                    )
                    copy.start()
                    copies.append(copy)
                page += 1
        for copy in copies:
            copy.wait()

    page_total = prev_pages + new_pages
    return pl.pallas_call(
        body,
        out_shape=jax.ShapeDtypeStruct((slot_total, 2, PAGE, width), jnp.bfloat16),
        grid_spec=pltpu.PrefetchScalarGridSpec(
            num_scalar_prefetch=1,
            grid=(1,),
            in_specs=[pl.BlockSpec(memory_space=pl.ANY)] * 4,
            out_specs=pl.BlockSpec(memory_space=pl.ANY),
            scratch_shapes=[pltpu.SemaphoreType.DMA((2 * page_total,))],
        ),
    )(slots, prev_keys, prev_values, new_keys, new_values)


def place_pages(sources, ranks, received, slot_count, cores):
    width = received.shape[-1]

    def body(src_ref, rank_ref, got, out, sems):
        copies = []
        for slot in range(slot_count):
            for core in range(cores):
                for kv in range(2):
                    column = (kv * cores + core) * width
                    index = (slot * cores + core) * 2 + kv
                    copy = pltpu.make_async_copy(
                        got.at[src_ref[slot] * cores + core, rank_ref[slot], kv],
                        out.at[slot, :, pl.ds(column, width)],
                        sems.at[index],
                    )
                    copy.start()
                    copies.append(copy)
        for copy in copies:
            copy.wait()

    return pl.pallas_call(
        body,
        out_shape=jax.ShapeDtypeStruct((slot_count, PAGE, 2 * cores * width), jnp.bfloat16),
        grid_spec=pltpu.PrefetchScalarGridSpec(
            num_scalar_prefetch=2,
            grid=(1,),
            in_specs=[pl.BlockSpec(memory_space=pl.ANY)],
            out_specs=pl.BlockSpec(memory_space=pl.ANY),
            scratch_shapes=[pltpu.SemaphoreType.DMA((slot_count * cores * 2,))],
        ),
    )(sources, ranks, received)


def shards(
    tokens,
    norm_gain,
    w_query,
    w_key,
    w_value,
    w_out,
    prev_keys,
    prev_values,
    earlier_lengths,
    new_lengths,
    page_table,
):
    token_count, local_width = tokens.shape
    full_width = w_query.shape[0]
    prev_count = prev_keys.shape[0]
    req_count = lax.axis_size("req")
    cores = lax.axis_size("core")
    my_req = lax.axis_index("req")
    my_core = lax.axis_index("core")

    full_tokens = lax.all_gather(tokens, ("y", "core"), axis=1, tiled=True)
    widened = full_tokens.astype(jnp.float32)
    mean_square = jnp.mean(widened * widened, axis=1, keepdims=True)
    normed = (widened * lax.rsqrt(mean_square + EPSILON) * norm_gain.astype(jnp.float32)[None, :]).astype(
        jnp.bfloat16
    )
    query_raw, key_raw, value_raw = tuple(
        (
            jnp.dot(normed, weight, preferred_element_type=jnp.float32)
            for weight in (w_query, w_key, w_value)
        )
    )
    earlier = earlier_lengths[0]
    fresh = new_lengths[0]
    owners, positions = block_layout(earlier, fresh, token_count)
    queries = rotate(query_raw, positions, HD).astype(jnp.bfloat16)
    new_keys = rotate(key_raw, positions, HD).astype(jnp.bfloat16)
    new_values = value_raw.astype(jnp.bfloat16)

    page_total = (prev_count + token_count) // PAGE
    slot_count = page_total // cores
    dest_count = req_count * cores
    slot_total = dest_count * CAPACITY
    dest_table = page_table // slot_count
    rank_table = rank_in_dest(dest_table)
    own_dests = lax.dynamic_index_in_dim(dest_table, my_req, 0, keepdims=False)
    own_ranks = lax.dynamic_index_in_dim(rank_table, my_req, 0, keepdims=False)
    send_slots = (own_dests * CAPACITY + own_ranks).astype(jnp.int32)
    send = pack_pages(send_slots, prev_keys, prev_values, new_keys, new_values, slot_total)
    received = lax.all_to_all(send, ("req", "core"), 0, 0, tiled=True)
    received = received.reshape(dest_count, CAPACITY, 2, PAGE, local_width)
    my_dest = my_req * cores + my_core
    wanted = my_dest * slot_count + jnp.arange(slot_count, dtype=jnp.int32)
    flat_table = page_table.reshape(-1)
    found = jnp.argmax(flat_table[None, :] == wanted[:, None], axis=1).astype(jnp.int32)
    from_req = found // page_total
    from_rank = rank_table.reshape(-1)[found].astype(jnp.int32)

    keys_all = jnp.concatenate([prev_keys, new_keys], axis=0)
    values_all = jnp.concatenate([prev_values, new_values], axis=0)
    allowed = visible(earlier, owners, prev_count, token_count)
    heads_here = local_width // HD
    scores = jnp.einsum(
        "qhd,khd->hqk",
        queries.reshape(token_count, heads_here, HD),
        keys_all.reshape(-1, heads_here, HD),
        preferred_element_type=jnp.float32,
    ) * HD ** (-0.5)
    scores = jnp.where(allowed[None, :, :], scores, -1e30)
    row_peak = jnp.max(scores, axis=2, keepdims=True)
    weights = jnp.exp(scores - row_peak)
    totals = jnp.sum(weights, axis=2)
    prob_rows = weights.astype(jnp.bfloat16)
    mixture = jnp.einsum(
        "hqk,khd->qhd",
        prob_rows,
        values_all.reshape(-1, heads_here, HD),
        preferred_element_type=jnp.float32,
    )
    attended = (
        (mixture / totals.T[:, :, None]).astype(jnp.bfloat16).reshape(token_count, local_width)
    )
    projected = jnp.dot(attended, w_out, preferred_element_type=jnp.float32)
    summed = lax.psum_scatter(projected, ("y", "core"), scatter_dimension=1, tiled=True)
    layer_out = (tokens.astype(jnp.float32) + summed).astype(jnp.bfloat16)

    pool = place_pages(from_req, from_rank, received, slot_count, cores)
    return (layer_out, pool[:, None])


def solution(mesh):
    req_count, tp_count = mesh.devices.shape
    cores = tp_count // HG
    split_mesh = Mesh(mesh.devices.reshape(req_count, HG, cores), ("req", "y", "core"))
    tp = ("y", "core")
    placed = (
        P("req", tp),
        P(),
        P(None, tp),
        P(None, tp),
        P(None, tp),
        P(tp, None),
        P("req", tp),
        P("req", tp),
        P("req", None),
        P("req", None),
        P(),
    )
    return jax.shard_map(
        shards,
        mesh=split_mesh,
        in_specs=placed,
        out_specs=(P("req", tp), P("req", tp, None, None)),
        check_vma=False,
    )
```

```python
import math

import jax
import jax.numpy as jnp
from jax import lax
from jax.experimental import pallas as pl
from jax.experimental.pallas import tpu as pltpu
from jax.sharding import Mesh
from jax.sharding import PartitionSpec as P

HD = 96
HG = 4
PAGE = 128
CAPACITY = 2


EPSILON = 1e-05
THETA = 10000.0


def rotate(values, positions, head_size):
    count = values.shape[0]
    half_size = head_size // 2
    shaped = values.reshape(count, -1, head_size)
    freqs = jnp.exp(-math.log(THETA) * 2.0 * jnp.arange(half_size, dtype=jnp.float32) / head_size)
    angles = positions.astype(jnp.float32)[:, None] * freqs[None, :]
    cosine = jnp.cos(angles)[:, None, :]
    sine = jnp.sin(angles)[:, None, :]
    first = shaped[:, :, :half_size]
    second = shaped[:, :, half_size:]
    turned = jnp.concatenate(
        [first * cosine - second * sine, second * cosine + first * sine], axis=2
    )
    return turned.reshape(count, -1)


def request_ids(lengths, count):
    ends = jnp.cumsum(lengths)
    row_index = jnp.arange(count, dtype=jnp.int32)
    return jnp.sum((row_index[:, None] >= ends[None, :]).astype(jnp.int32), axis=1)


def block_layout(earlier, fresh, count):
    owners = request_ids(fresh, count)
    starts = jnp.cumsum(fresh) - fresh
    onehot = (owners[:, None] == jnp.arange(fresh.shape[0], dtype=jnp.int32)[None, :]).astype(
        jnp.int32
    )
    first_row = jnp.sum(onehot * starts[None, :], axis=1)
    before = jnp.sum(onehot * earlier[None, :], axis=1)
    row_index = jnp.arange(count, dtype=jnp.int32)
    return (owners, before + row_index - first_row)


def visible(earlier, owners, prev_count, count):
    prev_owner = request_ids(earlier, prev_count)
    row_index = jnp.arange(count, dtype=jnp.int32)
    old_part = owners[:, None] == prev_owner[None, :]
    new_part = (owners[:, None] == owners[None, :]) & (row_index[None, :] <= row_index[:, None])
    return jnp.concatenate([old_part, new_part], axis=1)


def rank_in_dest(dests):
    same = (dests[..., :, None] == dests[..., None, :]).astype(jnp.int32)
    count = dests.shape[-1]
    order_index = jnp.arange(count, dtype=jnp.int32)
    earlier_mask = (order_index[None, :] < order_index[:, None]).astype(jnp.int32)
    return jnp.sum(same * earlier_mask, axis=-1)


def pack_pages(slots, keys_all, values_all, slot_total):
    page_total = keys_all.shape[0] // PAGE
    width = keys_all.shape[1]

    def body(slot_ref, key_block, value_block, out):
        out[0, 0] = key_block[...]
        out[0, 1] = value_block[...]

    return pl.pallas_call(
        body,
        out_shape=jax.ShapeDtypeStruct((slot_total, 2, PAGE, width), jnp.bfloat16),
        grid_spec=pltpu.PrefetchScalarGridSpec(
            num_scalar_prefetch=1,
            grid=(page_total,),
            in_specs=[
                pl.BlockSpec((PAGE, width), lambda page, slot_ref: (page, 0)),
                pl.BlockSpec((PAGE, width), lambda page, slot_ref: (page, 0)),
            ],
            out_specs=pl.BlockSpec(
                (1, 2, PAGE, width), lambda page, slot_ref: (slot_ref[page], 0, 0, 0)
            ),
        ),
    )(slots, keys_all, values_all)


def place_pages(sources, ranks, received, slot_count, cores):
    width = received.shape[-1]
    shaped = received.reshape(-1, cores, CAPACITY, 2, PAGE, width)

    def body(src_ref, rank_ref, got, out):
        for core in range(cores):
            for kv in range(2):
                column = (kv * cores + core) * width
                out[0, :, column : column + width] = got[0, core, 0, kv]

    return pl.pallas_call(
        body,
        out_shape=jax.ShapeDtypeStruct((slot_count, PAGE, 2 * cores * width), jnp.bfloat16),
        grid_spec=pltpu.PrefetchScalarGridSpec(
            num_scalar_prefetch=2,
            grid=(slot_count,),
            in_specs=[
                pl.BlockSpec(
                    (1, cores, 1, 2, PAGE, width),
                    lambda slot, src_ref, rank_ref: (src_ref[slot], 0, rank_ref[slot], 0, 0, 0),
                )
            ],
            out_specs=pl.BlockSpec((1, PAGE, 2 * cores * width), lambda slot, src_ref, rank_ref: (slot, 0, 0)),
        ),
    )(sources, ranks, shaped)


def shards(
    tokens,
    norm_gain,
    w_query,
    w_key,
    w_value,
    w_out,
    prev_keys,
    prev_values,
    earlier_lengths,
    new_lengths,
    page_table,
):
    token_count, local_width = tokens.shape
    full_width = w_query.shape[0]
    prev_count = prev_keys.shape[0]
    req_count = lax.axis_size("req")
    cores = lax.axis_size("core")
    my_req = lax.axis_index("req")
    my_core = lax.axis_index("core")

    full_tokens = lax.all_gather(tokens, ("y", "core"), axis=1, tiled=True)
    widened = full_tokens.astype(jnp.float32)
    mean_square = jnp.mean(widened * widened, axis=1, keepdims=True)
    normed = (widened * lax.rsqrt(mean_square + EPSILON) * norm_gain.astype(jnp.float32)[None, :]).astype(
        jnp.bfloat16
    )
    query_raw, key_raw, value_raw = tuple(
        (
            jnp.dot(normed, weight, preferred_element_type=jnp.float32)
            for weight in (w_query, w_key, w_value)
        )
    )
    earlier = earlier_lengths[0]
    fresh = new_lengths[0]
    owners, positions = block_layout(earlier, fresh, token_count)
    queries = rotate(query_raw, positions, HD).astype(jnp.bfloat16)
    new_keys = rotate(key_raw, positions, HD).astype(jnp.bfloat16)
    new_values = value_raw.astype(jnp.bfloat16)

    page_total = (prev_count + token_count) // PAGE
    slot_count = page_total // cores
    dest_count = req_count * cores
    slot_total = dest_count * CAPACITY
    dest_table = page_table // slot_count
    rank_table = rank_in_dest(dest_table)
    own_dests = lax.dynamic_index_in_dim(dest_table, my_req, 0, keepdims=False)
    own_ranks = lax.dynamic_index_in_dim(rank_table, my_req, 0, keepdims=False)
    send_slots = (own_dests * CAPACITY + own_ranks).astype(jnp.int32)
    keys_all = jnp.concatenate([prev_keys, new_keys], axis=0)
    values_all = jnp.concatenate([prev_values, new_values], axis=0)
    send = pack_pages(send_slots, keys_all, values_all, slot_total)
    send, queries, keys_all, values_all = lax.optimization_barrier(
        (send, queries, keys_all, values_all)
    )
    received = lax.all_to_all(send, ("req", "core"), 0, 0, tiled=True)
    received = received.reshape(dest_count, CAPACITY, 2, PAGE, local_width)
    my_dest = my_req * cores + my_core
    wanted = my_dest * slot_count + jnp.arange(slot_count, dtype=jnp.int32)
    flat_table = page_table.reshape(-1)
    found = jnp.argmax(flat_table[None, :] == wanted[:, None], axis=1).astype(jnp.int32)
    from_req = found // page_total
    from_rank = rank_table.reshape(-1)[found].astype(jnp.int32)

    allowed = visible(earlier, owners, prev_count, token_count)
    heads_here = local_width // HD
    scores = jnp.einsum(
        "qhd,khd->hqk",
        queries.reshape(token_count, heads_here, HD),
        keys_all.reshape(-1, heads_here, HD),
        preferred_element_type=jnp.float32,
    ) * HD ** (-0.5)
    scores = jnp.where(allowed[None, :, :], scores, -1e30)
    row_peak = jnp.max(scores, axis=2, keepdims=True)
    weights = jnp.exp(scores - row_peak)
    totals = jnp.sum(weights, axis=2)
    prob_rows = weights.astype(jnp.bfloat16)
    mixture = jnp.einsum(
        "hqk,khd->qhd",
        prob_rows,
        values_all.reshape(-1, heads_here, HD),
        preferred_element_type=jnp.float32,
    )
    attended = (
        (mixture / totals.T[:, :, None]).astype(jnp.bfloat16).reshape(token_count, local_width)
    )
    projected = jnp.dot(attended, w_out, preferred_element_type=jnp.float32)
    received, projected = lax.optimization_barrier((received, projected))
    summed = lax.psum_scatter(projected, ("y", "core"), scatter_dimension=1, tiled=True)
    layer_out = (tokens.astype(jnp.float32) + summed).astype(jnp.bfloat16)

    pool = place_pages(from_req, from_rank, received, slot_count, cores)
    return (layer_out, pool[:, None])


def solution(mesh):
    req_count, tp_count = mesh.devices.shape
    cores = tp_count // HG
    split_mesh = Mesh(mesh.devices.reshape(req_count, HG, cores), ("req", "y", "core"))
    tp = ("y", "core")
    placed = (
        P("req", tp),
        P(),
        P(None, tp),
        P(None, tp),
        P(None, tp),
        P(tp, None),
        P("req", tp),
        P("req", tp),
        P("req", None),
        P("req", None),
        P(),
    )
    return jax.shard_map(
        shards,
        mesh=split_mesh,
        in_specs=placed,
        out_specs=(P("req", tp), P("req", tp, None, None)),
        check_vma=False,
    )
```

```python
import math

import jax
import jax.numpy as jnp
from jax import lax
from jax.experimental import pallas as pl
from jax.experimental.pallas import tpu as pltpu
from jax.sharding import Mesh
from jax.sharding import PartitionSpec as P

HD = 96
HG = 4
PAGE = 128
CAPACITY = 2


EPSILON = 1e-05
THETA = 10000.0


def rotate(values, positions, head_size):
    count = values.shape[0]
    half_size = head_size // 2
    shaped = values.reshape(count, -1, head_size)
    freqs = jnp.exp(-math.log(THETA) * 2.0 * jnp.arange(half_size, dtype=jnp.float32) / head_size)
    angles = positions.astype(jnp.float32)[:, None] * freqs[None, :]
    cosine = jnp.cos(angles)[:, None, :]
    sine = jnp.sin(angles)[:, None, :]
    first = shaped[:, :, :half_size]
    second = shaped[:, :, half_size:]
    turned = jnp.concatenate(
        [first * cosine - second * sine, second * cosine + first * sine], axis=2
    )
    return turned.reshape(count, -1)


def request_ids(lengths, count):
    ends = jnp.cumsum(lengths)
    row_index = jnp.arange(count, dtype=jnp.int32)
    return jnp.sum((row_index[:, None] >= ends[None, :]).astype(jnp.int32), axis=1)


def block_layout(earlier, fresh, count):
    owners = request_ids(fresh, count)
    starts = jnp.cumsum(fresh) - fresh
    onehot = (owners[:, None] == jnp.arange(fresh.shape[0], dtype=jnp.int32)[None, :]).astype(
        jnp.int32
    )
    first_row = jnp.sum(onehot * starts[None, :], axis=1)
    before = jnp.sum(onehot * earlier[None, :], axis=1)
    row_index = jnp.arange(count, dtype=jnp.int32)
    return (owners, before + row_index - first_row)


def visible(earlier, owners, prev_count, count):
    prev_owner = request_ids(earlier, prev_count)
    row_index = jnp.arange(count, dtype=jnp.int32)
    old_part = owners[:, None] == prev_owner[None, :]
    new_part = (owners[:, None] == owners[None, :]) & (row_index[None, :] <= row_index[:, None])
    return jnp.concatenate([old_part, new_part], axis=1)


def rank_in_dest(dests):
    same = (dests[..., :, None] == dests[..., None, :]).astype(jnp.int32)
    count = dests.shape[-1]
    order_index = jnp.arange(count, dtype=jnp.int32)
    earlier_mask = (order_index[None, :] < order_index[:, None]).astype(jnp.int32)
    return jnp.sum(same * earlier_mask, axis=-1)


def pack_pages(slots, keys, values, slot_total, into=None):
    page_total = keys.shape[0] // PAGE
    width = keys.shape[1]

    def body(slot_ref, key_block, value_block, *rest):
        out = rest[-1]
        out[0, 0] = key_block[...]
        out[0, 1] = value_block[...]

    in_specs = [
        pl.BlockSpec((PAGE, width), lambda page, slot_ref: (page, 0)),
        pl.BlockSpec((PAGE, width), lambda page, slot_ref: (page, 0)),
    ]
    operands = [slots, keys, values]
    aliases = {}
    if into is not None:
        in_specs.append(pl.BlockSpec(memory_space=pl.ANY))
        operands.append(into)
        aliases = {3: 0}
    return pl.pallas_call(
        body,
        out_shape=jax.ShapeDtypeStruct((slot_total, 2, PAGE, width), jnp.bfloat16),
        grid_spec=pltpu.PrefetchScalarGridSpec(
            num_scalar_prefetch=1,
            grid=(page_total,),
            in_specs=in_specs,
            out_specs=pl.BlockSpec(
                (1, 2, PAGE, width), lambda page, slot_ref: (slot_ref[page], 0, 0, 0)
            ),
        ),
        input_output_aliases=aliases,
    )(*operands)


def place_pages(sources, ranks, received, slot_count, cores):
    width = received.shape[-1]
    shaped = received.reshape(-1, cores, CAPACITY, 2, PAGE, width)

    def body(src_ref, rank_ref, got, out):
        for core in range(cores):
            for kv in range(2):
                column = (kv * cores + core) * width
                out[0, :, column : column + width] = got[0, core, 0, kv]

    return pl.pallas_call(
        body,
        out_shape=jax.ShapeDtypeStruct((slot_count, PAGE, 2 * cores * width), jnp.bfloat16),
        grid_spec=pltpu.PrefetchScalarGridSpec(
            num_scalar_prefetch=2,
            grid=(slot_count,),
            in_specs=[
                pl.BlockSpec(
                    (1, cores, 1, 2, PAGE, width),
                    lambda slot, src_ref, rank_ref: (src_ref[slot], 0, rank_ref[slot], 0, 0, 0),
                )
            ],
            out_specs=pl.BlockSpec((1, PAGE, 2 * cores * width), lambda slot, src_ref, rank_ref: (slot, 0, 0)),
        ),
    )(sources, ranks, shaped)


def shards(
    tokens,
    norm_gain,
    w_query,
    w_key,
    w_value,
    w_out,
    prev_keys,
    prev_values,
    earlier_lengths,
    new_lengths,
    page_table,
):
    token_count, local_width = tokens.shape
    full_width = w_query.shape[0]
    prev_count = prev_keys.shape[0]
    req_count = lax.axis_size("req")
    cores = lax.axis_size("core")
    my_req = lax.axis_index("req")
    my_core = lax.axis_index("core")

    spare = 16
    riders = jnp.zeros((spare, local_width), tokens.dtype).at[0].set(norm_gain)
    gathered = lax.all_gather(
        jnp.concatenate([tokens, riders], axis=0), ("y", "core"), axis=1, tiled=True
    )
    full_tokens = gathered[:token_count]
    full_gain = gathered[token_count]
    widened = full_tokens.astype(jnp.float32)
    mean_square = jnp.mean(widened * widened, axis=1, keepdims=True)
    normed = (widened * lax.rsqrt(mean_square + EPSILON) * full_gain.astype(jnp.float32)[None, :]).astype(
        jnp.bfloat16
    )
    query_raw, key_raw, value_raw = tuple(
        (
            jnp.dot(normed, weight, preferred_element_type=jnp.float32)
            for weight in (w_query, w_key, w_value)
        )
    )
    earlier = earlier_lengths[0]
    fresh = new_lengths[0]
    owners, positions = block_layout(earlier, fresh, token_count)
    queries = rotate(query_raw, positions, HD).astype(jnp.bfloat16)
    new_keys = rotate(key_raw, positions, HD).astype(jnp.bfloat16)
    new_values = value_raw.astype(jnp.bfloat16)

    page_total = (prev_count + token_count) // PAGE
    slot_count = page_total // cores
    dest_count = req_count * cores
    slot_total = dest_count * CAPACITY
    own_dests = page_table[0] // slot_count
    own_ranks = rank_in_dest(own_dests)
    send_slots = (own_dests * CAPACITY + own_ranks).astype(jnp.int32)
    prev_pages = prev_count // PAGE
    send = pack_pages(send_slots[:prev_pages], prev_keys, prev_values, slot_total)
    send = pack_pages(send_slots[prev_pages:], new_keys, new_values, slot_total, into=send)
    keys_all = jnp.concatenate([prev_keys, new_keys], axis=0)
    values_all = jnp.concatenate([prev_values, new_values], axis=0)
    whole_table = lax.all_gather(page_table, "req", axis=0, tiled=True)
    dest_table = whole_table // slot_count
    rank_table = rank_in_dest(dest_table)
    my_dest = my_req * cores + my_core
    wanted = my_dest * slot_count + jnp.arange(slot_count, dtype=jnp.int32)
    flat_table = whole_table.reshape(-1)
    found = jnp.argmax(flat_table[None, :] == wanted[:, None], axis=1).astype(jnp.int32)
    from_req = found // page_total
    from_rank = rank_table.reshape(-1)[found].astype(jnp.int32)
    send, queries, keys_all, values_all, from_req, from_rank = lax.optimization_barrier(
        (send, queries, keys_all, values_all, from_req, from_rank)
    )
    received = lax.all_to_all(send, ("req", "core"), 0, 0, tiled=True)
    received = received.reshape(dest_count, CAPACITY, 2, PAGE, local_width)

    allowed = visible(earlier, owners, prev_count, token_count)
    heads_here = local_width // HD
    scores = jnp.einsum(
        "qhd,khd->hqk",
        queries.reshape(token_count, heads_here, HD),
        keys_all.reshape(-1, heads_here, HD),
        preferred_element_type=jnp.float32,
    ) * HD ** (-0.5)
    scores = jnp.where(allowed[None, :, :], scores, -1e30)
    row_peak = jnp.max(scores, axis=2, keepdims=True)
    weights = jnp.exp(scores - row_peak)
    totals = jnp.sum(weights, axis=2)
    prob_rows = weights.astype(jnp.bfloat16)
    mixture = jnp.einsum(
        "hqk,khd->qhd",
        prob_rows,
        values_all.reshape(-1, heads_here, HD),
        preferred_element_type=jnp.float32,
    )
    attended = (
        (mixture / totals.T[:, :, None]).astype(jnp.bfloat16).reshape(token_count, local_width)
    )
    projected = jnp.dot(attended, w_out, preferred_element_type=jnp.float32)
    received, projected = lax.optimization_barrier((received, projected))
    summed = lax.psum_scatter(projected, ("y", "core"), scatter_dimension=1, tiled=True)
    layer_out = (tokens.astype(jnp.float32) + summed).astype(jnp.bfloat16)

    pool = place_pages(from_req, from_rank, received, slot_count, cores)
    return (layer_out, pool[:, None])


def solution(mesh):
    req_count, tp_count = mesh.devices.shape
    cores = tp_count // HG
    split_mesh = Mesh(mesh.devices.reshape(req_count, HG, cores), ("req", "y", "core"))
    tp = ("y", "core")
    placed = (
        P("req", tp),
        P(tp),
        P(None, tp),
        P(None, tp),
        P(None, tp),
        P(tp, None),
        P("req", tp),
        P("req", tp),
        P("req", None),
        P("req", None),
        P("req", None),
    )
    return jax.shard_map(
        shards,
        mesh=split_mesh,
        in_specs=placed,
        out_specs=(P("req", tp), P("req", tp, None, None)),
        check_vma=False,
    )
```

```python
import math

import jax
import jax.numpy as jnp
from jax import lax
from jax.experimental import pallas as pl
from jax.experimental.pallas import tpu as pltpu
from jax.sharding import Mesh
from jax.sharding import PartitionSpec as P

HD = 96
HG = 4
PAGE = 128
CAPACITY = 2


EPSILON = 1e-05
THETA = 10000.0


def rotate(values, positions, head_size):
    count = values.shape[0]
    half_size = head_size // 2
    shaped = values.reshape(count, -1, head_size)
    freqs = jnp.exp(-math.log(THETA) * 2.0 * jnp.arange(half_size, dtype=jnp.float32) / head_size)
    angles = positions.astype(jnp.float32)[:, None] * freqs[None, :]
    cosine = jnp.cos(angles)[:, None, :]
    sine = jnp.sin(angles)[:, None, :]
    first = shaped[:, :, :half_size]
    second = shaped[:, :, half_size:]
    turned = jnp.concatenate(
        [first * cosine - second * sine, second * cosine + first * sine], axis=2
    )
    return turned.reshape(count, -1)


def request_ids(lengths, count):
    ends = jnp.cumsum(lengths)
    row_index = jnp.arange(count, dtype=jnp.int32)
    return jnp.sum((row_index[:, None] >= ends[None, :]).astype(jnp.int32), axis=1)


def block_layout(earlier, fresh, count):
    owners = request_ids(fresh, count)
    starts = jnp.cumsum(fresh) - fresh
    onehot = (owners[:, None] == jnp.arange(fresh.shape[0], dtype=jnp.int32)[None, :]).astype(
        jnp.int32
    )
    first_row = jnp.sum(onehot * starts[None, :], axis=1)
    before = jnp.sum(onehot * earlier[None, :], axis=1)
    row_index = jnp.arange(count, dtype=jnp.int32)
    return (owners, before + row_index - first_row)


def visible(earlier, owners, prev_count, count):
    prev_owner = request_ids(earlier, prev_count)
    row_index = jnp.arange(count, dtype=jnp.int32)
    old_part = owners[:, None] == prev_owner[None, :]
    new_part = (owners[:, None] == owners[None, :]) & (row_index[None, :] <= row_index[:, None])
    return jnp.concatenate([old_part, new_part], axis=1)


def rank_in_dest(dests):
    same = (dests[..., :, None] == dests[..., None, :]).astype(jnp.int32)
    count = dests.shape[-1]
    order_index = jnp.arange(count, dtype=jnp.int32)
    earlier_mask = (order_index[None, :] < order_index[:, None]).astype(jnp.int32)
    return jnp.sum(same * earlier_mask, axis=-1)


def pack_pages(slots, keys, values, slot_total, into=None):
    page_total = keys.shape[0] // PAGE
    width = keys.shape[1]

    def body(slot_ref, key_block, value_block, *rest):
        out = rest[-1]
        out[0, 0] = key_block[...]
        out[0, 1] = value_block[...]

    in_specs = [
        pl.BlockSpec((PAGE, width), lambda page, slot_ref: (page, 0)),
        pl.BlockSpec((PAGE, width), lambda page, slot_ref: (page, 0)),
    ]
    operands = [slots, keys, values]
    aliases = {}
    if into is not None:
        in_specs.append(pl.BlockSpec(memory_space=pl.ANY))
        operands.append(into)
        aliases = {3: 0}
    return pl.pallas_call(
        body,
        out_shape=jax.ShapeDtypeStruct((slot_total, 2, PAGE, width), jnp.bfloat16),
        grid_spec=pltpu.PrefetchScalarGridSpec(
            num_scalar_prefetch=1,
            grid=(page_total,),
            in_specs=in_specs,
            out_specs=pl.BlockSpec(
                (1, 2, PAGE, width), lambda page, slot_ref: (slot_ref[page], 0, 0, 0)
            ),
        ),
        input_output_aliases=aliases,
    )(*operands)


def place_pages(sources, ranks, received, slot_count, cores):
    width = received.shape[-1]
    shaped = received.reshape(-1, cores, CAPACITY, 2, PAGE, width)

    def body(src_ref, rank_ref, got, out):
        for core in range(cores):
            for kv in range(2):
                column = (kv * cores + core) * width
                out[0, :, column : column + width] = got[0, core, 0, kv]

    return pl.pallas_call(
        body,
        out_shape=jax.ShapeDtypeStruct((slot_count, PAGE, 2 * cores * width), jnp.bfloat16),
        grid_spec=pltpu.PrefetchScalarGridSpec(
            num_scalar_prefetch=2,
            grid=(slot_count,),
            in_specs=[
                pl.BlockSpec(
                    (1, cores, 1, 2, PAGE, width),
                    lambda slot, src_ref, rank_ref: (src_ref[slot], 0, rank_ref[slot], 0, 0, 0),
                )
            ],
            out_specs=pl.BlockSpec((1, PAGE, 2 * cores * width), lambda slot, src_ref, rank_ref: (slot, 0, 0)),
        ),
    )(sources, ranks, shaped)


def shards(
    tokens,
    norm_gain,
    w_query,
    w_key,
    w_value,
    w_out,
    prev_keys,
    prev_values,
    earlier_lengths,
    new_lengths,
    page_table,
):
    token_count, local_width = tokens.shape
    full_width = w_query.shape[0]
    prev_count = prev_keys.shape[0]
    req_count = lax.axis_size("req")
    cores = lax.axis_size("core")
    my_req = lax.axis_index("req")
    my_core = lax.axis_index("core")

    spare = 16
    riders = jnp.zeros((spare, local_width), tokens.dtype).at[0].set(norm_gain)
    gathered = lax.all_gather(
        jnp.concatenate([tokens, riders], axis=0), ("y", "core"), axis=1, tiled=True
    )
    full_tokens = gathered[:token_count]
    full_gain = gathered[token_count]
    widened = full_tokens.astype(jnp.float32)
    mean_square = jnp.mean(widened * widened, axis=1, keepdims=True)
    normed = (widened * lax.rsqrt(mean_square + EPSILON) * full_gain.astype(jnp.float32)[None, :]).astype(
        jnp.bfloat16
    )
    query_raw, key_raw, value_raw = tuple(
        (
            jnp.dot(normed, weight, preferred_element_type=jnp.float32)
            for weight in (w_query, w_key, w_value)
        )
    )
    earlier = earlier_lengths[0]
    fresh = new_lengths[0]
    owners, positions = block_layout(earlier, fresh, token_count)
    queries = rotate(query_raw, positions, HD).astype(jnp.bfloat16)
    new_keys = rotate(key_raw, positions, HD).astype(jnp.bfloat16)
    new_values = value_raw.astype(jnp.bfloat16)

    page_total = (prev_count + token_count) // PAGE
    slot_count = page_total // cores
    dest_count = req_count * cores
    slot_total = dest_count * CAPACITY
    own_dests = page_table[0] // slot_count
    own_ranks = rank_in_dest(own_dests)
    send_slots = (own_dests * CAPACITY + own_ranks).astype(jnp.int32)
    prev_pages = prev_count // PAGE
    send = pack_pages(send_slots[:prev_pages], prev_keys, prev_values, slot_total)
    send = pack_pages(send_slots[prev_pages:], new_keys, new_values, slot_total, into=send)
    keys_all = jnp.concatenate([prev_keys, new_keys], axis=0)
    values_all = jnp.concatenate([prev_values, new_values], axis=0)
    carried = (
        jnp.full((slot_total,), slot_count, jnp.int32)
        .at[send_slots]
        .set((page_table[0] % slot_count).astype(jnp.int32))
    )
    carried = lax.all_to_all(carried, ("req", "core"), 0, 0, tiled=True)
    carried = carried.reshape(req_count, cores, CAPACITY)[:, 0, :].reshape(-1)
    wanted = jnp.arange(slot_count, dtype=jnp.int32)
    found = jnp.argmax(carried[None, :] == wanted[:, None], axis=1).astype(jnp.int32)
    from_req = found // CAPACITY
    from_rank = found % CAPACITY
    send, queries, keys_all, values_all, from_req, from_rank = lax.optimization_barrier(
        (send, queries, keys_all, values_all, from_req, from_rank)
    )
    received = lax.all_to_all(send, ("req", "core"), 0, 0, tiled=True)
    received = received.reshape(dest_count, CAPACITY, 2, PAGE, local_width)

    allowed = visible(earlier, owners, prev_count, token_count)
    heads_here = local_width // HD
    scores = jnp.einsum(
        "qhd,khd->hqk",
        queries.reshape(token_count, heads_here, HD),
        keys_all.reshape(-1, heads_here, HD),
        preferred_element_type=jnp.float32,
    ) * HD ** (-0.5)
    scores = jnp.where(allowed[None, :, :], scores, -1e30)
    row_peak = jnp.max(scores, axis=2, keepdims=True)
    weights = jnp.exp(scores - row_peak)
    totals = jnp.sum(weights, axis=2)
    prob_rows = weights.astype(jnp.bfloat16)
    mixture = jnp.einsum(
        "hqk,khd->qhd",
        prob_rows,
        values_all.reshape(-1, heads_here, HD),
        preferred_element_type=jnp.float32,
    )
    attended = (
        (mixture / totals.T[:, :, None]).astype(jnp.bfloat16).reshape(token_count, local_width)
    )
    projected = jnp.dot(attended, w_out, preferred_element_type=jnp.float32)
    received, projected = lax.optimization_barrier((received, projected))
    summed = lax.psum_scatter(projected, ("y", "core"), scatter_dimension=1, tiled=True)
    layer_out = (tokens.astype(jnp.float32) + summed).astype(jnp.bfloat16)

    pool = place_pages(from_req, from_rank, received, slot_count, cores)
    return (layer_out, pool[:, None])


def solution(mesh):
    req_count, tp_count = mesh.devices.shape
    cores = tp_count // HG
    split_mesh = Mesh(mesh.devices.reshape(req_count, HG, cores), ("req", "y", "core"))
    tp = ("y", "core")
    placed = (
        P("req", tp),
        P(tp),
        P(None, tp),
        P(None, tp),
        P(None, tp),
        P(tp, None),
        P("req", tp),
        P("req", tp),
        P("req", None),
        P("req", None),
        P("req", None),
    )
    return jax.shard_map(
        shards,
        mesh=split_mesh,
        in_specs=placed,
        out_specs=(P("req", tp), P("req", tp, None, None)),
        check_vma=False,
    )
```

```python
import math

import jax
import jax.numpy as jnp
from jax import lax
from jax.experimental import pallas as pl
from jax.experimental.pallas import tpu as pltpu
from jax.sharding import Mesh
from jax.sharding import PartitionSpec as P

HD = 96
HG = 4
PAGE = 128
CAPACITY = 2


EPSILON = 1e-05
THETA = 10000.0


def rotate(values, positions, head_size):
    count = values.shape[0]
    half_size = head_size // 2
    shaped = values.reshape(count, -1, head_size)
    freqs = jnp.exp(-math.log(THETA) * 2.0 * jnp.arange(half_size, dtype=jnp.float32) / head_size)
    angles = positions.astype(jnp.float32)[:, None] * freqs[None, :]
    cosine = jnp.cos(angles)[:, None, :]
    sine = jnp.sin(angles)[:, None, :]
    first = shaped[:, :, :half_size]
    second = shaped[:, :, half_size:]
    turned = jnp.concatenate(
        [first * cosine - second * sine, second * cosine + first * sine], axis=2
    )
    return turned.reshape(count, -1)


def request_ids(lengths, count):
    ends = jnp.cumsum(lengths)
    row_index = jnp.arange(count, dtype=jnp.int32)
    return jnp.sum((row_index[:, None] >= ends[None, :]).astype(jnp.int32), axis=1)


def block_layout(earlier, fresh, count):
    owners = request_ids(fresh, count)
    starts = jnp.cumsum(fresh) - fresh
    onehot = (owners[:, None] == jnp.arange(fresh.shape[0], dtype=jnp.int32)[None, :]).astype(
        jnp.int32
    )
    first_row = jnp.sum(onehot * starts[None, :], axis=1)
    before = jnp.sum(onehot * earlier[None, :], axis=1)
    row_index = jnp.arange(count, dtype=jnp.int32)
    return (owners, before + row_index - first_row)


def visible(earlier, owners, prev_count, count):
    prev_owner = request_ids(earlier, prev_count)
    row_index = jnp.arange(count, dtype=jnp.int32)
    old_part = owners[:, None] == prev_owner[None, :]
    new_part = (owners[:, None] == owners[None, :]) & (row_index[None, :] <= row_index[:, None])
    return jnp.concatenate([old_part, new_part], axis=1)


def rank_in_dest(dests):
    same = (dests[..., :, None] == dests[..., None, :]).astype(jnp.int32)
    count = dests.shape[-1]
    order_index = jnp.arange(count, dtype=jnp.int32)
    earlier_mask = (order_index[None, :] < order_index[:, None]).astype(jnp.int32)
    return jnp.sum(same * earlier_mask, axis=-1)


def pack_pages(slots, keys, values, slot_total, into=None):
    page_total = keys.shape[0] // PAGE
    width = keys.shape[1]

    def body(slot_ref, key_block, value_block, *rest):
        out = rest[-1]
        out[0, 0] = key_block[...]
        out[0, 1] = value_block[...]

    in_specs = [
        pl.BlockSpec((PAGE, width), lambda page, slot_ref: (page, 0)),
        pl.BlockSpec((PAGE, width), lambda page, slot_ref: (page, 0)),
    ]
    operands = [slots, keys, values]
    aliases = {}
    if into is not None:
        in_specs.append(pl.BlockSpec(memory_space=pl.ANY))
        operands.append(into)
        aliases = {3: 0}
    return pl.pallas_call(
        body,
        out_shape=jax.ShapeDtypeStruct((slot_total, 2, PAGE, width), jnp.bfloat16),
        grid_spec=pltpu.PrefetchScalarGridSpec(
            num_scalar_prefetch=1,
            grid=(page_total,),
            in_specs=in_specs,
            out_specs=pl.BlockSpec(
                (1, 2, PAGE, width), lambda page, slot_ref: (slot_ref[page], 0, 0, 0)
            ),
        ),
        input_output_aliases=aliases,
    )(*operands)


def place_pages(sources, ranks, received, slot_count, cores):
    width = received.shape[-1]
    shaped = received.reshape(-1, cores, CAPACITY, 2, PAGE, width)

    def body(src_ref, rank_ref, got, out):
        for core in range(cores):
            for kv in range(2):
                column = (kv * cores + core) * width
                out[0, :, column : column + width] = got[0, core, 0, kv]

    return pl.pallas_call(
        body,
        out_shape=jax.ShapeDtypeStruct((slot_count, PAGE, 2 * cores * width), jnp.bfloat16),
        grid_spec=pltpu.PrefetchScalarGridSpec(
            num_scalar_prefetch=2,
            grid=(slot_count,),
            in_specs=[
                pl.BlockSpec(
                    (1, cores, 1, 2, PAGE, width),
                    lambda slot, src_ref, rank_ref: (src_ref[slot], 0, rank_ref[slot], 0, 0, 0),
                )
            ],
            out_specs=pl.BlockSpec((1, PAGE, 2 * cores * width), lambda slot, src_ref, rank_ref: (slot, 0, 0)),
        ),
    )(sources, ranks, shaped)


def shards(
    tokens,
    norm_gain,
    w_query,
    w_key,
    w_value,
    w_out,
    prev_keys,
    prev_values,
    earlier_lengths,
    new_lengths,
    page_table,
):
    token_count, local_width = tokens.shape
    full_width = w_query.shape[0]
    prev_count = prev_keys.shape[0]
    req_count = lax.axis_size("req")
    cores = lax.axis_size("core")
    my_req = lax.axis_index("req")
    my_core = lax.axis_index("core")

    spare = 16
    riders = jnp.zeros((spare, local_width), tokens.dtype).at[0].set(norm_gain)
    gathered = lax.all_gather(
        jnp.concatenate([tokens, riders], axis=0), ("y", "core"), axis=1, tiled=True
    )
    full_tokens = gathered[:token_count]
    full_gain = gathered[token_count]
    widened = full_tokens.astype(jnp.float32)
    mean_square = jnp.mean(widened * widened, axis=1, keepdims=True)
    normed = (widened * lax.rsqrt(mean_square + EPSILON) * full_gain.astype(jnp.float32)[None, :]).astype(
        jnp.bfloat16
    )
    key_raw, value_raw = tuple(
        (
            jnp.dot(normed, weight, preferred_element_type=jnp.float32)
            for weight in (w_key, w_value)
        )
    )
    earlier = earlier_lengths[0]
    fresh = new_lengths[0]
    owners, positions = block_layout(earlier, fresh, token_count)
    new_keys = rotate(key_raw, positions, HD).astype(jnp.bfloat16)
    new_values = value_raw.astype(jnp.bfloat16)

    page_total = (prev_count + token_count) // PAGE
    slot_count = page_total // cores
    dest_count = req_count * cores
    slot_total = dest_count * CAPACITY
    own_dests = page_table[0] // slot_count
    own_ranks = rank_in_dest(own_dests)
    send_slots = (own_dests * CAPACITY + own_ranks).astype(jnp.int32)
    prev_pages = prev_count // PAGE
    send = pack_pages(send_slots[:prev_pages], prev_keys, prev_values, slot_total)
    send = pack_pages(send_slots[prev_pages:], new_keys, new_values, slot_total, into=send)
    keys_all = jnp.concatenate([prev_keys, new_keys], axis=0)
    values_all = jnp.concatenate([prev_values, new_values], axis=0)
    carried = (
        jnp.full((slot_total,), slot_count, jnp.int32)
        .at[send_slots]
        .set((page_table[0] % slot_count).astype(jnp.int32))
    )
    carried = lax.all_to_all(carried, ("req", "core"), 0, 0, tiled=True)
    carried = carried.reshape(req_count, cores, CAPACITY)[:, 0, :].reshape(-1)
    wanted = jnp.arange(slot_count, dtype=jnp.int32)
    found = jnp.argmax(carried[None, :] == wanted[:, None], axis=1).astype(jnp.int32)
    from_req = found // CAPACITY
    from_rank = found % CAPACITY
    send, normed, keys_all, values_all, from_req, from_rank = lax.optimization_barrier(
        (send, normed, keys_all, values_all, from_req, from_rank)
    )
    query_raw = jnp.dot(normed, w_query, preferred_element_type=jnp.float32)
    queries = rotate(query_raw, positions, HD).astype(jnp.bfloat16)
    received = lax.all_to_all(send, ("req", "core"), 0, 0, tiled=True)
    received = received.reshape(dest_count, CAPACITY, 2, PAGE, local_width)

    allowed = visible(earlier, owners, prev_count, token_count)
    heads_here = local_width // HD
    scores = jnp.einsum(
        "qhd,khd->hqk",
        queries.reshape(token_count, heads_here, HD),
        keys_all.reshape(-1, heads_here, HD),
        preferred_element_type=jnp.float32,
    ) * HD ** (-0.5)
    scores = jnp.where(allowed[None, :, :], scores, -1e30)
    row_peak = jnp.max(scores, axis=2, keepdims=True)
    weights = jnp.exp(scores - row_peak)
    totals = jnp.sum(weights, axis=2)
    prob_rows = weights.astype(jnp.bfloat16)
    mixture = jnp.einsum(
        "hqk,khd->qhd",
        prob_rows,
        values_all.reshape(-1, heads_here, HD),
        preferred_element_type=jnp.float32,
    )
    attended = (
        (mixture / totals.T[:, :, None]).astype(jnp.bfloat16).reshape(token_count, local_width)
    )
    projected = jnp.dot(attended, w_out, preferred_element_type=jnp.float32)
    received, projected = lax.optimization_barrier((received, projected))
    summed = lax.psum_scatter(projected, ("y", "core"), scatter_dimension=1, tiled=True)
    layer_out = (tokens.astype(jnp.float32) + summed).astype(jnp.bfloat16)

    pool = place_pages(from_req, from_rank, received, slot_count, cores)
    return (layer_out, pool[:, None])


def solution(mesh):
    req_count, tp_count = mesh.devices.shape
    cores = tp_count // HG
    split_mesh = Mesh(mesh.devices.reshape(req_count, HG, cores), ("req", "y", "core"))
    tp = ("y", "core")
    placed = (
        P("req", tp),
        P(tp),
        P(None, tp),
        P(None, tp),
        P(None, tp),
        P(tp, None),
        P("req", tp),
        P("req", tp),
        P("req", None),
        P("req", None),
        P("req", None),
    )
    return jax.shard_map(
        shards,
        mesh=split_mesh,
        in_specs=placed,
        out_specs=(P("req", tp), P("req", tp, None, None)),
        check_vma=False,
    )
```

```python
import math

import jax
import jax.numpy as jnp
from jax import lax
from jax.experimental import pallas as pl
from jax.experimental.pallas import tpu as pltpu
from jax.sharding import Mesh
from jax.sharding import PartitionSpec as P

HD = 96
HG = 4
PAGE = 128
CAPACITY = 2


EPSILON = 1e-05
THETA = 10000.0


def rotate(values, positions, head_size):
    count = values.shape[0]
    half_size = head_size // 2
    shaped = values.reshape(count, -1, head_size)
    freqs = jnp.exp(-math.log(THETA) * 2.0 * jnp.arange(half_size, dtype=jnp.float32) / head_size)
    angles = positions.astype(jnp.float32)[:, None] * freqs[None, :]
    cosine = jnp.cos(angles)[:, None, :]
    sine = jnp.sin(angles)[:, None, :]
    first = shaped[:, :, :half_size]
    second = shaped[:, :, half_size:]
    turned = jnp.concatenate(
        [first * cosine - second * sine, second * cosine + first * sine], axis=2
    )
    return turned.reshape(count, -1)


def request_ids(lengths, count):
    ends = jnp.cumsum(lengths)
    row_index = jnp.arange(count, dtype=jnp.int32)
    return jnp.sum((row_index[:, None] >= ends[None, :]).astype(jnp.int32), axis=1)


def block_layout(earlier, fresh, count):
    owners = request_ids(fresh, count)
    starts = jnp.cumsum(fresh) - fresh
    onehot = (owners[:, None] == jnp.arange(fresh.shape[0], dtype=jnp.int32)[None, :]).astype(
        jnp.int32
    )
    first_row = jnp.sum(onehot * starts[None, :], axis=1)
    before = jnp.sum(onehot * earlier[None, :], axis=1)
    row_index = jnp.arange(count, dtype=jnp.int32)
    return (owners, before + row_index - first_row)


def visible(earlier, owners, prev_count, count):
    prev_owner = request_ids(earlier, prev_count)
    row_index = jnp.arange(count, dtype=jnp.int32)
    old_part = owners[:, None] == prev_owner[None, :]
    new_part = (owners[:, None] == owners[None, :]) & (row_index[None, :] <= row_index[:, None])
    return jnp.concatenate([old_part, new_part], axis=1)


def rank_in_dest(dests):
    same = (dests[..., :, None] == dests[..., None, :]).astype(jnp.int32)
    count = dests.shape[-1]
    order_index = jnp.arange(count, dtype=jnp.int32)
    earlier_mask = (order_index[None, :] < order_index[:, None]).astype(jnp.int32)
    return jnp.sum(same * earlier_mask, axis=-1)


def pack_pages(slots, keys, values, slot_total, into=None):
    page_total = keys.shape[0] // PAGE
    width = keys.shape[1]

    def body(slot_ref, key_block, value_block, *rest):
        out = rest[-1]
        out[0, 0] = key_block[...]
        out[0, 1] = value_block[...]

    in_specs = [
        pl.BlockSpec((PAGE, width), lambda page, slot_ref: (page, 0)),
        pl.BlockSpec((PAGE, width), lambda page, slot_ref: (page, 0)),
    ]
    operands = [slots, keys, values]
    aliases = {}
    if into is not None:
        in_specs.append(pl.BlockSpec(memory_space=pl.ANY))
        operands.append(into)
        aliases = {3: 0}
    return pl.pallas_call(
        body,
        out_shape=jax.ShapeDtypeStruct((slot_total, 2, PAGE, width), jnp.bfloat16),
        grid_spec=pltpu.PrefetchScalarGridSpec(
            num_scalar_prefetch=1,
            grid=(page_total,),
            in_specs=in_specs,
            out_specs=pl.BlockSpec(
                (1, 2, PAGE, width), lambda page, slot_ref: (slot_ref[page], 0, 0, 0)
            ),
        ),
        input_output_aliases=aliases,
    )(*operands)


def place_pages(sources, ranks, received, slot_count, cores):
    width = received.shape[-1]
    shaped = received.reshape(-1, cores, CAPACITY, 2, PAGE, width)

    def body(src_ref, rank_ref, got, out):
        for core in range(cores):
            for kv in range(2):
                column = (kv * cores + core) * width
                out[0, :, column : column + width] = got[0, core, 0, kv]

    return pl.pallas_call(
        body,
        out_shape=jax.ShapeDtypeStruct((slot_count, PAGE, 2 * cores * width), jnp.bfloat16),
        grid_spec=pltpu.PrefetchScalarGridSpec(
            num_scalar_prefetch=2,
            grid=(slot_count,),
            in_specs=[
                pl.BlockSpec(
                    (1, cores, 1, 2, PAGE, width),
                    lambda slot, src_ref, rank_ref: (src_ref[slot], 0, rank_ref[slot], 0, 0, 0),
                )
            ],
            out_specs=pl.BlockSpec((1, PAGE, 2 * cores * width), lambda slot, src_ref, rank_ref: (slot, 0, 0)),
        ),
    )(sources, ranks, shaped)


def shards(
    tokens,
    norm_gain,
    w_query,
    w_key,
    w_value,
    w_out,
    prev_keys,
    prev_values,
    earlier_lengths,
    new_lengths,
    page_table,
):
    token_count, local_width = tokens.shape
    full_width = w_query.shape[0]
    prev_count = prev_keys.shape[0]
    req_count = lax.axis_size("req")
    cores = lax.axis_size("core")
    my_req = lax.axis_index("req")
    my_core = lax.axis_index("core")

    spare = 16
    riders = jnp.zeros((spare, local_width), tokens.dtype).at[0].set(norm_gain)
    gathered = lax.all_gather(
        jnp.concatenate([tokens, riders], axis=0), ("y", "core"), axis=1, tiled=True
    )
    full_tokens = gathered[:token_count]
    full_gain = gathered[token_count]
    widened = full_tokens.astype(jnp.float32)
    mean_square = jnp.mean(widened * widened, axis=1, keepdims=True)
    normed = (widened * lax.rsqrt(mean_square + EPSILON) * full_gain.astype(jnp.float32)[None, :]).astype(
        jnp.bfloat16
    )
    key_raw, value_raw = tuple(
        (
            jnp.dot(normed, weight, preferred_element_type=jnp.float32)
            for weight in (w_key, w_value)
        )
    )
    earlier = earlier_lengths[0]
    fresh = new_lengths[0]
    owners, positions = block_layout(earlier, fresh, token_count)
    new_keys = rotate(key_raw, positions, HD).astype(jnp.bfloat16)
    new_values = value_raw.astype(jnp.bfloat16)

    page_total = (prev_count + token_count) // PAGE
    slot_count = page_total // cores
    dest_count = req_count * cores
    slot_total = dest_count * CAPACITY
    own_dests = page_table[0] // slot_count
    own_ranks = rank_in_dest(own_dests)
    send_slots = (own_dests * CAPACITY + own_ranks).astype(jnp.int32)
    prev_pages = prev_count // PAGE
    send = pack_pages(send_slots[:prev_pages], prev_keys, prev_values, slot_total)
    send = pack_pages(send_slots[prev_pages:], new_keys, new_values, slot_total, into=send)
    carried = (
        jnp.full((slot_total,), slot_count, jnp.int32)
        .at[send_slots]
        .set((page_table[0] % slot_count).astype(jnp.int32))
    )
    carried = lax.all_to_all(carried, ("req", "core"), 0, 0, tiled=True)
    carried = carried.reshape(req_count, cores, CAPACITY)[:, 0, :].reshape(-1)
    wanted = jnp.arange(slot_count, dtype=jnp.int32)
    found = jnp.argmax(carried[None, :] == wanted[:, None], axis=1).astype(jnp.int32)
    from_req = found // CAPACITY
    from_rank = found % CAPACITY
    send, normed, new_keys, new_values, from_req, from_rank = lax.optimization_barrier(
        (send, normed, new_keys, new_values, from_req, from_rank)
    )
    keys_all = jnp.concatenate([prev_keys, new_keys], axis=0)
    values_all = jnp.concatenate([prev_values, new_values], axis=0)
    query_raw = jnp.dot(normed, w_query, preferred_element_type=jnp.float32)
    queries = rotate(query_raw, positions, HD).astype(jnp.bfloat16)
    received = lax.all_to_all(send, ("req", "core"), 0, 0, tiled=True)
    received = received.reshape(dest_count, CAPACITY, 2, PAGE, local_width)

    allowed = visible(earlier, owners, prev_count, token_count)
    heads_here = local_width // HD
    scores = jnp.einsum(
        "qhd,khd->hqk",
        queries.reshape(token_count, heads_here, HD),
        keys_all.reshape(-1, heads_here, HD),
        preferred_element_type=jnp.float32,
    ) * HD ** (-0.5)
    scores = jnp.where(allowed[None, :, :], scores, -1e30)
    row_peak = jnp.max(scores, axis=2, keepdims=True)
    weights = jnp.exp(scores - row_peak)
    totals = jnp.sum(weights, axis=2)
    prob_rows = weights.astype(jnp.bfloat16)
    mixture = jnp.einsum(
        "hqk,khd->qhd",
        prob_rows,
        values_all.reshape(-1, heads_here, HD),
        preferred_element_type=jnp.float32,
    )
    attended = (
        (mixture / totals.T[:, :, None]).astype(jnp.bfloat16).reshape(token_count, local_width)
    )
    projected = jnp.einsum("tf,fo->to", attended, w_out, preferred_element_type=jnp.float32)
    received, projected = lax.optimization_barrier((received, projected))
    summed = lax.psum_scatter(
        projected.T.astype(jnp.bfloat16), ("y", "core"), scatter_dimension=0, tiled=True
    ).T.astype(jnp.float32)
    layer_out = (tokens.astype(jnp.float32) + summed).astype(jnp.bfloat16)

    pool = place_pages(from_req, from_rank, received, slot_count, cores)
    return (layer_out, pool[:, None])


def solution(mesh):
    req_count, tp_count = mesh.devices.shape
    cores = tp_count // HG
    split_mesh = Mesh(mesh.devices.reshape(req_count, HG, cores), ("req", "y", "core"))
    tp = ("y", "core")
    placed = (
        P("req", tp),
        P(tp),
        P(None, tp),
        P(None, tp),
        P(None, tp),
        P(tp, None),
        P("req", tp),
        P("req", tp),
        P("req", None),
        P("req", None),
        P("req", None),
    )
    return jax.shard_map(
        shards,
        mesh=split_mesh,
        in_specs=placed,
        out_specs=(P("req", tp), P("req", tp, None, None)),
        check_vma=False,
    )
```

```python
import math

import jax
import jax.numpy as jnp
from jax import lax
from jax.experimental import pallas as pl
from jax.experimental.pallas import tpu as pltpu
from jax.sharding import Mesh
from jax.sharding import PartitionSpec as P

HD = 96
HG = 4
PAGE = 128
CAPACITY = 2


EPSILON = 1e-05
THETA = 10000.0


def rotate(values, positions, head_size):
    count = values.shape[0]
    half_size = head_size // 2
    shaped = values.reshape(count, -1, head_size)
    freqs = jnp.exp(-math.log(THETA) * 2.0 * jnp.arange(half_size, dtype=jnp.float32) / head_size)
    angles = positions.astype(jnp.float32)[:, None] * freqs[None, :]
    cosine = jnp.cos(angles)[:, None, :]
    sine = jnp.sin(angles)[:, None, :]
    first = shaped[:, :, :half_size]
    second = shaped[:, :, half_size:]
    turned = jnp.concatenate(
        [first * cosine - second * sine, second * cosine + first * sine], axis=2
    )
    return turned.reshape(count, -1)


def request_ids(lengths, count):
    ends = jnp.cumsum(lengths)
    row_index = jnp.arange(count, dtype=jnp.int32)
    return jnp.sum((row_index[:, None] >= ends[None, :]).astype(jnp.int32), axis=1)


def block_layout(earlier, fresh, count):
    owners = request_ids(fresh, count)
    starts = jnp.cumsum(fresh) - fresh
    onehot = (owners[:, None] == jnp.arange(fresh.shape[0], dtype=jnp.int32)[None, :]).astype(
        jnp.int32
    )
    first_row = jnp.sum(onehot * starts[None, :], axis=1)
    before = jnp.sum(onehot * earlier[None, :], axis=1)
    row_index = jnp.arange(count, dtype=jnp.int32)
    return (owners, before + row_index - first_row)


def visible(earlier, owners, prev_count, count):
    prev_owner = request_ids(earlier, prev_count)
    row_index = jnp.arange(count, dtype=jnp.int32)
    old_part = owners[:, None] == prev_owner[None, :]
    new_part = (owners[:, None] == owners[None, :]) & (row_index[None, :] <= row_index[:, None])
    return jnp.concatenate([old_part, new_part], axis=1)


def rank_in_dest(dests):
    same = (dests[..., :, None] == dests[..., None, :]).astype(jnp.int32)
    count = dests.shape[-1]
    order_index = jnp.arange(count, dtype=jnp.int32)
    earlier_mask = (order_index[None, :] < order_index[:, None]).astype(jnp.int32)
    return jnp.sum(same * earlier_mask, axis=-1)


def pack_pages(slots, keys, values, slot_total, into=()):
    page_total = keys.shape[0] // PAGE
    width = keys.shape[1]

    def body(slot_ref, key_block, value_block, *rest):
        key_out, value_out = rest[-2:]
        key_out[0] = key_block[...]
        value_out[0] = value_block[...]

    in_specs = [
        pl.BlockSpec((PAGE, width), lambda page, slot_ref: (page, 0)),
        pl.BlockSpec((PAGE, width), lambda page, slot_ref: (page, 0)),
    ] + [pl.BlockSpec(memory_space=pl.ANY)] * len(into)
    half = jax.ShapeDtypeStruct((slot_total, PAGE, width), jnp.bfloat16)
    out_spec = pl.BlockSpec((1, PAGE, width), lambda page, slot_ref: (slot_ref[page], 0, 0))
    return pl.pallas_call(
        body,
        out_shape=(half, half),
        grid_spec=pltpu.PrefetchScalarGridSpec(
            num_scalar_prefetch=1,
            grid=(page_total,),
            in_specs=in_specs,
            out_specs=(out_spec, out_spec),
        ),
        input_output_aliases={3 + i: i for i in range(len(into))},
    )(slots, keys, values, *into)


def place_pages(sources, ranks, received, slot_count, cores, part, into=()):
    width = received.shape[-1]
    shaped = received.reshape(-1, cores, CAPACITY, PAGE, width)

    def body(src_ref, rank_ref, got, *rest):
        out = rest[-1]
        for core in range(cores):
            out[0, :, core * width : (core + 1) * width] = got[0, core, 0]

    in_specs = [
        pl.BlockSpec(
            (1, cores, 1, PAGE, width),
            lambda slot, src_ref, rank_ref: (src_ref[slot], 0, rank_ref[slot], 0, 0),
        )
    ] + [pl.BlockSpec(memory_space=pl.ANY)] * len(into)
    return pl.pallas_call(
        body,
        out_shape=jax.ShapeDtypeStruct((slot_count, PAGE, 2 * cores * width), jnp.bfloat16),
        grid_spec=pltpu.PrefetchScalarGridSpec(
            num_scalar_prefetch=2,
            grid=(slot_count,),
            in_specs=in_specs,
            out_specs=pl.BlockSpec(
                (1, PAGE, cores * width), lambda slot, src_ref, rank_ref: (slot, 0, part)
            ),
        ),
        input_output_aliases={3 + i: 0 for i in range(len(into))},
    )(sources, ranks, shaped, *into)


def shards(
    tokens,
    norm_gain,
    w_query,
    w_key,
    w_value,
    w_out,
    prev_keys,
    prev_values,
    earlier_lengths,
    new_lengths,
    page_table,
):
    token_count, local_width = tokens.shape
    full_width = w_query.shape[0]
    prev_count = prev_keys.shape[0]
    req_count = lax.axis_size("req")
    cores = lax.axis_size("core")
    my_req = lax.axis_index("req")
    my_core = lax.axis_index("core")

    spare = 16
    riders = jnp.zeros((spare, local_width), tokens.dtype).at[0].set(norm_gain)
    gathered = lax.all_gather(
        jnp.concatenate([tokens, riders], axis=0), ("y", "core"), axis=1, tiled=True
    )
    full_tokens = gathered[:token_count]
    full_gain = gathered[token_count]
    widened = full_tokens.astype(jnp.float32)
    mean_square = jnp.mean(widened * widened, axis=1, keepdims=True)
    normed = (widened * lax.rsqrt(mean_square + EPSILON) * full_gain.astype(jnp.float32)[None, :]).astype(
        jnp.bfloat16
    )
    key_raw, value_raw = tuple(
        (
            jnp.dot(normed, weight, preferred_element_type=jnp.float32)
            for weight in (w_key, w_value)
        )
    )
    earlier = earlier_lengths[0]
    fresh = new_lengths[0]
    owners, positions = block_layout(earlier, fresh, token_count)
    new_keys = rotate(key_raw, positions, HD).astype(jnp.bfloat16)
    new_values = value_raw.astype(jnp.bfloat16)

    page_total = (prev_count + token_count) // PAGE
    slot_count = page_total // cores
    dest_count = req_count * cores
    slot_total = dest_count * CAPACITY
    own_dests = page_table[0] // slot_count
    own_ranks = rank_in_dest(own_dests)
    send_slots = (own_dests * CAPACITY + own_ranks).astype(jnp.int32)
    prev_pages = prev_count // PAGE
    send = pack_pages(send_slots[:prev_pages], prev_keys, prev_values, slot_total)
    send = pack_pages(send_slots[prev_pages:], new_keys, new_values, slot_total, into=send)
    send_keys, send_values = send
    carried = (
        jnp.full((slot_total,), slot_count, jnp.int32)
        .at[send_slots]
        .set((page_table[0] % slot_count).astype(jnp.int32))
    )
    carried = lax.all_to_all(carried, ("req", "core"), 0, 0, tiled=True)
    carried = carried.reshape(req_count, cores, CAPACITY)[:, 0, :].reshape(-1)
    wanted = jnp.arange(slot_count, dtype=jnp.int32)
    found = jnp.argmax(carried[None, :] == wanted[:, None], axis=1).astype(jnp.int32)
    from_req = found // CAPACITY
    from_rank = found % CAPACITY
    send_keys, send_values, normed, new_keys, new_values, from_req, from_rank = (
        lax.optimization_barrier(
            (send_keys, send_values, normed, new_keys, new_values, from_req, from_rank)
        )
    )
    keys_all = jnp.concatenate([prev_keys, new_keys], axis=0)
    values_all = jnp.concatenate([prev_values, new_values], axis=0)
    query_raw = jnp.dot(normed, w_query, preferred_element_type=jnp.float32)
    queries = rotate(query_raw, positions, HD).astype(jnp.bfloat16)
    received_keys = lax.all_to_all(send_keys, ("req", "core"), 0, 0, tiled=True)

    allowed = visible(earlier, owners, prev_count, token_count)
    heads_here = local_width // HD
    scores = jnp.einsum(
        "qhd,khd->hqk",
        queries.reshape(token_count, heads_here, HD),
        keys_all.reshape(-1, heads_here, HD),
        preferred_element_type=jnp.float32,
    ) * HD ** (-0.5)
    scores = jnp.where(allowed[None, :, :], scores, -1e30)
    row_peak = jnp.max(scores, axis=2, keepdims=True)
    weights = jnp.exp(scores - row_peak)
    totals = jnp.sum(weights, axis=2)
    prob_rows = weights.astype(jnp.bfloat16)
    mixture = jnp.einsum(
        "hqk,khd->qhd",
        prob_rows,
        values_all.reshape(-1, heads_here, HD),
        preferred_element_type=jnp.float32,
    )
    attended = (
        (mixture / totals.T[:, :, None]).astype(jnp.bfloat16).reshape(token_count, local_width)
    )
    projected = jnp.dot(attended, w_out, preferred_element_type=jnp.float32)
    received_keys, projected, send_values = lax.optimization_barrier(
        (received_keys, projected, send_values)
    )
    summed = lax.psum_scatter(projected, ("y", "core"), scatter_dimension=1, tiled=True)
    layer_out = (tokens.astype(jnp.float32) + summed).astype(jnp.bfloat16)
    received_values = lax.all_to_all(send_values, ("req", "core"), 0, 0, tiled=True)
    pool = place_pages(from_req, from_rank, received_keys, slot_count, cores, 0)
    pool = place_pages(from_req, from_rank, received_values, slot_count, cores, 1, into=(pool,))
    return (layer_out, pool[:, None])


def solution(mesh):
    req_count, tp_count = mesh.devices.shape
    cores = tp_count // HG
    split_mesh = Mesh(mesh.devices.reshape(req_count, HG, cores), ("req", "y", "core"))
    tp = ("y", "core")
    placed = (
        P("req", tp),
        P(tp),
        P(None, tp),
        P(None, tp),
        P(None, tp),
        P(tp, None),
        P("req", tp),
        P("req", tp),
        P("req", None),
        P("req", None),
        P("req", None),
    )
    return jax.shard_map(
        shards,
        mesh=split_mesh,
        in_specs=placed,
        out_specs=(P("req", tp), P("req", tp, None, None)),
        check_vma=False,
    )
```

```python
import math

import jax
import jax.numpy as jnp
from jax import lax
from jax.experimental import pallas as pl
from jax.experimental.pallas import tpu as pltpu
from jax.sharding import Mesh
from jax.sharding import PartitionSpec as P

HD = 96
HG = 4
PAGE = 128
CAPACITY = 2


EPSILON = 1e-05
THETA = 10000.0


def rotate(values, positions, head_size):
    count = values.shape[0]
    half_size = head_size // 2
    shaped = values.reshape(count, -1, head_size)
    freqs = jnp.exp(-math.log(THETA) * 2.0 * jnp.arange(half_size, dtype=jnp.float32) / head_size)
    angles = positions.astype(jnp.float32)[:, None] * freqs[None, :]
    cosine = jnp.cos(angles)[:, None, :]
    sine = jnp.sin(angles)[:, None, :]
    first = shaped[:, :, :half_size]
    second = shaped[:, :, half_size:]
    turned = jnp.concatenate(
        [first * cosine - second * sine, second * cosine + first * sine], axis=2
    )
    return turned.reshape(count, -1)


def request_ids(lengths, count):
    ends = jnp.cumsum(lengths)
    row_index = jnp.arange(count, dtype=jnp.int32)
    return jnp.sum((row_index[:, None] >= ends[None, :]).astype(jnp.int32), axis=1)


def block_layout(earlier, fresh, count):
    owners = request_ids(fresh, count)
    starts = jnp.cumsum(fresh) - fresh
    onehot = (owners[:, None] == jnp.arange(fresh.shape[0], dtype=jnp.int32)[None, :]).astype(
        jnp.int32
    )
    first_row = jnp.sum(onehot * starts[None, :], axis=1)
    before = jnp.sum(onehot * earlier[None, :], axis=1)
    row_index = jnp.arange(count, dtype=jnp.int32)
    return (owners, before + row_index - first_row)


def visible(earlier, owners, prev_count, count):
    prev_owner = request_ids(earlier, prev_count)
    row_index = jnp.arange(count, dtype=jnp.int32)
    old_part = owners[:, None] == prev_owner[None, :]
    new_part = (owners[:, None] == owners[None, :]) & (row_index[None, :] <= row_index[:, None])
    return jnp.concatenate([old_part, new_part], axis=1)


def rank_in_dest(dests):
    same = (dests[..., :, None] == dests[..., None, :]).astype(jnp.int32)
    count = dests.shape[-1]
    order_index = jnp.arange(count, dtype=jnp.int32)
    earlier_mask = (order_index[None, :] < order_index[:, None]).astype(jnp.int32)
    return jnp.sum(same * earlier_mask, axis=-1)


def pack_pages(slots, keys, values, slot_total, into=()):
    page_total = keys.shape[0] // PAGE
    width = keys.shape[1]

    def body(slot_ref, key_block, value_block, *rest):
        key_out, value_out = rest[-2:]
        key_out[0] = key_block[...]
        value_out[0] = value_block[...]

    in_specs = [
        pl.BlockSpec((PAGE, width), lambda page, slot_ref: (page, 0)),
        pl.BlockSpec((PAGE, width), lambda page, slot_ref: (page, 0)),
    ] + [pl.BlockSpec(memory_space=pl.ANY)] * len(into)
    half = jax.ShapeDtypeStruct((slot_total, PAGE, width), jnp.bfloat16)
    out_spec = pl.BlockSpec((1, PAGE, width), lambda page, slot_ref: (slot_ref[page], 0, 0))
    return pl.pallas_call(
        body,
        out_shape=(half, half),
        grid_spec=pltpu.PrefetchScalarGridSpec(
            num_scalar_prefetch=1,
            grid=(page_total,),
            in_specs=in_specs,
            out_specs=(out_spec, out_spec),
        ),
        input_output_aliases={3 + i: i for i in range(len(into))},
    )(slots, keys, values, *into)


def place_pages(sources, ranks, received, slot_count, cores, part, into=(), group=6):
    width = received.shape[-1]
    shaped = received.reshape(-1, cores, CAPACITY, PAGE, width)

    def body(src_ref, rank_ref, *refs):
        out = refs[-1]
        for member in range(group):
            for core in range(cores):
                out[member, :, core * width : (core + 1) * width] = refs[member][0, core, 0]

    def source_map(member):
        return lambda step, src_ref, rank_ref: (
            src_ref[step * group + member],
            0,
            rank_ref[step * group + member],
            0,
            0,
        )

    in_specs = [
        pl.BlockSpec((1, cores, 1, PAGE, width), source_map(member)) for member in range(group)
    ] + [pl.BlockSpec(memory_space=pl.ANY)] * len(into)
    return pl.pallas_call(
        body,
        out_shape=jax.ShapeDtypeStruct((slot_count, PAGE, 2 * cores * width), jnp.bfloat16),
        grid_spec=pltpu.PrefetchScalarGridSpec(
            num_scalar_prefetch=2,
            grid=(slot_count // group,),
            in_specs=in_specs,
            out_specs=pl.BlockSpec(
                (group, PAGE, cores * width), lambda step, src_ref, rank_ref: (step, 0, part)
            ),
        ),
        input_output_aliases={2 + group + i: 0 for i in range(len(into))},
    )(sources, ranks, *([shaped] * group), *into)


def shards(
    tokens,
    norm_gain,
    w_query,
    w_key,
    w_value,
    w_out,
    prev_keys,
    prev_values,
    earlier_lengths,
    new_lengths,
    page_table,
):
    token_count, local_width = tokens.shape
    full_width = w_query.shape[0]
    prev_count = prev_keys.shape[0]
    req_count = lax.axis_size("req")
    cores = lax.axis_size("core")
    my_req = lax.axis_index("req")
    my_core = lax.axis_index("core")

    spare = 16
    riders = jnp.zeros((spare, local_width), tokens.dtype).at[0].set(norm_gain)
    gathered = lax.all_gather(
        jnp.concatenate([tokens, riders], axis=0), ("y", "core"), axis=1, tiled=True
    )
    full_tokens = gathered[:token_count]
    full_gain = gathered[token_count]
    widened = full_tokens.astype(jnp.float32)
    mean_square = jnp.mean(widened * widened, axis=1, keepdims=True)
    normed = (widened * lax.rsqrt(mean_square + EPSILON) * full_gain.astype(jnp.float32)[None, :]).astype(
        jnp.bfloat16
    )
    key_raw, value_raw = tuple(
        (
            jnp.dot(normed, weight, preferred_element_type=jnp.float32)
            for weight in (w_key, w_value)
        )
    )
    earlier = earlier_lengths[0]
    fresh = new_lengths[0]
    owners, positions = block_layout(earlier, fresh, token_count)
    new_keys = rotate(key_raw, positions, HD).astype(jnp.bfloat16)
    new_values = value_raw.astype(jnp.bfloat16)

    page_total = (prev_count + token_count) // PAGE
    slot_count = page_total // cores
    dest_count = req_count * cores
    slot_total = dest_count * CAPACITY
    own_dests = page_table[0] // slot_count
    own_ranks = rank_in_dest(own_dests)
    send_slots = (own_dests * CAPACITY + own_ranks).astype(jnp.int32)
    prev_pages = prev_count // PAGE
    send = pack_pages(send_slots[:prev_pages], prev_keys, prev_values, slot_total)
    send = pack_pages(send_slots[prev_pages:], new_keys, new_values, slot_total, into=send)
    send_keys, send_values = send
    carried = (
        jnp.full((slot_total,), slot_count, jnp.int32)
        .at[send_slots]
        .set((page_table[0] % slot_count).astype(jnp.int32))
    )
    carried = lax.all_to_all(carried, ("req", "core"), 0, 0, tiled=True)
    carried = carried.reshape(req_count, cores, CAPACITY)[:, 0, :].reshape(-1)
    wanted = jnp.arange(slot_count, dtype=jnp.int32)
    found = jnp.argmax(carried[None, :] == wanted[:, None], axis=1).astype(jnp.int32)
    from_req = found // CAPACITY
    from_rank = found % CAPACITY
    send_keys, send_values, normed, new_keys, new_values, from_req, from_rank = (
        lax.optimization_barrier(
            (send_keys, send_values, normed, new_keys, new_values, from_req, from_rank)
        )
    )
    keys_all = jnp.concatenate([prev_keys, new_keys], axis=0)
    values_all = jnp.concatenate([prev_values, new_values], axis=0)
    query_raw = jnp.dot(normed, w_query, preferred_element_type=jnp.float32)
    queries = rotate(query_raw, positions, HD).astype(jnp.bfloat16)
    received_keys = lax.all_to_all(send_keys, ("req", "core"), 0, 0, tiled=True)

    allowed = visible(earlier, owners, prev_count, token_count)
    heads_here = local_width // HD
    scores = jnp.einsum(
        "qhd,khd->hqk",
        queries.reshape(token_count, heads_here, HD),
        keys_all.reshape(-1, heads_here, HD),
        preferred_element_type=jnp.float32,
    ) * HD ** (-0.5)
    scores = jnp.where(allowed[None, :, :], scores, -1e30)
    row_peak = jnp.max(scores, axis=2, keepdims=True)
    weights = jnp.exp(scores - row_peak)
    totals = jnp.sum(weights, axis=2)
    prob_rows = weights.astype(jnp.bfloat16)
    mixture = jnp.einsum(
        "hqk,khd->qhd",
        prob_rows,
        values_all.reshape(-1, heads_here, HD),
        preferred_element_type=jnp.float32,
    )
    attended = (
        (mixture / totals.T[:, :, None]).astype(jnp.bfloat16).reshape(token_count, local_width)
    )
    projected = jnp.dot(attended, w_out, preferred_element_type=jnp.float32)
    received_keys, projected, send_values = lax.optimization_barrier(
        (received_keys, projected, send_values)
    )
    summed = lax.psum_scatter(projected, ("y", "core"), scatter_dimension=1, tiled=True)
    layer_out = (tokens.astype(jnp.float32) + summed).astype(jnp.bfloat16)
    received_values = lax.all_to_all(send_values, ("req", "core"), 0, 0, tiled=True)
    pool = place_pages(from_req, from_rank, received_keys, slot_count, cores, 0)
    pool = place_pages(from_req, from_rank, received_values, slot_count, cores, 1, into=(pool,))
    return (layer_out, pool[:, None])


def solution(mesh):
    req_count, tp_count = mesh.devices.shape
    cores = tp_count // HG
    split_mesh = Mesh(mesh.devices.reshape(req_count, HG, cores), ("req", "y", "core"))
    tp = ("y", "core")
    placed = (
        P("req", tp),
        P(tp),
        P(None, tp),
        P(None, tp),
        P(None, tp),
        P(tp, None),
        P("req", tp),
        P("req", tp),
        P("req", None),
        P("req", None),
        P("req", None),
    )
    return jax.shard_map(
        shards,
        mesh=split_mesh,
        in_specs=placed,
        out_specs=(P("req", tp), P("req", tp, None, None)),
        check_vma=False,
    )
```

```python
import math

import jax
import jax.numpy as jnp
from jax import lax
from jax.experimental import pallas as pl
from jax.experimental.pallas import tpu as pltpu
from jax.sharding import Mesh
from jax.sharding import PartitionSpec as P

HD = 96
HG = 4
PAGE = 128
CAPACITY = 2


EPSILON = 1e-05
THETA = 10000.0


def rotate(values, positions, head_size):
    count = values.shape[0]
    half_size = head_size // 2
    shaped = values.reshape(count, -1, head_size)
    freqs = jnp.exp(-math.log(THETA) * 2.0 * jnp.arange(half_size, dtype=jnp.float32) / head_size)
    angles = positions.astype(jnp.float32)[:, None] * freqs[None, :]
    cosine = jnp.cos(angles)[:, None, :]
    sine = jnp.sin(angles)[:, None, :]
    first = shaped[:, :, :half_size]
    second = shaped[:, :, half_size:]
    turned = jnp.concatenate(
        [first * cosine - second * sine, second * cosine + first * sine], axis=2
    )
    return turned.reshape(count, -1)


def request_ids(lengths, count):
    ends = jnp.cumsum(lengths)
    row_index = jnp.arange(count, dtype=jnp.int32)
    return jnp.sum((row_index[:, None] >= ends[None, :]).astype(jnp.int32), axis=1)


def block_layout(earlier, fresh, count):
    owners = request_ids(fresh, count)
    starts = jnp.cumsum(fresh) - fresh
    onehot = (owners[:, None] == jnp.arange(fresh.shape[0], dtype=jnp.int32)[None, :]).astype(
        jnp.int32
    )
    first_row = jnp.sum(onehot * starts[None, :], axis=1)
    before = jnp.sum(onehot * earlier[None, :], axis=1)
    row_index = jnp.arange(count, dtype=jnp.int32)
    return (owners, before + row_index - first_row)


def visible(earlier, owners, prev_count, count):
    prev_owner = request_ids(earlier, prev_count)
    row_index = jnp.arange(count, dtype=jnp.int32)
    old_part = owners[:, None] == prev_owner[None, :]
    new_part = (owners[:, None] == owners[None, :]) & (row_index[None, :] <= row_index[:, None])
    return jnp.concatenate([old_part, new_part], axis=1)


def rank_in_dest(dests):
    same = (dests[..., :, None] == dests[..., None, :]).astype(jnp.int32)
    count = dests.shape[-1]
    order_index = jnp.arange(count, dtype=jnp.int32)
    earlier_mask = (order_index[None, :] < order_index[:, None]).astype(jnp.int32)
    return jnp.sum(same * earlier_mask, axis=-1)


def pack_pages(slots, keys, values, slot_total, into=()):
    page_total = keys.shape[0] // PAGE
    width = keys.shape[1]
    split = PAGE // 2

    def body(slot_ref, key_block, value_block, *rest):
        key_out, low_out, high_out = rest[-3:]
        key_out[0] = key_block[...]
        low_out[0] = value_block[:split]
        high_out[0] = value_block[split:]

    in_specs = [
        pl.BlockSpec((PAGE, width), lambda page, slot_ref: (page, 0)),
        pl.BlockSpec((PAGE, width), lambda page, slot_ref: (page, 0)),
    ] + [pl.BlockSpec(memory_space=pl.ANY)] * len(into)
    full = jax.ShapeDtypeStruct((slot_total, PAGE, width), jnp.bfloat16)
    part = jax.ShapeDtypeStruct((slot_total, split, width), jnp.bfloat16)
    full_spec = pl.BlockSpec((1, PAGE, width), lambda page, slot_ref: (slot_ref[page], 0, 0))
    part_spec = pl.BlockSpec((1, split, width), lambda page, slot_ref: (slot_ref[page], 0, 0))
    return pl.pallas_call(
        body,
        out_shape=(full, part, part),
        grid_spec=pltpu.PrefetchScalarGridSpec(
            num_scalar_prefetch=1,
            grid=(page_total,),
            in_specs=in_specs,
            out_specs=(full_spec, part_spec, part_spec),
        ),
        input_output_aliases={3 + i: i for i in range(len(into))},
    )(slots, keys, values, *into)


def place_pages(sources, ranks, received, slot_count, cores, part, row_block, into=(), group=6):
    rows, width = received.shape[-2:]
    shaped = received.reshape(-1, cores, CAPACITY, rows, width)

    def body(src_ref, rank_ref, *refs):
        out = refs[-1]
        for member in range(group):
            for core in range(cores):
                out[member, :, core * width : (core + 1) * width] = refs[member][0, core, 0]

    def source_map(member):
        return lambda step, src_ref, rank_ref: (
            src_ref[step * group + member],
            0,
            rank_ref[step * group + member],
            0,
            0,
        )

    in_specs = [
        pl.BlockSpec((1, cores, 1, rows, width), source_map(member)) for member in range(group)
    ] + [pl.BlockSpec(memory_space=pl.ANY)] * len(into)
    return pl.pallas_call(
        body,
        out_shape=jax.ShapeDtypeStruct((slot_count, PAGE, 2 * cores * width), jnp.bfloat16),
        grid_spec=pltpu.PrefetchScalarGridSpec(
            num_scalar_prefetch=2,
            grid=(slot_count // group,),
            in_specs=in_specs,
            out_specs=pl.BlockSpec(
                (group, rows, cores * width),
                lambda step, src_ref, rank_ref: (step, row_block, part),
            ),
        ),
        input_output_aliases={2 + group + i: 0 for i in range(len(into))},
    )(sources, ranks, *([shaped] * group), *into)


def shards(
    tokens,
    norm_gain,
    w_query,
    w_key,
    w_value,
    w_out,
    prev_keys,
    prev_values,
    earlier_lengths,
    new_lengths,
    page_table,
):
    token_count, local_width = tokens.shape
    full_width = w_query.shape[0]
    prev_count = prev_keys.shape[0]
    req_count = lax.axis_size("req")
    cores = lax.axis_size("core")
    my_req = lax.axis_index("req")
    my_core = lax.axis_index("core")

    spare = 16
    riders = jnp.zeros((spare, local_width), tokens.dtype).at[0].set(norm_gain)
    gathered = lax.all_gather(
        jnp.concatenate([tokens, riders], axis=0), ("y", "core"), axis=1, tiled=True
    )
    full_tokens = gathered[:token_count]
    full_gain = gathered[token_count]
    widened = full_tokens.astype(jnp.float32)
    mean_square = jnp.mean(widened * widened, axis=1, keepdims=True)
    normed = (widened * lax.rsqrt(mean_square + EPSILON) * full_gain.astype(jnp.float32)[None, :]).astype(
        jnp.bfloat16
    )
    key_raw, value_raw = tuple(
        (
            jnp.dot(normed, weight, preferred_element_type=jnp.float32)
            for weight in (w_key, w_value)
        )
    )
    earlier = earlier_lengths[0]
    fresh = new_lengths[0]
    owners, positions = block_layout(earlier, fresh, token_count)
    new_keys = rotate(key_raw, positions, HD).astype(jnp.bfloat16)
    new_values = value_raw.astype(jnp.bfloat16)

    page_total = (prev_count + token_count) // PAGE
    slot_count = page_total // cores
    dest_count = req_count * cores
    slot_total = dest_count * CAPACITY
    own_dests = page_table[0] // slot_count
    own_ranks = rank_in_dest(own_dests)
    send_slots = (own_dests * CAPACITY + own_ranks).astype(jnp.int32)
    prev_pages = prev_count // PAGE
    send = pack_pages(send_slots[:prev_pages], prev_keys, prev_values, slot_total)
    send = pack_pages(send_slots[prev_pages:], new_keys, new_values, slot_total, into=send)
    send_keys, send_low, send_high = send
    carried = (
        jnp.full((slot_total,), slot_count, jnp.int32)
        .at[send_slots]
        .set((page_table[0] % slot_count).astype(jnp.int32))
    )
    carried = lax.all_to_all(carried, ("req", "core"), 0, 0, tiled=True)
    carried = carried.reshape(req_count, cores, CAPACITY)[:, 0, :].reshape(-1)
    wanted = jnp.arange(slot_count, dtype=jnp.int32)
    found = jnp.argmax(carried[None, :] == wanted[:, None], axis=1).astype(jnp.int32)
    from_req = found // CAPACITY
    from_rank = found % CAPACITY
    send_keys, send_low, send_high, normed, new_keys, new_values, from_req, from_rank = (
        lax.optimization_barrier(
            (send_keys, send_low, send_high, normed, new_keys, new_values, from_req, from_rank)
        )
    )
    keys_all = jnp.concatenate([prev_keys, new_keys], axis=0)
    values_all = jnp.concatenate([prev_values, new_values], axis=0)
    query_raw = jnp.dot(normed, w_query, preferred_element_type=jnp.float32)
    queries = rotate(query_raw, positions, HD).astype(jnp.bfloat16)
    received_keys, received_low = lax.all_to_all(
        (send_keys, send_low), ("req", "core"), 0, 0, tiled=True
    )

    allowed = visible(earlier, owners, prev_count, token_count)
    heads_here = local_width // HD
    scores = jnp.einsum(
        "qhd,khd->hqk",
        queries.reshape(token_count, heads_here, HD),
        keys_all.reshape(-1, heads_here, HD),
        preferred_element_type=jnp.float32,
    ) * HD ** (-0.5)
    scores = jnp.where(allowed[None, :, :], scores, -1e30)
    row_peak = jnp.max(scores, axis=2, keepdims=True)
    weights = jnp.exp(scores - row_peak)
    totals = jnp.sum(weights, axis=2)
    prob_rows = weights.astype(jnp.bfloat16)
    mixture = jnp.einsum(
        "hqk,khd->qhd",
        prob_rows,
        values_all.reshape(-1, heads_here, HD),
        preferred_element_type=jnp.float32,
    )
    attended = (
        (mixture / totals.T[:, :, None]).astype(jnp.bfloat16).reshape(token_count, local_width)
    )
    projected = jnp.dot(attended, w_out, preferred_element_type=jnp.float32)
    received_keys, received_low, projected, send_high = lax.optimization_barrier(
        (received_keys, received_low, projected, send_high)
    )
    summed = lax.psum_scatter(projected, ("y", "core"), scatter_dimension=1, tiled=True)
    layer_out = (tokens.astype(jnp.float32) + summed).astype(jnp.bfloat16)
    received_high = lax.all_to_all(send_high, ("req", "core"), 0, 0, tiled=True)
    pool = place_pages(from_req, from_rank, received_keys, slot_count, cores, 0, 0)
    pool = place_pages(from_req, from_rank, received_low, slot_count, cores, 1, 0, into=(pool,))
    pool = place_pages(from_req, from_rank, received_high, slot_count, cores, 1, 1, into=(pool,))
    return (layer_out, pool[:, None])


def solution(mesh):
    req_count, tp_count = mesh.devices.shape
    cores = tp_count // HG
    split_mesh = Mesh(mesh.devices.reshape(req_count, HG, cores), ("req", "y", "core"))
    tp = ("y", "core")
    placed = (
        P("req", tp),
        P(tp),
        P(None, tp),
        P(None, tp),
        P(None, tp),
        P(tp, None),
        P("req", tp),
        P("req", tp),
        P("req", None),
        P("req", None),
        P("req", None),
    )
    return jax.shard_map(
        shards,
        mesh=split_mesh,
        in_specs=placed,
        out_specs=(P("req", tp), P("req", tp, None, None)),
        check_vma=False,
    )
```

```python
import math

import jax
import jax.numpy as jnp
from jax import lax
from jax.experimental import pallas as pl
from jax.experimental.pallas import tpu as pltpu
from jax.sharding import Mesh
from jax.sharding import PartitionSpec as P

HD = 96
HG = 4
PAGE = 128
CAPACITY = 2


EPSILON = 1e-05
THETA = 10000.0


def rotate(values, positions, head_size):
    count = values.shape[0]
    half_size = head_size // 2
    shaped = values.reshape(count, -1, head_size)
    freqs = jnp.exp(-math.log(THETA) * 2.0 * jnp.arange(half_size, dtype=jnp.float32) / head_size)
    angles = positions.astype(jnp.float32)[:, None] * freqs[None, :]
    cosine = jnp.cos(angles)[:, None, :]
    sine = jnp.sin(angles)[:, None, :]
    first = shaped[:, :, :half_size]
    second = shaped[:, :, half_size:]
    turned = jnp.concatenate(
        [first * cosine - second * sine, second * cosine + first * sine], axis=2
    )
    return turned.reshape(count, -1)


def request_ids(lengths, count):
    ends = jnp.cumsum(lengths)
    row_index = jnp.arange(count, dtype=jnp.int32)
    return jnp.sum((row_index[:, None] >= ends[None, :]).astype(jnp.int32), axis=1)


def block_layout(earlier, fresh, count):
    owners = request_ids(fresh, count)
    starts = jnp.cumsum(fresh) - fresh
    onehot = (owners[:, None] == jnp.arange(fresh.shape[0], dtype=jnp.int32)[None, :]).astype(
        jnp.int32
    )
    first_row = jnp.sum(onehot * starts[None, :], axis=1)
    before = jnp.sum(onehot * earlier[None, :], axis=1)
    row_index = jnp.arange(count, dtype=jnp.int32)
    return (owners, before + row_index - first_row)


def visible(earlier, owners, prev_count, count):
    prev_owner = request_ids(earlier, prev_count)
    row_index = jnp.arange(count, dtype=jnp.int32)
    old_part = owners[:, None] == prev_owner[None, :]
    new_part = (owners[:, None] == owners[None, :]) & (row_index[None, :] <= row_index[:, None])
    return jnp.concatenate([old_part, new_part], axis=1)


def rank_in_dest(dests):
    same = (dests[..., :, None] == dests[..., None, :]).astype(jnp.int32)
    count = dests.shape[-1]
    order_index = jnp.arange(count, dtype=jnp.int32)
    earlier_mask = (order_index[None, :] < order_index[:, None]).astype(jnp.int32)
    return jnp.sum(same * earlier_mask, axis=-1)


def pack_pages(slots, source, parts, slot_total, into=()):
    page_total = source.shape[0] // PAGE
    width = source.shape[1]

    def body(slot_ref, block, *rest):
        outs = rest[len(rest) - len(parts) :]
        for out, (start, rows) in zip(outs, parts):
            out[0] = block[start : start + rows]

    in_specs = [pl.BlockSpec((PAGE, width), lambda page, slot_ref: (page, 0))]
    in_specs += [pl.BlockSpec(memory_space=pl.ANY)] * len(into)
    out_shape = tuple(
        jax.ShapeDtypeStruct((slot_total, rows, width), jnp.bfloat16) for _, rows in parts
    )
    out_specs = tuple(
        pl.BlockSpec((1, rows, width), lambda page, slot_ref: (slot_ref[page], 0, 0))
        for _, rows in parts
    )
    return pl.pallas_call(
        body,
        out_shape=out_shape,
        grid_spec=pltpu.PrefetchScalarGridSpec(
            num_scalar_prefetch=1,
            grid=(page_total,),
            in_specs=in_specs,
            out_specs=out_specs,
        ),
        input_output_aliases={2 + i: i for i in range(len(into))},
    )(slots, source, *into)


def place_pages(sources, ranks, received, slot_count, cores, part, row_block, into=(), group=6):
    rows, width = received.shape[-2:]
    shaped = received.reshape(-1, cores, CAPACITY, rows, width)

    def body(src_ref, rank_ref, *refs):
        out = refs[-1]
        for member in range(group):
            for core in range(cores):
                out[member, :, core * width : (core + 1) * width] = refs[member][0, core, 0]

    def source_map(member):
        return lambda step, src_ref, rank_ref: (
            src_ref[step * group + member],
            0,
            rank_ref[step * group + member],
            0,
            0,
        )

    in_specs = [
        pl.BlockSpec((1, cores, 1, rows, width), source_map(member)) for member in range(group)
    ] + [pl.BlockSpec(memory_space=pl.ANY)] * len(into)
    return pl.pallas_call(
        body,
        out_shape=jax.ShapeDtypeStruct((slot_count, PAGE, 2 * cores * width), jnp.bfloat16),
        grid_spec=pltpu.PrefetchScalarGridSpec(
            num_scalar_prefetch=2,
            grid=(slot_count // group,),
            in_specs=in_specs,
            out_specs=pl.BlockSpec(
                (group, rows, cores * width),
                lambda step, src_ref, rank_ref: (step, row_block, part),
            ),
        ),
        input_output_aliases={2 + group + i: 0 for i in range(len(into))},
    )(sources, ranks, *([shaped] * group), *into)


def shards(
    tokens,
    norm_gain,
    w_query,
    w_key,
    w_value,
    w_out,
    prev_keys,
    prev_values,
    earlier_lengths,
    new_lengths,
    page_table,
):
    token_count, local_width = tokens.shape
    full_width = w_query.shape[0]
    prev_count = prev_keys.shape[0]
    req_count = lax.axis_size("req")
    cores = lax.axis_size("core")
    my_req = lax.axis_index("req")
    my_core = lax.axis_index("core")

    spare = 16
    riders = jnp.zeros((spare, local_width), tokens.dtype).at[0].set(norm_gain)
    gathered = lax.all_gather(
        jnp.concatenate([tokens, riders], axis=0), ("y", "core"), axis=1, tiled=True
    )
    full_tokens = gathered[:token_count]
    full_gain = gathered[token_count]
    widened = full_tokens.astype(jnp.float32)
    mean_square = jnp.mean(widened * widened, axis=1, keepdims=True)
    normed = (widened * lax.rsqrt(mean_square + EPSILON) * full_gain.astype(jnp.float32)[None, :]).astype(
        jnp.bfloat16
    )
    value_raw = jnp.dot(normed, w_value, preferred_element_type=jnp.float32)
    earlier = earlier_lengths[0]
    fresh = new_lengths[0]
    owners, positions = block_layout(earlier, fresh, token_count)
    new_values = value_raw.astype(jnp.bfloat16)

    page_total = (prev_count + token_count) // PAGE
    slot_count = page_total // cores
    dest_count = req_count * cores
    slot_total = dest_count * CAPACITY
    own_dests = page_table[0] // slot_count
    own_ranks = rank_in_dest(own_dests)
    send_slots = (own_dests * CAPACITY + own_ranks).astype(jnp.int32)
    prev_pages = prev_count // PAGE
    whole = ((0, PAGE),)
    halves = ((0, PAGE // 2), (PAGE // 2, PAGE // 2))
    (send_keys,) = pack_pages(send_slots[:prev_pages], prev_keys, whole, slot_total)
    send_low, send_high = pack_pages(send_slots[:prev_pages], prev_values, halves, slot_total)
    send_low, send_high = pack_pages(
        send_slots[prev_pages:], new_values, halves, slot_total, into=(send_low, send_high)
    )
    carried = (
        jnp.full((slot_total,), slot_count, jnp.int32)
        .at[send_slots]
        .set((page_table[0] % slot_count).astype(jnp.int32))
    )
    carried = lax.all_to_all(carried, ("req", "core"), 0, 0, tiled=True)
    carried = carried.reshape(req_count, cores, CAPACITY)[:, 0, :].reshape(-1)
    wanted = jnp.arange(slot_count, dtype=jnp.int32)
    found = jnp.argmax(carried[None, :] == wanted[:, None], axis=1).astype(jnp.int32)
    from_req = found // CAPACITY
    from_rank = found % CAPACITY
    send_keys, send_low, send_high, normed, new_values, from_req, from_rank = (
        lax.optimization_barrier(
            (send_keys, send_low, send_high, normed, new_values, from_req, from_rank)
        )
    )
    received_low = lax.all_to_all(send_low, ("req", "core"), 0, 0, tiled=True)
    key_raw = jnp.dot(normed, w_key, preferred_element_type=jnp.float32)
    new_keys = rotate(key_raw, positions, HD).astype(jnp.bfloat16)
    (send_keys,) = pack_pages(
        send_slots[prev_pages:], new_keys, whole, slot_total, into=(send_keys,)
    )
    keys_all = jnp.concatenate([prev_keys, new_keys], axis=0)
    values_all = jnp.concatenate([prev_values, new_values], axis=0)
    query_raw = jnp.dot(normed, w_query, preferred_element_type=jnp.float32)
    queries = rotate(query_raw, positions, HD).astype(jnp.bfloat16)
    received_keys = lax.all_to_all(send_keys, ("req", "core"), 0, 0, tiled=True)

    allowed = visible(earlier, owners, prev_count, token_count)
    heads_here = local_width // HD
    scores = jnp.einsum(
        "qhd,khd->hqk",
        queries.reshape(token_count, heads_here, HD),
        keys_all.reshape(-1, heads_here, HD),
        preferred_element_type=jnp.float32,
    ) * HD ** (-0.5)
    scores = jnp.where(allowed[None, :, :], scores, -1e30)
    row_peak = jnp.max(scores, axis=2, keepdims=True)
    weights = jnp.exp(scores - row_peak)
    totals = jnp.sum(weights, axis=2)
    prob_rows = weights.astype(jnp.bfloat16)
    mixture = jnp.einsum(
        "hqk,khd->qhd",
        prob_rows,
        values_all.reshape(-1, heads_here, HD),
        preferred_element_type=jnp.float32,
    )
    attended = (
        (mixture / totals.T[:, :, None]).astype(jnp.bfloat16).reshape(token_count, local_width)
    )
    projected = jnp.dot(attended, w_out, preferred_element_type=jnp.float32)
    received_keys, received_low, projected, send_high = lax.optimization_barrier(
        (received_keys, received_low, projected, send_high)
    )
    summed = lax.psum_scatter(projected, ("y", "core"), scatter_dimension=1, tiled=True)
    layer_out = (tokens.astype(jnp.float32) + summed).astype(jnp.bfloat16)
    received_high = lax.all_to_all(send_high, ("req", "core"), 0, 0, tiled=True)
    pool = place_pages(from_req, from_rank, received_keys, slot_count, cores, 0, 0)
    pool = place_pages(from_req, from_rank, received_low, slot_count, cores, 1, 0, into=(pool,))
    pool = place_pages(from_req, from_rank, received_high, slot_count, cores, 1, 1, into=(pool,))
    return (layer_out, pool[:, None])


def solution(mesh):
    req_count, tp_count = mesh.devices.shape
    cores = tp_count // HG
    split_mesh = Mesh(mesh.devices.reshape(req_count, HG, cores), ("req", "y", "core"))
    tp = ("y", "core")
    placed = (
        P("req", tp),
        P(tp),
        P(None, tp),
        P(None, tp),
        P(None, tp),
        P(tp, None),
        P("req", tp),
        P("req", tp),
        P("req", None),
        P("req", None),
        P("req", None),
    )
    return jax.shard_map(
        shards,
        mesh=split_mesh,
        in_specs=placed,
        out_specs=(P("req", tp), P("req", tp, None, None)),
        check_vma=False,
    )
```

```python
import math

import jax
import jax.numpy as jnp
from jax import lax
from jax.experimental import pallas as pl
from jax.experimental.pallas import tpu as pltpu
from jax.sharding import Mesh
from jax.sharding import PartitionSpec as P

HD = 96
HG = 4
PAGE = 128
CAPACITY = 2


EPSILON = 1e-05
THETA = 10000.0


def rotate(values, positions, head_size):
    count = values.shape[0]
    half_size = head_size // 2
    shaped = values.reshape(count, -1, head_size)
    freqs = jnp.exp(-math.log(THETA) * 2.0 * jnp.arange(half_size, dtype=jnp.float32) / head_size)
    angles = positions.astype(jnp.float32)[:, None] * freqs[None, :]
    cosine = jnp.cos(angles)[:, None, :]
    sine = jnp.sin(angles)[:, None, :]
    first = shaped[:, :, :half_size]
    second = shaped[:, :, half_size:]
    turned = jnp.concatenate(
        [first * cosine - second * sine, second * cosine + first * sine], axis=2
    )
    return turned.reshape(count, -1)


def request_ids(lengths, count):
    ends = jnp.cumsum(lengths)
    row_index = jnp.arange(count, dtype=jnp.int32)
    return jnp.sum((row_index[:, None] >= ends[None, :]).astype(jnp.int32), axis=1)


def block_layout(earlier, fresh, count):
    owners = request_ids(fresh, count)
    starts = jnp.cumsum(fresh) - fresh
    onehot = (owners[:, None] == jnp.arange(fresh.shape[0], dtype=jnp.int32)[None, :]).astype(
        jnp.int32
    )
    first_row = jnp.sum(onehot * starts[None, :], axis=1)
    before = jnp.sum(onehot * earlier[None, :], axis=1)
    row_index = jnp.arange(count, dtype=jnp.int32)
    return (owners, before + row_index - first_row)


def visible(earlier, owners, prev_count, count):
    prev_owner = request_ids(earlier, prev_count)
    row_index = jnp.arange(count, dtype=jnp.int32)
    old_part = owners[:, None] == prev_owner[None, :]
    new_part = (owners[:, None] == owners[None, :]) & (row_index[None, :] <= row_index[:, None])
    return jnp.concatenate([old_part, new_part], axis=1)


def rank_in_dest(dests):
    same = (dests[..., :, None] == dests[..., None, :]).astype(jnp.int32)
    count = dests.shape[-1]
    order_index = jnp.arange(count, dtype=jnp.int32)
    earlier_mask = (order_index[None, :] < order_index[:, None]).astype(jnp.int32)
    return jnp.sum(same * earlier_mask, axis=-1)


def pack_pages(slots, sources, parts, slot_total, into=()):
    page_total = sources[0].shape[0] // PAGE
    width = sources[0].shape[1]

    def body(slot_ref, *rest):
        blocks = rest[: len(sources)]
        outs = rest[len(rest) - len(parts) :]
        for out, (which, start, rows) in zip(outs, parts):
            out[0] = blocks[which][start : start + rows]

    in_specs = [pl.BlockSpec((PAGE, width), lambda page, slot_ref: (page, 0))] * len(sources)
    in_specs += [pl.BlockSpec(memory_space=pl.ANY)] * len(into)
    out_shape = tuple(
        jax.ShapeDtypeStruct((slot_total, rows, width), jnp.bfloat16) for _, _, rows in parts
    )
    out_specs = tuple(
        pl.BlockSpec((1, rows, width), lambda page, slot_ref: (slot_ref[page], 0, 0))
        for _, _, rows in parts
    )
    first_alias = 1 + len(sources)
    return pl.pallas_call(
        body,
        out_shape=out_shape,
        grid_spec=pltpu.PrefetchScalarGridSpec(
            num_scalar_prefetch=1,
            grid=(page_total,),
            in_specs=in_specs,
            out_specs=out_specs,
        ),
        input_output_aliases={first_alias + i: i for i in range(len(into))},
    )(slots, *sources, *into)


def place_pages(sources, ranks, received, slot_count, cores, part, row_block, into=(), group=6):
    rows, width = received.shape[-2:]
    shaped = received.reshape(-1, cores, CAPACITY, rows, width)

    def body(src_ref, rank_ref, *refs):
        out = refs[-1]
        for member in range(group):
            for core in range(cores):
                out[member, :, core * width : (core + 1) * width] = refs[member][0, core, 0]

    def source_map(member):
        return lambda step, src_ref, rank_ref: (
            src_ref[step * group + member],
            0,
            rank_ref[step * group + member],
            0,
            0,
        )

    in_specs = [
        pl.BlockSpec((1, cores, 1, rows, width), source_map(member)) for member in range(group)
    ] + [pl.BlockSpec(memory_space=pl.ANY)] * len(into)
    return pl.pallas_call(
        body,
        out_shape=jax.ShapeDtypeStruct((slot_count, PAGE, 2 * cores * width), jnp.bfloat16),
        grid_spec=pltpu.PrefetchScalarGridSpec(
            num_scalar_prefetch=2,
            grid=(slot_count // group,),
            in_specs=in_specs,
            out_specs=pl.BlockSpec(
                (group, rows, cores * width),
                lambda step, src_ref, rank_ref: (step, row_block, part),
            ),
        ),
        input_output_aliases={2 + group + i: 0 for i in range(len(into))},
    )(sources, ranks, *([shaped] * group), *into)


def shards(
    tokens,
    norm_gain,
    w_query,
    w_key,
    w_value,
    w_out,
    prev_keys,
    prev_values,
    earlier_lengths,
    new_lengths,
    page_table,
):
    token_count, local_width = tokens.shape
    full_width = w_query.shape[0]
    prev_count = prev_keys.shape[0]
    req_count = lax.axis_size("req")
    cores = lax.axis_size("core")
    my_req = lax.axis_index("req")
    my_core = lax.axis_index("core")

    spare = 16
    riders = jnp.zeros((spare, local_width), tokens.dtype).at[0].set(norm_gain)
    gathered = lax.all_gather(
        jnp.concatenate([tokens, riders], axis=0), ("y", "core"), axis=1, tiled=True
    )
    full_tokens = gathered[:token_count]
    full_gain = gathered[token_count]
    widened = full_tokens.astype(jnp.float32)
    mean_square = jnp.mean(widened * widened, axis=1, keepdims=True)
    normed = (widened * lax.rsqrt(mean_square + EPSILON) * full_gain.astype(jnp.float32)[None, :]).astype(
        jnp.bfloat16
    )
    value_raw = jnp.dot(normed, w_value, preferred_element_type=jnp.float32)
    earlier = earlier_lengths[0]
    fresh = new_lengths[0]
    owners, positions = block_layout(earlier, fresh, token_count)
    new_values = value_raw.astype(jnp.bfloat16)

    page_total = (prev_count + token_count) // PAGE
    slot_count = page_total // cores
    dest_count = req_count * cores
    slot_total = dest_count * CAPACITY
    own_dests = page_table[0] // slot_count
    own_ranks = rank_in_dest(own_dests)
    send_slots = (own_dests * CAPACITY + own_ranks).astype(jnp.int32)
    prev_pages = prev_count // PAGE
    whole = ((0, 0, PAGE),)
    halves = ((0, 0, PAGE // 2), (0, PAGE // 2, PAGE // 2))
    both = ((0, 0, PAGE), (1, 0, PAGE // 2), (1, PAGE // 2, PAGE // 2))
    send_keys, send_low, send_high = pack_pages(
        send_slots[:prev_pages], (prev_keys, prev_values), both, slot_total
    )
    send_low, send_high = pack_pages(
        send_slots[prev_pages:], (new_values,), halves, slot_total, into=(send_low, send_high)
    )
    carried = (
        jnp.full((slot_total,), slot_count, jnp.int32)
        .at[send_slots]
        .set((page_table[0] % slot_count).astype(jnp.int32))
    )
    carried = lax.all_to_all(carried, ("req", "core"), 0, 0, tiled=True)
    carried = carried.reshape(req_count, cores, CAPACITY)[:, 0, :].reshape(-1)
    wanted = jnp.arange(slot_count, dtype=jnp.int32)
    found = jnp.argmax(carried[None, :] == wanted[:, None], axis=1).astype(jnp.int32)
    from_req = found // CAPACITY
    from_rank = found % CAPACITY
    send_keys, send_low, send_high, normed, new_values, from_req, from_rank = (
        lax.optimization_barrier(
            (send_keys, send_low, send_high, normed, new_values, from_req, from_rank)
        )
    )
    received_low = lax.all_to_all(send_low, ("req", "core"), 0, 0, tiled=True)
    key_raw = jnp.dot(normed, w_key, preferred_element_type=jnp.float32)
    new_keys = rotate(key_raw, positions, HD).astype(jnp.bfloat16)
    (send_keys,) = pack_pages(
        send_slots[prev_pages:], (new_keys,), whole, slot_total, into=(send_keys,)
    )
    keys_all = jnp.concatenate([prev_keys, new_keys], axis=0)
    values_all = jnp.concatenate([prev_values, new_values], axis=0)
    query_raw = jnp.dot(normed, w_query, preferred_element_type=jnp.float32)
    queries = rotate(query_raw, positions, HD).astype(jnp.bfloat16)
    received_keys = lax.all_to_all(send_keys, ("req", "core"), 0, 0, tiled=True)

    allowed = visible(earlier, owners, prev_count, token_count)
    heads_here = local_width // HD
    scores = jnp.einsum(
        "qhd,khd->hqk",
        queries.reshape(token_count, heads_here, HD),
        keys_all.reshape(-1, heads_here, HD),
        preferred_element_type=jnp.float32,
    ) * HD ** (-0.5)
    scores = jnp.where(allowed[None, :, :], scores, -1e30)
    row_peak = jnp.max(scores, axis=2, keepdims=True)
    weights = jnp.exp(scores - row_peak)
    totals = jnp.sum(weights, axis=2)
    prob_rows = weights.astype(jnp.bfloat16)
    mixture = jnp.einsum(
        "hqk,khd->qhd",
        prob_rows,
        values_all.reshape(-1, heads_here, HD),
        preferred_element_type=jnp.float32,
    )
    attended = (
        (mixture / totals.T[:, :, None]).astype(jnp.bfloat16).reshape(token_count, local_width)
    )
    projected = jnp.dot(attended, w_out, preferred_element_type=jnp.float32)
    received_keys, received_low, projected, send_high = lax.optimization_barrier(
        (received_keys, received_low, projected, send_high)
    )
    summed = lax.psum_scatter(projected, ("y", "core"), scatter_dimension=1, tiled=True)
    layer_out = (tokens.astype(jnp.float32) + summed).astype(jnp.bfloat16)
    received_high = lax.all_to_all(send_high, ("req", "core"), 0, 0, tiled=True)
    pool = place_pages(from_req, from_rank, received_keys, slot_count, cores, 0, 0)
    pool = place_pages(from_req, from_rank, received_low, slot_count, cores, 1, 0, into=(pool,))
    pool = place_pages(from_req, from_rank, received_high, slot_count, cores, 1, 1, into=(pool,))
    return (layer_out, pool[:, None])


def solution(mesh):
    req_count, tp_count = mesh.devices.shape
    cores = tp_count // HG
    split_mesh = Mesh(mesh.devices.reshape(req_count, HG, cores), ("req", "y", "core"))
    tp = ("y", "core")
    placed = (
        P("req", tp),
        P(tp),
        P(None, tp),
        P(None, tp),
        P(None, tp),
        P(tp, None),
        P("req", tp),
        P("req", tp),
        P("req", None),
        P("req", None),
        P("req", None),
    )
    return jax.shard_map(
        shards,
        mesh=split_mesh,
        in_specs=placed,
        out_specs=(P("req", tp), P("req", tp, None, None)),
        check_vma=False,
    )
```

```python
import math

import jax
import jax.numpy as jnp
from jax import lax
from jax.experimental import pallas as pl
from jax.experimental.pallas import tpu as pltpu
from jax.sharding import Mesh
from jax.sharding import PartitionSpec as P

HD = 96
HG = 4
PAGE = 128
CAPACITY = 2


EPSILON = 1e-05
THETA = 10000.0


def rotate(values, positions, head_size):
    count = values.shape[0]
    half_size = head_size // 2
    shaped = values.reshape(count, -1, head_size)
    freqs = jnp.exp(-math.log(THETA) * 2.0 * jnp.arange(half_size, dtype=jnp.float32) / head_size)
    angles = positions.astype(jnp.float32)[:, None] * freqs[None, :]
    cosine = jnp.cos(angles)[:, None, :]
    sine = jnp.sin(angles)[:, None, :]
    first = shaped[:, :, :half_size]
    second = shaped[:, :, half_size:]
    turned = jnp.concatenate(
        [first * cosine - second * sine, second * cosine + first * sine], axis=2
    )
    return turned.reshape(count, -1)


def request_ids(lengths, count):
    ends = jnp.cumsum(lengths)
    row_index = jnp.arange(count, dtype=jnp.int32)
    return jnp.sum((row_index[:, None] >= ends[None, :]).astype(jnp.int32), axis=1)


def block_layout(earlier, fresh, count):
    owners = request_ids(fresh, count)
    starts = jnp.cumsum(fresh) - fresh
    onehot = (owners[:, None] == jnp.arange(fresh.shape[0], dtype=jnp.int32)[None, :]).astype(
        jnp.int32
    )
    first_row = jnp.sum(onehot * starts[None, :], axis=1)
    before = jnp.sum(onehot * earlier[None, :], axis=1)
    row_index = jnp.arange(count, dtype=jnp.int32)
    return (owners, before + row_index - first_row)


def visible(earlier, owners, prev_count, count):
    prev_owner = request_ids(earlier, prev_count)
    row_index = jnp.arange(count, dtype=jnp.int32)
    old_part = owners[:, None] == prev_owner[None, :]
    new_part = (owners[:, None] == owners[None, :]) & (row_index[None, :] <= row_index[:, None])
    return jnp.concatenate([old_part, new_part], axis=1)


def rank_in_dest(dests):
    same = (dests[..., :, None] == dests[..., None, :]).astype(jnp.int32)
    count = dests.shape[-1]
    order_index = jnp.arange(count, dtype=jnp.int32)
    earlier_mask = (order_index[None, :] < order_index[:, None]).astype(jnp.int32)
    return jnp.sum(same * earlier_mask, axis=-1)


def pack_pages(slots, sources, parts, slot_total, into=(), shapes=None):
    page_total = sources[0].shape[0] // PAGE
    width = sources[0].shape[1]

    def body(slot_ref, *rest):
        blocks = rest[: len(sources)]
        outs = rest[len(rest) - len(parts) :]
        for out, (which, start, rows) in zip(outs, parts):
            out[0] = blocks[which][start : start + rows]

    in_specs = [pl.BlockSpec((PAGE, width), lambda page, slot_ref: (page, 0))] * len(sources)
    in_specs += [pl.BlockSpec(memory_space=pl.ANY)] * len(into)
    if shapes is None:
        shapes = [rows for _, _, rows in parts]
    out_shape = tuple(
        jax.ShapeDtypeStruct((slot_total, full, width), jnp.bfloat16) for full in shapes
    )
    out_specs = tuple(
        pl.BlockSpec((1, rows, width), lambda page, slot_ref: (slot_ref[page], 0, 0))
        for _, _, rows in parts
    )
    first_alias = 1 + len(sources)
    return pl.pallas_call(
        body,
        out_shape=out_shape,
        grid_spec=pltpu.PrefetchScalarGridSpec(
            num_scalar_prefetch=1,
            grid=(page_total,),
            in_specs=in_specs,
            out_specs=out_specs,
        ),
        input_output_aliases={first_alias + i: out for i, out in enumerate(into)},
    )(slots, *sources, *into.values())


def stamp_tags(tags, first_row):
    slot_total, tag_rows, width = tags.shape

    def body(tag_block, out):
        out[...] = tag_block[...]

    return pl.pallas_call(
        body,
        out_shape=jax.ShapeDtypeStruct((slot_total, first_row + tag_rows, width), jnp.bfloat16),
        grid=(1,),
        in_specs=[pl.BlockSpec((slot_total, tag_rows, width), lambda step: (0, 0, 0))],
        out_specs=pl.BlockSpec(
            (slot_total, tag_rows, width), lambda step: (0, first_row // tag_rows, 0)
        ),
    )(tags)


def place_pages(
    sources, ranks, received, slot_count, cores, part, row_block, rows, into=(), group=6
):
    stored, width = received.shape[-2:]
    shaped = received.reshape(-1, cores, CAPACITY, stored, width)

    def body(src_ref, rank_ref, *refs):
        out = refs[-1]
        for member in range(group):
            for core in range(cores):
                out[member, :, core * width : (core + 1) * width] = refs[member][0, core, 0]

    def source_map(member):
        return lambda step, src_ref, rank_ref: (
            src_ref[step * group + member],
            0,
            rank_ref[step * group + member],
            0,
            0,
        )

    in_specs = [
        pl.BlockSpec((1, cores, 1, rows, width), source_map(member)) for member in range(group)
    ] + [pl.BlockSpec(memory_space=pl.ANY)] * len(into)
    return pl.pallas_call(
        body,
        out_shape=jax.ShapeDtypeStruct((slot_count, PAGE, 2 * cores * width), jnp.bfloat16),
        grid_spec=pltpu.PrefetchScalarGridSpec(
            num_scalar_prefetch=2,
            grid=(slot_count // group,),
            in_specs=in_specs,
            out_specs=pl.BlockSpec(
                (group, rows, cores * width),
                lambda step, src_ref, rank_ref: (step, row_block, part),
            ),
        ),
        input_output_aliases={2 + group + i: 0 for i in range(len(into))},
    )(sources, ranks, *([shaped] * group), *into)


def shards(
    tokens,
    norm_gain,
    w_query,
    w_key,
    w_value,
    w_out,
    prev_keys,
    prev_values,
    earlier_lengths,
    new_lengths,
    page_table,
):
    token_count, local_width = tokens.shape
    full_width = w_query.shape[0]
    prev_count = prev_keys.shape[0]
    req_count = lax.axis_size("req")
    cores = lax.axis_size("core")
    my_req = lax.axis_index("req")
    my_core = lax.axis_index("core")

    spare = 16
    riders = jnp.zeros((spare, local_width), tokens.dtype).at[0].set(norm_gain)
    gathered = lax.all_gather(
        jnp.concatenate([tokens, riders], axis=0), ("y", "core"), axis=1, tiled=True
    )
    full_tokens = gathered[:token_count]
    full_gain = gathered[token_count]
    widened = full_tokens.astype(jnp.float32)
    mean_square = jnp.mean(widened * widened, axis=1, keepdims=True)
    normed = (widened * lax.rsqrt(mean_square + EPSILON) * full_gain.astype(jnp.float32)[None, :]).astype(
        jnp.bfloat16
    )
    value_raw = jnp.dot(normed, w_value, preferred_element_type=jnp.float32)
    earlier = earlier_lengths[0]
    fresh = new_lengths[0]
    owners, positions = block_layout(earlier, fresh, token_count)
    new_values = value_raw.astype(jnp.bfloat16)

    page_total = (prev_count + token_count) // PAGE
    slot_count = page_total // cores
    dest_count = req_count * cores
    slot_total = dest_count * CAPACITY
    own_dests = page_table[0] // slot_count
    own_ranks = rank_in_dest(own_dests)
    send_slots = (own_dests * CAPACITY + own_ranks).astype(jnp.int32)
    prev_pages = prev_count // PAGE
    whole = ((0, 0, PAGE),)
    halves = ((0, 0, PAGE // 2), (0, PAGE // 2, PAGE // 2))
    both = ((0, 0, PAGE), (1, 0, PAGE // 2), (1, PAGE // 2, PAGE // 2))
    half_rows = PAGE // 2
    tag_rows = 16
    carried = (
        jnp.full((slot_total,), slot_count, jnp.int32)
        .at[send_slots]
        .set((page_table[0] % slot_count).astype(jnp.int32))
    )
    tags = jnp.zeros((slot_total, tag_rows, local_width), jnp.bfloat16)
    tags = tags.at[:, 0, 0].set(carried.astype(jnp.bfloat16))
    send_low = stamp_tags(tags, half_rows)
    send_keys, send_low, send_high = pack_pages(
        send_slots[:prev_pages],
        (prev_keys, prev_values),
        both,
        slot_total,
        into={1: send_low},
        shapes=(PAGE, half_rows + tag_rows, half_rows),
    )
    send_low, send_high = pack_pages(
        send_slots[prev_pages:],
        (new_values,),
        halves,
        slot_total,
        into={0: send_low, 1: send_high},
        shapes=(half_rows + tag_rows, half_rows),
    )
    send_keys, send_low, send_high, normed, new_values = lax.optimization_barrier(
        (send_keys, send_low, send_high, normed, new_values)
    )
    received_low = lax.all_to_all(send_low, ("req", "core"), 0, 0, tiled=True)
    carried = received_low[:, half_rows, 0].astype(jnp.int32)
    carried = carried.reshape(req_count, cores, CAPACITY)[:, 0, :].reshape(-1)
    wanted = jnp.arange(slot_count, dtype=jnp.int32)
    found = jnp.argmax(carried[None, :] == wanted[:, None], axis=1).astype(jnp.int32)
    from_req = found // CAPACITY
    from_rank = found % CAPACITY
    key_raw = jnp.dot(normed, w_key, preferred_element_type=jnp.float32)
    new_keys = rotate(key_raw, positions, HD).astype(jnp.bfloat16)
    (send_keys,) = pack_pages(
        send_slots[prev_pages:], (new_keys,), whole, slot_total, into={0: send_keys}
    )
    keys_all = jnp.concatenate([prev_keys, new_keys], axis=0)
    values_all = jnp.concatenate([prev_values, new_values], axis=0)
    query_raw = jnp.dot(normed, w_query, preferred_element_type=jnp.float32)
    queries = rotate(query_raw, positions, HD).astype(jnp.bfloat16)
    received_keys = lax.all_to_all(send_keys, ("req", "core"), 0, 0, tiled=True)

    allowed = visible(earlier, owners, prev_count, token_count)
    heads_here = local_width // HD
    scores = jnp.einsum(
        "qhd,khd->hqk",
        queries.reshape(token_count, heads_here, HD),
        keys_all.reshape(-1, heads_here, HD),
        preferred_element_type=jnp.float32,
    ) * HD ** (-0.5)
    scores = jnp.where(allowed[None, :, :], scores, -1e30)
    row_peak = jnp.max(scores, axis=2, keepdims=True)
    weights = jnp.exp(scores - row_peak)
    totals = jnp.sum(weights, axis=2)
    prob_rows = weights.astype(jnp.bfloat16)
    mixture = jnp.einsum(
        "hqk,khd->qhd",
        prob_rows,
        values_all.reshape(-1, heads_here, HD),
        preferred_element_type=jnp.float32,
    )
    attended = (
        (mixture / totals.T[:, :, None]).astype(jnp.bfloat16).reshape(token_count, local_width)
    )
    projected = jnp.dot(attended, w_out, preferred_element_type=jnp.float32)
    received_keys, received_low, projected, send_high = lax.optimization_barrier(
        (received_keys, received_low, projected, send_high)
    )
    summed = lax.psum_scatter(projected, ("y", "core"), scatter_dimension=1, tiled=True)
    layer_out = (tokens.astype(jnp.float32) + summed).astype(jnp.bfloat16)
    received_high = lax.all_to_all(send_high, ("req", "core"), 0, 0, tiled=True)
    half_rows = PAGE // 2
    pool = place_pages(from_req, from_rank, received_keys, slot_count, cores, 0, 0, PAGE)
    pool = place_pages(
        from_req, from_rank, received_low, slot_count, cores, 1, 0, half_rows, into=(pool,)
    )
    pool = place_pages(
        from_req, from_rank, received_high, slot_count, cores, 1, 1, half_rows, into=(pool,)
    )
    return (layer_out, pool[:, None])


def solution(mesh):
    req_count, tp_count = mesh.devices.shape
    cores = tp_count // HG
    split_mesh = Mesh(mesh.devices.reshape(req_count, HG, cores), ("req", "y", "core"))
    tp = ("y", "core")
    placed = (
        P("req", tp),
        P(tp),
        P(None, tp),
        P(None, tp),
        P(None, tp),
        P(tp, None),
        P("req", tp),
        P("req", tp),
        P("req", None),
        P("req", None),
        P("req", None),
    )
    return jax.shard_map(
        shards,
        mesh=split_mesh,
        in_specs=placed,
        out_specs=(P("req", tp), P("req", tp, None, None)),
        check_vma=False,
    )
```

```python
import math

import jax
import jax.numpy as jnp
from jax import lax
from jax.experimental import pallas as pl
from jax.experimental.pallas import tpu as pltpu
from jax.sharding import Mesh
from jax.sharding import PartitionSpec as P

HD = 96
HG = 4
PAGE = 128
CAPACITY = 2


EPSILON = 1e-05
THETA = 10000.0


def rotate(values, positions, head_size):
    count = values.shape[0]
    half_size = head_size // 2
    shaped = values.reshape(count, -1, head_size)
    freqs = jnp.exp(-math.log(THETA) * 2.0 * jnp.arange(half_size, dtype=jnp.float32) / head_size)
    angles = positions.astype(jnp.float32)[:, None] * freqs[None, :]
    cosine = jnp.cos(angles)[:, None, :]
    sine = jnp.sin(angles)[:, None, :]
    first = shaped[:, :, :half_size]
    second = shaped[:, :, half_size:]
    turned = jnp.concatenate(
        [first * cosine - second * sine, second * cosine + first * sine], axis=2
    )
    return turned.reshape(count, -1)


def request_ids(lengths, count):
    ends = jnp.cumsum(lengths)
    row_index = jnp.arange(count, dtype=jnp.int32)
    return jnp.sum((row_index[:, None] >= ends[None, :]).astype(jnp.int32), axis=1)


def block_layout(earlier, fresh, count):
    owners = request_ids(fresh, count)
    starts = jnp.cumsum(fresh) - fresh
    onehot = (owners[:, None] == jnp.arange(fresh.shape[0], dtype=jnp.int32)[None, :]).astype(
        jnp.int32
    )
    first_row = jnp.sum(onehot * starts[None, :], axis=1)
    before = jnp.sum(onehot * earlier[None, :], axis=1)
    row_index = jnp.arange(count, dtype=jnp.int32)
    return (owners, before + row_index - first_row)


def visible(earlier, owners, prev_count, count):
    prev_owner = request_ids(earlier, prev_count)
    row_index = jnp.arange(count, dtype=jnp.int32)
    old_part = owners[:, None] == prev_owner[None, :]
    new_part = (owners[:, None] == owners[None, :]) & (row_index[None, :] <= row_index[:, None])
    return jnp.concatenate([old_part, new_part], axis=1)


def rank_in_dest(dests):
    same = (dests[..., :, None] == dests[..., None, :]).astype(jnp.int32)
    count = dests.shape[-1]
    order_index = jnp.arange(count, dtype=jnp.int32)
    earlier_mask = (order_index[None, :] < order_index[:, None]).astype(jnp.int32)
    return jnp.sum(same * earlier_mask, axis=-1)


def pack_pages(slots, sources, parts, slot_total, into=(), shapes=None, paired=()):
    page_total = sources[0].shape[0] // PAGE
    width = sources[0].shape[1]

    def body(slot_ref, *rest):
        blocks = rest[: len(sources)]
        outs = rest[len(rest) - len(parts) :]
        for out, (which, start, rows) in zip(outs, parts):
            out[0] = blocks[which][start : start + rows]

    in_specs = [pl.BlockSpec((PAGE, width), lambda page, slot_ref: (page, 0))] * len(sources)
    in_specs += [pl.BlockSpec(memory_space=pl.ANY)] * len(into)
    if shapes is None:
        shapes = [rows for _, _, rows in parts]
    out_shape = tuple(
        jax.ShapeDtypeStruct(
            (slot_total // CAPACITY if index in paired else slot_total, full, width),
            jnp.bfloat16,
        )
        for index, full in enumerate(shapes)
    )

    def out_map(index):
        if index in paired:
            return lambda page, slot_ref: (
                slot_ref[page] // CAPACITY,
                slot_ref[page] % CAPACITY,
                0,
            )
        return lambda page, slot_ref: (slot_ref[page], 0, 0)

    out_specs = tuple(
        pl.BlockSpec((1, rows, width), out_map(index)) for index, (_, _, rows) in enumerate(parts)
    )
    first_alias = 1 + len(sources)
    return pl.pallas_call(
        body,
        out_shape=out_shape,
        grid_spec=pltpu.PrefetchScalarGridSpec(
            num_scalar_prefetch=1,
            grid=(page_total,),
            in_specs=in_specs,
            out_specs=out_specs,
        ),
        input_output_aliases={first_alias + i: out for i, out in enumerate(into)},
    )(slots, *sources, *into.values())


def stamp_tags(tags, first_row):
    dest_total, tag_rows, width = tags.shape

    def body(tag_block, out):
        out[...] = tag_block[...]

    return pl.pallas_call(
        body,
        out_shape=jax.ShapeDtypeStruct((dest_total, first_row + tag_rows, width), jnp.bfloat16),
        grid=(1,),
        in_specs=[pl.BlockSpec((dest_total, tag_rows, width), lambda step: (0, 0, 0))],
        out_specs=pl.BlockSpec(
            (dest_total, tag_rows, width), lambda step: (0, first_row // tag_rows, 0)
        ),
    )(tags)


def place_pages(
    sources, ranks, received, slot_count, cores, part, row_block, rows, into=(), group=6,
    paired=False,
):
    stored, width = received.shape[-2:]
    if paired:
        shaped = received.reshape(-1, cores, stored, width)
        block = (1, cores, rows, width)
    else:
        shaped = received.reshape(-1, cores, CAPACITY, stored, width)
        block = (1, cores, 1, rows, width)

    def body(src_ref, rank_ref, *refs):
        out = refs[-1]
        for member in range(group):
            for core in range(cores):
                piece = refs[member][0, core] if paired else refs[member][0, core, 0]
                out[member, :, core * width : (core + 1) * width] = piece

    def source_map(member):
        if paired:
            return lambda step, src_ref, rank_ref: (
                src_ref[step * group + member],
                0,
                rank_ref[step * group + member],
                0,
            )
        return lambda step, src_ref, rank_ref: (
            src_ref[step * group + member],
            0,
            rank_ref[step * group + member],
            0,
            0,
        )

    in_specs = [
        pl.BlockSpec(block, source_map(member)) for member in range(group)
    ] + [pl.BlockSpec(memory_space=pl.ANY)] * len(into)
    return pl.pallas_call(
        body,
        out_shape=jax.ShapeDtypeStruct((slot_count, PAGE, 2 * cores * width), jnp.bfloat16),
        grid_spec=pltpu.PrefetchScalarGridSpec(
            num_scalar_prefetch=2,
            grid=(slot_count // group,),
            in_specs=in_specs,
            out_specs=pl.BlockSpec(
                (group, rows, cores * width),
                lambda step, src_ref, rank_ref: (step, row_block, part),
            ),
        ),
        input_output_aliases={2 + group + i: 0 for i in range(len(into))},
    )(sources, ranks, *([shaped] * group), *into)


def shards(
    tokens,
    norm_gain,
    w_query,
    w_key,
    w_value,
    w_out,
    prev_keys,
    prev_values,
    earlier_lengths,
    new_lengths,
    page_table,
):
    token_count, local_width = tokens.shape
    full_width = w_query.shape[0]
    prev_count = prev_keys.shape[0]
    req_count = lax.axis_size("req")
    cores = lax.axis_size("core")
    my_req = lax.axis_index("req")
    my_core = lax.axis_index("core")

    spare = 16
    riders = jnp.zeros((spare, local_width), tokens.dtype).at[0].set(norm_gain)
    gathered = lax.all_gather(
        jnp.concatenate([tokens, riders], axis=0), ("y", "core"), axis=1, tiled=True
    )
    full_tokens = gathered[:token_count]
    full_gain = gathered[token_count]
    widened = full_tokens.astype(jnp.float32)
    mean_square = jnp.mean(widened * widened, axis=1, keepdims=True)
    normed = (widened * lax.rsqrt(mean_square + EPSILON) * full_gain.astype(jnp.float32)[None, :]).astype(
        jnp.bfloat16
    )
    value_raw = jnp.dot(normed, w_value, preferred_element_type=jnp.float32)
    earlier = earlier_lengths[0]
    fresh = new_lengths[0]
    owners, positions = block_layout(earlier, fresh, token_count)
    new_values = value_raw.astype(jnp.bfloat16)

    page_total = (prev_count + token_count) // PAGE
    slot_count = page_total // cores
    dest_count = req_count * cores
    slot_total = dest_count * CAPACITY
    own_dests = page_table[0] // slot_count
    own_ranks = rank_in_dest(own_dests)
    send_slots = (own_dests * CAPACITY + own_ranks).astype(jnp.int32)
    prev_pages = prev_count // PAGE
    whole = ((0, 0, PAGE),)
    halves = ((0, 0, PAGE // 2), (0, PAGE // 2, PAGE // 2))
    both = ((0, 0, PAGE), (1, 0, PAGE // 2), (1, PAGE // 2, PAGE // 2))
    half_rows = PAGE // 2
    tag_rows = 16
    carried = (
        jnp.full((slot_total,), slot_count, jnp.int32)
        .at[send_slots]
        .set((page_table[0] % slot_count).astype(jnp.int32))
    )
    tags = jnp.zeros((dest_count, tag_rows, local_width), jnp.bfloat16)
    tags = tags.at[:, 0, :CAPACITY].set(
        carried.reshape(dest_count, CAPACITY).astype(jnp.bfloat16)
    )
    send_low = stamp_tags(tags, CAPACITY * half_rows)
    send_keys, send_low, send_high = pack_pages(
        send_slots[:prev_pages],
        (prev_keys, prev_values),
        both,
        slot_total,
        into={1: send_low},
        shapes=(PAGE, CAPACITY * half_rows + tag_rows, half_rows),
        paired=(1,),
    )
    send_low, send_high = pack_pages(
        send_slots[prev_pages:],
        (new_values,),
        halves,
        slot_total,
        into={0: send_low, 1: send_high},
        shapes=(CAPACITY * half_rows + tag_rows, half_rows),
        paired=(0,),
    )
    send_keys, send_low, send_high, normed, new_values = lax.optimization_barrier(
        (send_keys, send_low, send_high, normed, new_values)
    )
    received_low = lax.all_to_all(send_low, ("req", "core"), 0, 0, tiled=True)
    carried = received_low[:, CAPACITY * half_rows, :CAPACITY].astype(jnp.int32)
    carried = carried.reshape(req_count, cores, CAPACITY)[:, 0, :].reshape(-1)
    wanted = jnp.arange(slot_count, dtype=jnp.int32)
    found = jnp.argmax(carried[None, :] == wanted[:, None], axis=1).astype(jnp.int32)
    from_req = found // CAPACITY
    from_rank = found % CAPACITY
    key_raw = jnp.dot(normed, w_key, preferred_element_type=jnp.float32)
    new_keys = rotate(key_raw, positions, HD).astype(jnp.bfloat16)
    (send_keys,) = pack_pages(
        send_slots[prev_pages:], (new_keys,), whole, slot_total, into={0: send_keys}
    )
    keys_all = jnp.concatenate([prev_keys, new_keys], axis=0)
    values_all = jnp.concatenate([prev_values, new_values], axis=0)
    query_raw = jnp.dot(normed, w_query, preferred_element_type=jnp.float32)
    queries = rotate(query_raw, positions, HD).astype(jnp.bfloat16)
    received_keys = lax.all_to_all(send_keys, ("req", "core"), 0, 0, tiled=True)

    allowed = visible(earlier, owners, prev_count, token_count)
    heads_here = local_width // HD
    scores = jnp.einsum(
        "qhd,khd->hqk",
        queries.reshape(token_count, heads_here, HD),
        keys_all.reshape(-1, heads_here, HD),
        preferred_element_type=jnp.float32,
    ) * HD ** (-0.5)
    scores = jnp.where(allowed[None, :, :], scores, -1e30)
    row_peak = jnp.max(scores, axis=2, keepdims=True)
    weights = jnp.exp(scores - row_peak)
    totals = jnp.sum(weights, axis=2)
    prob_rows = weights.astype(jnp.bfloat16)
    mixture = jnp.einsum(
        "hqk,khd->qhd",
        prob_rows,
        values_all.reshape(-1, heads_here, HD),
        preferred_element_type=jnp.float32,
    )
    attended = (
        (mixture / totals.T[:, :, None]).astype(jnp.bfloat16).reshape(token_count, local_width)
    )
    projected = jnp.dot(attended, w_out, preferred_element_type=jnp.float32)
    received_keys, received_low, projected, send_high = lax.optimization_barrier(
        (received_keys, received_low, projected, send_high)
    )
    summed = lax.psum_scatter(projected, ("y", "core"), scatter_dimension=1, tiled=True)
    layer_out = (tokens.astype(jnp.float32) + summed).astype(jnp.bfloat16)
    received_high = lax.all_to_all(send_high, ("req", "core"), 0, 0, tiled=True)
    half_rows = PAGE // 2
    pool = place_pages(from_req, from_rank, received_keys, slot_count, cores, 0, 0, PAGE)
    pool = place_pages(
        from_req, from_rank, received_low, slot_count, cores, 1, 0, half_rows, into=(pool,),
        paired=True,
    )
    pool = place_pages(
        from_req, from_rank, received_high, slot_count, cores, 1, 1, half_rows, into=(pool,)
    )
    return (layer_out, pool[:, None])


def solution(mesh):
    req_count, tp_count = mesh.devices.shape
    cores = tp_count // HG
    split_mesh = Mesh(mesh.devices.reshape(req_count, HG, cores), ("req", "y", "core"))
    tp = ("y", "core")
    placed = (
        P("req", tp),
        P(tp),
        P(None, tp),
        P(None, tp),
        P(None, tp),
        P(tp, None),
        P("req", tp),
        P("req", tp),
        P("req", None),
        P("req", None),
        P("req", None),
    )
    return jax.shard_map(
        shards,
        mesh=split_mesh,
        in_specs=placed,
        out_specs=(P("req", tp), P("req", tp, None, None)),
        check_vma=False,
    )
```

```python
import math

import jax
import jax.numpy as jnp
from jax import lax
from jax.experimental import pallas as pl
from jax.experimental.pallas import tpu as pltpu
from jax.sharding import Mesh
from jax.sharding import PartitionSpec as P

HD = 96
HG = 4
PAGE = 128
CAPACITY = 2


EPSILON = 1e-05
THETA = 10000.0


def rotate(values, positions, head_size):
    count = values.shape[0]
    half_size = head_size // 2
    shaped = values.reshape(count, -1, head_size)
    freqs = jnp.exp(-math.log(THETA) * 2.0 * jnp.arange(half_size, dtype=jnp.float32) / head_size)
    angles = positions.astype(jnp.float32)[:, None] * freqs[None, :]
    cosine = jnp.cos(angles)[:, None, :]
    sine = jnp.sin(angles)[:, None, :]
    first = shaped[:, :, :half_size]
    second = shaped[:, :, half_size:]
    turned = jnp.concatenate(
        [first * cosine - second * sine, second * cosine + first * sine], axis=2
    )
    return turned.reshape(count, -1)


def request_ids(lengths, count):
    ends = jnp.cumsum(lengths)
    row_index = jnp.arange(count, dtype=jnp.int32)
    return jnp.sum((row_index[:, None] >= ends[None, :]).astype(jnp.int32), axis=1)


def block_layout(earlier, fresh, count):
    owners = request_ids(fresh, count)
    starts = jnp.cumsum(fresh) - fresh
    onehot = (owners[:, None] == jnp.arange(fresh.shape[0], dtype=jnp.int32)[None, :]).astype(
        jnp.int32
    )
    first_row = jnp.sum(onehot * starts[None, :], axis=1)
    before = jnp.sum(onehot * earlier[None, :], axis=1)
    row_index = jnp.arange(count, dtype=jnp.int32)
    return (owners, before + row_index - first_row)


def visible(earlier, owners, prev_count, count):
    prev_owner = request_ids(earlier, prev_count)
    row_index = jnp.arange(count, dtype=jnp.int32)
    old_part = owners[:, None] == prev_owner[None, :]
    new_part = (owners[:, None] == owners[None, :]) & (row_index[None, :] <= row_index[:, None])
    return jnp.concatenate([old_part, new_part], axis=1)


def rank_in_dest(dests):
    same = (dests[..., :, None] == dests[..., None, :]).astype(jnp.int32)
    count = dests.shape[-1]
    order_index = jnp.arange(count, dtype=jnp.int32)
    earlier_mask = (order_index[None, :] < order_index[:, None]).astype(jnp.int32)
    return jnp.sum(same * earlier_mask, axis=-1)


def pack_pages(slots, sources, parts, slot_total, into=(), shapes=None, paired=()):
    page_total = sources[0].shape[0] // PAGE
    width = sources[0].shape[1]

    def body(slot_ref, *rest):
        blocks = rest[: len(sources)]
        outs = rest[len(rest) - len(parts) :]
        for out, (which, start, rows) in zip(outs, parts):
            out[0] = blocks[which][start : start + rows]

    in_specs = [pl.BlockSpec((PAGE, width), lambda page, slot_ref: (page, 0))] * len(sources)
    in_specs += [pl.BlockSpec(memory_space=pl.ANY)] * len(into)
    if shapes is None:
        shapes = [rows for _, _, rows in parts]
    out_shape = tuple(
        jax.ShapeDtypeStruct(
            (slot_total // CAPACITY if index in paired else slot_total, full, width),
            jnp.bfloat16,
        )
        for index, full in enumerate(shapes)
    )

    def out_map(index):
        if index in paired:
            return lambda page, slot_ref: (
                slot_ref[page] // CAPACITY,
                slot_ref[page] % CAPACITY,
                0,
            )
        return lambda page, slot_ref: (slot_ref[page], 0, 0)

    out_specs = tuple(
        pl.BlockSpec((1, rows, width), out_map(index)) for index, (_, _, rows) in enumerate(parts)
    )
    first_alias = 1 + len(sources)
    return pl.pallas_call(
        body,
        out_shape=out_shape,
        grid_spec=pltpu.PrefetchScalarGridSpec(
            num_scalar_prefetch=1,
            grid=(page_total,),
            in_specs=in_specs,
            out_specs=out_specs,
        ),
        input_output_aliases={first_alias + i: out for i, out in enumerate(into)},
    )(slots, *sources, *into.values())


def stamp_tags(tags, first_row):
    dest_total, tag_rows, width = tags.shape

    def body(tag_block, out):
        out[...] = tag_block[...]

    return pl.pallas_call(
        body,
        out_shape=jax.ShapeDtypeStruct((dest_total, first_row + tag_rows, width), jnp.bfloat16),
        grid=(1,),
        in_specs=[pl.BlockSpec((dest_total, tag_rows, width), lambda step: (0, 0, 0))],
        out_specs=pl.BlockSpec(
            (dest_total, tag_rows, width), lambda step: (0, first_row // tag_rows, 0)
        ),
    )(tags)


def place_pages(
    sources, ranks, received, slot_count, cores, part, row_block, rows, into=(), group=9,
    paired=False,
):
    stored, width = received.shape[-2:]
    if paired:
        shaped = received.reshape(-1, cores, stored, width)
        block = (1, cores, rows, width)
    else:
        shaped = received.reshape(-1, cores, CAPACITY, stored, width)
        block = (1, cores, 1, rows, width)

    def body(src_ref, rank_ref, *refs):
        out = refs[-1]
        for member in range(group):
            for core in range(cores):
                piece = refs[member][0, core] if paired else refs[member][0, core, 0]
                out[member, :, core * width : (core + 1) * width] = piece

    def source_map(member):
        if paired:
            return lambda step, src_ref, rank_ref: (
                src_ref[step * group + member],
                0,
                rank_ref[step * group + member],
                0,
            )
        return lambda step, src_ref, rank_ref: (
            src_ref[step * group + member],
            0,
            rank_ref[step * group + member],
            0,
            0,
        )

    in_specs = [
        pl.BlockSpec(block, source_map(member)) for member in range(group)
    ] + [pl.BlockSpec(memory_space=pl.ANY)] * len(into)
    return pl.pallas_call(
        body,
        out_shape=jax.ShapeDtypeStruct((slot_count, PAGE, 2 * cores * width), jnp.bfloat16),
        grid_spec=pltpu.PrefetchScalarGridSpec(
            num_scalar_prefetch=2,
            grid=(slot_count // group,),
            in_specs=in_specs,
            out_specs=pl.BlockSpec(
                (group, rows, cores * width),
                lambda step, src_ref, rank_ref: (step, row_block, part),
            ),
        ),
        input_output_aliases={2 + group + i: 0 for i in range(len(into))},
    )(sources, ranks, *([shaped] * group), *into)


def shards(
    tokens,
    norm_gain,
    w_query,
    w_key,
    w_value,
    w_out,
    prev_keys,
    prev_values,
    earlier_lengths,
    new_lengths,
    page_table,
):
    token_count, local_width = tokens.shape
    full_width = w_query.shape[0]
    prev_count = prev_keys.shape[0]
    req_count = lax.axis_size("req")
    cores = lax.axis_size("core")
    my_req = lax.axis_index("req")
    my_core = lax.axis_index("core")

    spare = 16
    riders = jnp.zeros((spare, local_width), tokens.dtype).at[0].set(norm_gain)
    gathered = lax.all_gather(
        jnp.concatenate([tokens, riders], axis=0), ("y", "core"), axis=1, tiled=True
    )
    full_tokens = gathered[:token_count]
    full_gain = gathered[token_count]
    widened = full_tokens.astype(jnp.float32)
    mean_square = jnp.mean(widened * widened, axis=1, keepdims=True)
    normed = (widened * lax.rsqrt(mean_square + EPSILON) * full_gain.astype(jnp.float32)[None, :]).astype(
        jnp.bfloat16
    )
    value_raw = jnp.dot(normed, w_value, preferred_element_type=jnp.float32)
    earlier = earlier_lengths[0]
    fresh = new_lengths[0]
    owners, positions = block_layout(earlier, fresh, token_count)
    new_values = value_raw.astype(jnp.bfloat16)

    page_total = (prev_count + token_count) // PAGE
    slot_count = page_total // cores
    dest_count = req_count * cores
    slot_total = dest_count * CAPACITY
    own_dests = page_table[0] // slot_count
    own_ranks = rank_in_dest(own_dests)
    send_slots = (own_dests * CAPACITY + own_ranks).astype(jnp.int32)
    prev_pages = prev_count // PAGE
    whole = ((0, 0, PAGE),)
    halves = ((0, 0, PAGE // 2), (0, PAGE // 2, PAGE // 2))
    both = ((0, 0, PAGE), (1, 0, PAGE // 2), (1, PAGE // 2, PAGE // 2))
    half_rows = PAGE // 2
    tag_rows = 16
    carried = (
        jnp.full((slot_total,), slot_count, jnp.int32)
        .at[send_slots]
        .set((page_table[0] % slot_count).astype(jnp.int32))
    )
    tags = jnp.zeros((dest_count, tag_rows, local_width), jnp.bfloat16)
    tags = tags.at[:, 0, :CAPACITY].set(
        carried.reshape(dest_count, CAPACITY).astype(jnp.bfloat16)
    )
    send_low = stamp_tags(tags, CAPACITY * half_rows)
    send_keys, send_low, send_high = pack_pages(
        send_slots[:prev_pages],
        (prev_keys, prev_values),
        both,
        slot_total,
        into={1: send_low},
        shapes=(PAGE, CAPACITY * half_rows + tag_rows, half_rows),
        paired=(1,),
    )
    send_low, send_high = pack_pages(
        send_slots[prev_pages:],
        (new_values,),
        halves,
        slot_total,
        into={0: send_low, 1: send_high},
        shapes=(CAPACITY * half_rows + tag_rows, half_rows),
        paired=(0,),
    )
    send_keys, send_low, send_high, normed, new_values = lax.optimization_barrier(
        (send_keys, send_low, send_high, normed, new_values)
    )
    received_low = lax.all_to_all(send_low, ("req", "core"), 0, 0, tiled=True)
    carried = received_low[:, CAPACITY * half_rows, :CAPACITY].astype(jnp.int32)
    carried = carried.reshape(req_count, cores, CAPACITY)[:, 0, :].reshape(-1)
    wanted = jnp.arange(slot_count, dtype=jnp.int32)
    found = jnp.argmax(carried[None, :] == wanted[:, None], axis=1).astype(jnp.int32)
    from_req = found // CAPACITY
    from_rank = found % CAPACITY
    key_raw = jnp.dot(normed, w_key, preferred_element_type=jnp.float32)
    new_keys = rotate(key_raw, positions, HD).astype(jnp.bfloat16)
    (send_keys,) = pack_pages(
        send_slots[prev_pages:], (new_keys,), whole, slot_total, into={0: send_keys}
    )
    keys_all = jnp.concatenate([prev_keys, new_keys], axis=0)
    values_all = jnp.concatenate([prev_values, new_values], axis=0)
    query_raw = jnp.dot(normed, w_query, preferred_element_type=jnp.float32)
    queries = rotate(query_raw, positions, HD).astype(jnp.bfloat16)
    received_keys = lax.all_to_all(send_keys, ("req", "core"), 0, 0, tiled=True)

    allowed = visible(earlier, owners, prev_count, token_count)
    heads_here = local_width // HD
    scores = jnp.einsum(
        "qhd,khd->hqk",
        queries.reshape(token_count, heads_here, HD),
        keys_all.reshape(-1, heads_here, HD),
        preferred_element_type=jnp.float32,
    ) * HD ** (-0.5)
    scores = jnp.where(allowed[None, :, :], scores, -1e30)
    row_peak = jnp.max(scores, axis=2, keepdims=True)
    weights = jnp.exp(scores - row_peak)
    totals = jnp.sum(weights, axis=2)
    prob_rows = weights.astype(jnp.bfloat16)
    mixture = jnp.einsum(
        "hqk,khd->qhd",
        prob_rows,
        values_all.reshape(-1, heads_here, HD),
        preferred_element_type=jnp.float32,
    )
    attended = (
        (mixture / totals.T[:, :, None]).astype(jnp.bfloat16).reshape(token_count, local_width)
    )
    projected = jnp.dot(attended, w_out, preferred_element_type=jnp.float32)
    received_keys, received_low, projected, send_high = lax.optimization_barrier(
        (received_keys, received_low, projected, send_high)
    )
    summed = lax.psum_scatter(projected, ("y", "core"), scatter_dimension=1, tiled=True)
    layer_out = (tokens.astype(jnp.float32) + summed).astype(jnp.bfloat16)
    received_high = lax.all_to_all(send_high, ("req", "core"), 0, 0, tiled=True)
    half_rows = PAGE // 2
    pool = place_pages(from_req, from_rank, received_keys, slot_count, cores, 0, 0, PAGE)
    pool = place_pages(
        from_req, from_rank, received_low, slot_count, cores, 1, 0, half_rows, into=(pool,),
        paired=True,
    )
    pool = place_pages(
        from_req, from_rank, received_high, slot_count, cores, 1, 1, half_rows, into=(pool,)
    )
    return (layer_out, pool[:, None])


def solution(mesh):
    req_count, tp_count = mesh.devices.shape
    cores = tp_count // HG
    split_mesh = Mesh(mesh.devices.reshape(req_count, HG, cores), ("req", "y", "core"))
    tp = ("y", "core")
    placed = (
        P("req", tp),
        P(tp),
        P(None, tp),
        P(None, tp),
        P(None, tp),
        P(tp, None),
        P("req", tp),
        P("req", tp),
        P("req", None),
        P("req", None),
        P("req", None),
    )
    return jax.shard_map(
        shards,
        mesh=split_mesh,
        in_specs=placed,
        out_specs=(P("req", tp), P("req", tp, None, None)),
        check_vma=False,
    )
```

```python
import math

import jax
import jax.numpy as jnp
from jax import lax
from jax.experimental import pallas as pl
from jax.experimental.pallas import tpu as pltpu
from jax.sharding import Mesh
from jax.sharding import PartitionSpec as P

HD = 96
HG = 4
PAGE = 128
CAPACITY = 2


EPSILON = 1e-05
THETA = 10000.0


def rotate(values, positions, head_size):
    count = values.shape[0]
    half_size = head_size // 2
    shaped = values.reshape(count, -1, head_size)
    freqs = jnp.exp(-math.log(THETA) * 2.0 * jnp.arange(half_size, dtype=jnp.float32) / head_size)
    angles = positions.astype(jnp.float32)[:, None] * freqs[None, :]
    cosine = jnp.cos(angles)[:, None, :]
    sine = jnp.sin(angles)[:, None, :]
    first = shaped[:, :, :half_size]
    second = shaped[:, :, half_size:]
    turned = jnp.concatenate(
        [first * cosine - second * sine, second * cosine + first * sine], axis=2
    )
    return turned.reshape(count, -1)


def request_ids(lengths, count):
    ends = jnp.cumsum(lengths)
    row_index = jnp.arange(count, dtype=jnp.int32)
    return jnp.sum((row_index[:, None] >= ends[None, :]).astype(jnp.int32), axis=1)


def block_layout(earlier, fresh, count):
    owners = request_ids(fresh, count)
    starts = jnp.cumsum(fresh) - fresh
    onehot = (owners[:, None] == jnp.arange(fresh.shape[0], dtype=jnp.int32)[None, :]).astype(
        jnp.int32
    )
    first_row = jnp.sum(onehot * starts[None, :], axis=1)
    before = jnp.sum(onehot * earlier[None, :], axis=1)
    row_index = jnp.arange(count, dtype=jnp.int32)
    return (owners, before + row_index - first_row)


def visible(earlier, owners, prev_count, count):
    prev_owner = request_ids(earlier, prev_count)
    row_index = jnp.arange(count, dtype=jnp.int32)
    old_part = owners[:, None] == prev_owner[None, :]
    new_part = (owners[:, None] == owners[None, :]) & (row_index[None, :] <= row_index[:, None])
    return jnp.concatenate([old_part, new_part], axis=1)


def rank_in_dest(dests):
    same = (dests[..., :, None] == dests[..., None, :]).astype(jnp.int32)
    count = dests.shape[-1]
    order_index = jnp.arange(count, dtype=jnp.int32)
    earlier_mask = (order_index[None, :] < order_index[:, None]).astype(jnp.int32)
    return jnp.sum(same * earlier_mask, axis=-1)


def pack_pages(slots, sources, parts, slot_total, into=(), shapes=None, paired=()):
    page_total = sources[0].shape[0] // PAGE
    width = sources[0].shape[1]

    def body(slot_ref, *rest):
        blocks = rest[: len(sources)]
        outs = rest[len(rest) - len(parts) :]
        for out, (which, start, rows) in zip(outs, parts):
            out[0] = blocks[which][start : start + rows]

    in_specs = [pl.BlockSpec((PAGE, width), lambda page, slot_ref: (page, 0))] * len(sources)
    in_specs += [pl.BlockSpec(memory_space=pl.ANY)] * len(into)
    if shapes is None:
        shapes = [rows for _, _, rows in parts]
    out_shape = tuple(
        jax.ShapeDtypeStruct(
            (slot_total // CAPACITY if index in paired else slot_total, full, width),
            jnp.bfloat16,
        )
        for index, full in enumerate(shapes)
    )

    def out_map(index):
        if index in paired:
            return lambda page, slot_ref: (
                slot_ref[page] // CAPACITY,
                slot_ref[page] % CAPACITY,
                0,
            )
        return lambda page, slot_ref: (slot_ref[page], 0, 0)

    out_specs = tuple(
        pl.BlockSpec((1, rows, width), out_map(index)) for index, (_, _, rows) in enumerate(parts)
    )
    first_alias = 1 + len(sources)
    return pl.pallas_call(
        body,
        out_shape=out_shape,
        grid_spec=pltpu.PrefetchScalarGridSpec(
            num_scalar_prefetch=1,
            grid=(page_total,),
            in_specs=in_specs,
            out_specs=out_specs,
        ),
        input_output_aliases={first_alias + i: out for i, out in enumerate(into)},
    )(slots, *sources, *into.values())


def stamp_tags(tags, first_row):
    dest_total, tag_rows, width = tags.shape

    def body(tag_block, out):
        out[...] = tag_block[...]

    return pl.pallas_call(
        body,
        out_shape=jax.ShapeDtypeStruct((dest_total, first_row + tag_rows, width), jnp.bfloat16),
        grid=(1,),
        in_specs=[pl.BlockSpec((dest_total, tag_rows, width), lambda step: (0, 0, 0))],
        out_specs=pl.BlockSpec(
            (dest_total, tag_rows, width), lambda step: (0, first_row // tag_rows, 0)
        ),
    )(tags)


def place_pages(
    sources, ranks, received, slot_count, cores, part, row_block, rows, into=(), group=9,
    paired=False,
):
    stored, width = received.shape[-2:]
    if paired:
        shaped = received.reshape(-1, cores, stored, width)
        block = (1, cores, rows, width)
    else:
        shaped = received.reshape(-1, cores, CAPACITY, stored, width)
        block = (1, cores, 1, rows, width)

    def body(src_ref, rank_ref, *refs):
        out = refs[-1]
        for member in range(group):
            for core in range(cores):
                piece = refs[member][0, core] if paired else refs[member][0, core, 0]
                out[member, :, core * width : (core + 1) * width] = piece

    def source_map(member):
        if paired:
            return lambda step, src_ref, rank_ref: (
                src_ref[step * group + member],
                0,
                rank_ref[step * group + member],
                0,
            )
        return lambda step, src_ref, rank_ref: (
            src_ref[step * group + member],
            0,
            rank_ref[step * group + member],
            0,
            0,
        )

    in_specs = [
        pl.BlockSpec(block, source_map(member)) for member in range(group)
    ] + [pl.BlockSpec(memory_space=pl.ANY)] * len(into)
    return pl.pallas_call(
        body,
        out_shape=jax.ShapeDtypeStruct((slot_count, PAGE, 2 * cores * width), jnp.bfloat16),
        grid_spec=pltpu.PrefetchScalarGridSpec(
            num_scalar_prefetch=2,
            grid=(slot_count // group,),
            in_specs=in_specs,
            out_specs=pl.BlockSpec(
                (group, rows, cores * width),
                lambda step, src_ref, rank_ref: (step, row_block, part),
            ),
        ),
        input_output_aliases={2 + group + i: 0 for i in range(len(into))},
    )(sources, ranks, *([shaped] * group), *into)


def shards(
    tokens,
    norm_gain,
    w_query,
    w_key,
    w_value,
    w_out,
    prev_keys,
    prev_values,
    earlier_lengths,
    new_lengths,
    page_table,
):
    token_count, local_width = tokens.shape
    full_width = w_query.shape[0]
    prev_count = prev_keys.shape[0]
    req_count = lax.axis_size("req")
    cores = lax.axis_size("core")
    my_req = lax.axis_index("req")
    my_core = lax.axis_index("core")

    spare = 16
    riders = jnp.zeros((spare, local_width), tokens.dtype).at[0].set(norm_gain)
    half = token_count // 2
    first = lax.all_gather(
        jnp.concatenate([tokens[:half], riders], axis=0), ("y", "core"), axis=1, tiled=True
    )
    second = lax.all_gather(tokens[half:], ("y", "core"), axis=1, tiled=True)
    full_gain = first[half].astype(jnp.float32)

    def normalize(rows):
        widened = rows.astype(jnp.float32)
        mean_square = jnp.mean(widened * widened, axis=1, keepdims=True)
        return (widened * lax.rsqrt(mean_square + EPSILON) * full_gain[None, :]).astype(
            jnp.bfloat16
        )

    normed_parts = (normalize(first[:half]), normalize(second))
    value_raw = jnp.concatenate(
        [jnp.dot(part, w_value, preferred_element_type=jnp.float32) for part in normed_parts],
        axis=0,
    )
    normed = jnp.concatenate(normed_parts, axis=0)
    earlier = earlier_lengths[0]
    fresh = new_lengths[0]
    owners, positions = block_layout(earlier, fresh, token_count)
    new_values = value_raw.astype(jnp.bfloat16)

    page_total = (prev_count + token_count) // PAGE
    slot_count = page_total // cores
    dest_count = req_count * cores
    slot_total = dest_count * CAPACITY
    own_dests = page_table[0] // slot_count
    own_ranks = rank_in_dest(own_dests)
    send_slots = (own_dests * CAPACITY + own_ranks).astype(jnp.int32)
    prev_pages = prev_count // PAGE
    whole = ((0, 0, PAGE),)
    halves = ((0, 0, PAGE // 2), (0, PAGE // 2, PAGE // 2))
    both = ((0, 0, PAGE), (1, 0, PAGE // 2), (1, PAGE // 2, PAGE // 2))
    half_rows = PAGE // 2
    tag_rows = 16
    carried = (
        jnp.full((slot_total,), slot_count, jnp.int32)
        .at[send_slots]
        .set((page_table[0] % slot_count).astype(jnp.int32))
    )
    tags = jnp.zeros((dest_count, tag_rows, local_width), jnp.bfloat16)
    tags = tags.at[:, 0, :CAPACITY].set(
        carried.reshape(dest_count, CAPACITY).astype(jnp.bfloat16)
    )
    send_low = stamp_tags(tags, CAPACITY * half_rows)
    send_keys, send_low, send_high = pack_pages(
        send_slots[:prev_pages],
        (prev_keys, prev_values),
        both,
        slot_total,
        into={1: send_low},
        shapes=(PAGE, CAPACITY * half_rows + tag_rows, half_rows),
        paired=(1,),
    )
    send_low, send_high = pack_pages(
        send_slots[prev_pages:],
        (new_values,),
        halves,
        slot_total,
        into={0: send_low, 1: send_high},
        shapes=(CAPACITY * half_rows + tag_rows, half_rows),
        paired=(0,),
    )
    send_keys, send_low, send_high, normed, new_values = lax.optimization_barrier(
        (send_keys, send_low, send_high, normed, new_values)
    )
    received_low = lax.all_to_all(send_low, ("req", "core"), 0, 0, tiled=True)
    carried = received_low[:, CAPACITY * half_rows, :CAPACITY].astype(jnp.int32)
    carried = carried.reshape(req_count, cores, CAPACITY)[:, 0, :].reshape(-1)
    wanted = jnp.arange(slot_count, dtype=jnp.int32)
    found = jnp.argmax(carried[None, :] == wanted[:, None], axis=1).astype(jnp.int32)
    from_req = found // CAPACITY
    from_rank = found % CAPACITY
    key_raw = jnp.dot(normed, w_key, preferred_element_type=jnp.float32)
    new_keys = rotate(key_raw, positions, HD).astype(jnp.bfloat16)
    (send_keys,) = pack_pages(
        send_slots[prev_pages:], (new_keys,), whole, slot_total, into={0: send_keys}
    )
    keys_all = jnp.concatenate([prev_keys, new_keys], axis=0)
    values_all = jnp.concatenate([prev_values, new_values], axis=0)
    query_raw = jnp.dot(normed, w_query, preferred_element_type=jnp.float32)
    queries = rotate(query_raw, positions, HD).astype(jnp.bfloat16)
    received_keys = lax.all_to_all(send_keys, ("req", "core"), 0, 0, tiled=True)

    allowed = visible(earlier, owners, prev_count, token_count)
    heads_here = local_width // HD
    scores = jnp.einsum(
        "qhd,khd->hqk",
        queries.reshape(token_count, heads_here, HD),
        keys_all.reshape(-1, heads_here, HD),
        preferred_element_type=jnp.float32,
    ) * HD ** (-0.5)
    scores = jnp.where(allowed[None, :, :], scores, -1e30)
    row_peak = jnp.max(scores, axis=2, keepdims=True)
    weights = jnp.exp(scores - row_peak)
    totals = jnp.sum(weights, axis=2)
    prob_rows = weights.astype(jnp.bfloat16)
    mixture = jnp.einsum(
        "hqk,khd->qhd",
        prob_rows,
        values_all.reshape(-1, heads_here, HD),
        preferred_element_type=jnp.float32,
    )
    attended = (
        (mixture / totals.T[:, :, None]).astype(jnp.bfloat16).reshape(token_count, local_width)
    )
    projected = jnp.dot(attended, w_out, preferred_element_type=jnp.float32)
    received_keys, received_low, projected, send_high = lax.optimization_barrier(
        (received_keys, received_low, projected, send_high)
    )
    summed = lax.psum_scatter(projected, ("y", "core"), scatter_dimension=1, tiled=True)
    layer_out = (tokens.astype(jnp.float32) + summed).astype(jnp.bfloat16)
    received_high = lax.all_to_all(send_high, ("req", "core"), 0, 0, tiled=True)
    half_rows = PAGE // 2
    pool = place_pages(from_req, from_rank, received_keys, slot_count, cores, 0, 0, PAGE)
    pool = place_pages(
        from_req, from_rank, received_low, slot_count, cores, 1, 0, half_rows, into=(pool,),
        paired=True,
    )
    pool = place_pages(
        from_req, from_rank, received_high, slot_count, cores, 1, 1, half_rows, into=(pool,)
    )
    return (layer_out, pool[:, None])


def solution(mesh):
    req_count, tp_count = mesh.devices.shape
    cores = tp_count // HG
    split_mesh = Mesh(mesh.devices.reshape(req_count, HG, cores), ("req", "y", "core"))
    tp = ("y", "core")
    placed = (
        P("req", tp),
        P(tp),
        P(None, tp),
        P(None, tp),
        P(None, tp),
        P(tp, None),
        P("req", tp),
        P("req", tp),
        P("req", None),
        P("req", None),
        P("req", None),
    )
    return jax.shard_map(
        shards,
        mesh=split_mesh,
        in_specs=placed,
        out_specs=(P("req", tp), P("req", tp, None, None)),
        check_vma=False,
    )
```

```python
import math

import jax
import jax.numpy as jnp
from jax import lax
from jax.experimental import pallas as pl
from jax.experimental.pallas import tpu as pltpu
from jax.sharding import Mesh
from jax.sharding import PartitionSpec as P

HD = 96
HG = 4
PAGE = 128
CAPACITY = 2


EPSILON = 1e-05
THETA = 10000.0


def rotate(values, positions, head_size):
    count = values.shape[0]
    half_size = head_size // 2
    shaped = values.reshape(count, -1, head_size)
    freqs = jnp.exp(-math.log(THETA) * 2.0 * jnp.arange(half_size, dtype=jnp.float32) / head_size)
    angles = positions.astype(jnp.float32)[:, None] * freqs[None, :]
    cosine = jnp.cos(angles)[:, None, :]
    sine = jnp.sin(angles)[:, None, :]
    first = shaped[:, :, :half_size]
    second = shaped[:, :, half_size:]
    turned = jnp.concatenate(
        [first * cosine - second * sine, second * cosine + first * sine], axis=2
    )
    return turned.reshape(count, -1)


def request_ids(lengths, count):
    ends = jnp.cumsum(lengths)
    row_index = jnp.arange(count, dtype=jnp.int32)
    return jnp.sum((row_index[:, None] >= ends[None, :]).astype(jnp.int32), axis=1)


def block_layout(earlier, fresh, count):
    owners = request_ids(fresh, count)
    starts = jnp.cumsum(fresh) - fresh
    onehot = (owners[:, None] == jnp.arange(fresh.shape[0], dtype=jnp.int32)[None, :]).astype(
        jnp.int32
    )
    first_row = jnp.sum(onehot * starts[None, :], axis=1)
    before = jnp.sum(onehot * earlier[None, :], axis=1)
    row_index = jnp.arange(count, dtype=jnp.int32)
    return (owners, before + row_index - first_row)


def visible(earlier, owners, prev_count, count):
    prev_owner = request_ids(earlier, prev_count)
    row_index = jnp.arange(count, dtype=jnp.int32)
    old_part = owners[:, None] == prev_owner[None, :]
    new_part = (owners[:, None] == owners[None, :]) & (row_index[None, :] <= row_index[:, None])
    return jnp.concatenate([old_part, new_part], axis=1)


def rank_in_dest(dests):
    same = (dests[..., :, None] == dests[..., None, :]).astype(jnp.int32)
    count = dests.shape[-1]
    order_index = jnp.arange(count, dtype=jnp.int32)
    earlier_mask = (order_index[None, :] < order_index[:, None]).astype(jnp.int32)
    return jnp.sum(same * earlier_mask, axis=-1)


def pack_pages(slots, sources, parts, slot_total, into=(), shapes=None, paired=()):
    page_total = sources[0].shape[0] // PAGE
    width = sources[0].shape[1]

    def body(slot_ref, *rest):
        blocks = rest[: len(sources)]
        outs = rest[len(rest) - len(parts) :]
        for out, (which, start, rows) in zip(outs, parts):
            out[0] = blocks[which][start : start + rows]

    in_specs = [pl.BlockSpec((PAGE, width), lambda page, slot_ref: (page, 0))] * len(sources)
    in_specs += [pl.BlockSpec(memory_space=pl.ANY)] * len(into)
    if shapes is None:
        shapes = [rows for _, _, rows in parts]
    out_shape = tuple(
        jax.ShapeDtypeStruct(
            (slot_total // CAPACITY if index in paired else slot_total, full, width),
            jnp.bfloat16,
        )
        for index, full in enumerate(shapes)
    )

    def out_map(index):
        if index in paired:
            return lambda page, slot_ref: (
                slot_ref[page] // CAPACITY,
                slot_ref[page] % CAPACITY,
                0,
            )
        return lambda page, slot_ref: (slot_ref[page], 0, 0)

    out_specs = tuple(
        pl.BlockSpec((1, rows, width), out_map(index)) for index, (_, _, rows) in enumerate(parts)
    )
    first_alias = 1 + len(sources)
    return pl.pallas_call(
        body,
        out_shape=out_shape,
        grid_spec=pltpu.PrefetchScalarGridSpec(
            num_scalar_prefetch=1,
            grid=(page_total,),
            in_specs=in_specs,
            out_specs=out_specs,
        ),
        input_output_aliases={first_alias + i: out for i, out in enumerate(into)},
    )(slots, *sources, *into.values())


def stamp_tags(tags, first_row):
    dest_total, tag_rows, width = tags.shape

    def body(tag_block, out):
        out[...] = tag_block[...]

    return pl.pallas_call(
        body,
        out_shape=jax.ShapeDtypeStruct((dest_total, first_row + tag_rows, width), jnp.bfloat16),
        grid=(1,),
        in_specs=[pl.BlockSpec((dest_total, tag_rows, width), lambda step: (0, 0, 0))],
        out_specs=pl.BlockSpec(
            (dest_total, tag_rows, width), lambda step: (0, first_row // tag_rows, 0)
        ),
    )(tags)


def place_pages(
    sources, ranks, received, slot_count, cores, part, row_block, rows, into=(), group=9,
    paired=False,
):
    stored, width = received.shape[-2:]
    if paired:
        shaped = received.reshape(-1, cores, stored, width)
        block = (1, cores, rows, width)
    else:
        shaped = received.reshape(-1, cores, CAPACITY, stored, width)
        block = (1, cores, 1, rows, width)

    def body(src_ref, rank_ref, *refs):
        out = refs[-1]
        for member in range(group):
            for core in range(cores):
                piece = refs[member][0, core] if paired else refs[member][0, core, 0]
                out[member, :, core * width : (core + 1) * width] = piece

    def source_map(member):
        if paired:
            return lambda step, src_ref, rank_ref: (
                src_ref[step * group + member],
                0,
                rank_ref[step * group + member],
                0,
            )
        return lambda step, src_ref, rank_ref: (
            src_ref[step * group + member],
            0,
            rank_ref[step * group + member],
            0,
            0,
        )

    in_specs = [
        pl.BlockSpec(block, source_map(member)) for member in range(group)
    ] + [pl.BlockSpec(memory_space=pl.ANY)] * len(into)
    return pl.pallas_call(
        body,
        out_shape=jax.ShapeDtypeStruct((slot_count, PAGE, 2 * cores * width), jnp.bfloat16),
        grid_spec=pltpu.PrefetchScalarGridSpec(
            num_scalar_prefetch=2,
            grid=(slot_count // group,),
            in_specs=in_specs,
            out_specs=pl.BlockSpec(
                (group, rows, cores * width),
                lambda step, src_ref, rank_ref: (step, row_block, part),
            ),
        ),
        input_output_aliases={2 + group + i: 0 for i in range(len(into))},
    )(sources, ranks, *([shaped] * group), *into)


def shards(
    tokens,
    norm_gain,
    w_query,
    w_key,
    w_value,
    w_out,
    prev_keys,
    prev_values,
    earlier_lengths,
    new_lengths,
    page_table,
):
    token_count, local_width = tokens.shape
    full_width = w_query.shape[0]
    prev_count = prev_keys.shape[0]
    req_count = lax.axis_size("req")
    cores = lax.axis_size("core")
    my_req = lax.axis_index("req")
    my_core = lax.axis_index("core")

    spare = 16
    riders = jnp.zeros((spare, local_width), tokens.dtype).at[0].set(norm_gain)
    gathered = lax.all_gather(
        jnp.concatenate([tokens, riders], axis=0), ("y", "core"), axis=1, tiled=True
    )
    full_tokens = gathered[:token_count]
    full_gain = gathered[token_count]
    widened = full_tokens.astype(jnp.float32)
    mean_square = jnp.mean(widened * widened, axis=1, keepdims=True)
    normed = (widened * lax.rsqrt(mean_square + EPSILON) * full_gain.astype(jnp.float32)[None, :]).astype(
        jnp.bfloat16
    )
    value_raw = jnp.dot(normed, w_value, preferred_element_type=jnp.float32)
    earlier = earlier_lengths[0]
    fresh = new_lengths[0]
    owners, positions = block_layout(earlier, fresh, token_count)
    new_values = value_raw.astype(jnp.bfloat16)

    page_total = (prev_count + token_count) // PAGE
    slot_count = page_total // cores
    dest_count = req_count * cores
    slot_total = dest_count * CAPACITY
    own_dests = page_table[0] // slot_count
    own_ranks = rank_in_dest(own_dests)
    send_slots = (own_dests * CAPACITY + own_ranks).astype(jnp.int32)
    prev_pages = prev_count // PAGE
    whole = ((0, 0, PAGE),)
    halves = ((0, 0, PAGE // 2), (0, PAGE // 2, PAGE // 2))
    both = ((0, 0, PAGE), (1, 0, PAGE // 2), (1, PAGE // 2, PAGE // 2))
    half_rows = PAGE // 2
    tag_rows = 16
    carried = (
        jnp.full((slot_total,), slot_count, jnp.int32)
        .at[send_slots]
        .set((page_table[0] % slot_count).astype(jnp.int32))
    )
    tags = jnp.zeros((dest_count, tag_rows, local_width), jnp.bfloat16)
    tags = tags.at[:, 0, :CAPACITY].set(
        carried.reshape(dest_count, CAPACITY).astype(jnp.bfloat16)
    )
    send_low = stamp_tags(tags, CAPACITY * half_rows)
    send_keys, send_low, send_high = pack_pages(
        send_slots[:prev_pages],
        (prev_keys, prev_values),
        both,
        slot_total,
        into={1: send_low},
        shapes=(PAGE, CAPACITY * half_rows + tag_rows, half_rows),
        paired=(1,),
    )
    send_low, send_high = pack_pages(
        send_slots[prev_pages:],
        (new_values,),
        halves,
        slot_total,
        into={0: send_low, 1: send_high},
        shapes=(CAPACITY * half_rows + tag_rows, half_rows),
        paired=(0,),
    )
    send_keys, send_low, send_high, normed, new_values = lax.optimization_barrier(
        (send_keys, send_low, send_high, normed, new_values)
    )
    received_low = lax.all_to_all(send_low, ("req", "core"), 0, 0, tiled=True)
    carried = received_low[:, CAPACITY * half_rows, :CAPACITY].astype(jnp.int32)
    carried = carried.reshape(req_count, cores, CAPACITY)[:, 0, :].reshape(-1)
    wanted = jnp.arange(slot_count, dtype=jnp.int32)
    found = jnp.argmax(carried[None, :] == wanted[:, None], axis=1).astype(jnp.int32)
    from_req = found // CAPACITY
    from_rank = found % CAPACITY
    key_raw = jnp.dot(normed, w_key, preferred_element_type=jnp.float32)
    new_keys = rotate(key_raw, positions, HD).astype(jnp.bfloat16)
    (send_keys,) = pack_pages(
        send_slots[prev_pages:], (new_keys,), whole, slot_total, into={0: send_keys}
    )
    keys_all = jnp.concatenate([prev_keys, new_keys], axis=0)
    values_all = jnp.concatenate([prev_values, new_values], axis=0)
    query_raw = jnp.dot(normed, w_query, preferred_element_type=jnp.float32)
    queries = rotate(query_raw, positions, HD).astype(jnp.bfloat16)
    received_keys = lax.all_to_all(send_keys, ("req", "core"), 0, 0, tiled=True)

    allowed = visible(earlier, owners, prev_count, token_count)
    heads_here = local_width // HD
    scores = jnp.einsum(
        "qhd,khd->hqk",
        queries.reshape(token_count, heads_here, HD),
        keys_all.reshape(-1, heads_here, HD),
        preferred_element_type=jnp.float32,
    ) * HD ** (-0.5)
    scores = jnp.where(allowed[None, :, :], scores, -1e30)
    row_peak = jnp.max(scores, axis=2, keepdims=True)
    weights = jnp.exp(scores - row_peak)
    totals = jnp.sum(weights, axis=2)
    prob_rows = weights.astype(jnp.bfloat16)
    mixture = jnp.einsum(
        "hqk,khd->qhd",
        prob_rows,
        values_all.reshape(-1, heads_here, HD),
        preferred_element_type=jnp.float32,
    )
    attended = (
        (mixture / totals.T[:, :, None]).astype(jnp.bfloat16).reshape(token_count, local_width)
    )
    projected = jnp.dot(attended, w_out, preferred_element_type=jnp.float32)
    received_keys, received_low, projected, send_high = lax.optimization_barrier(
        (received_keys, received_low, projected, send_high)
    )
    summed = lax.psum_scatter(projected, ("y", "core"), scatter_dimension=1, tiled=True)
    layer_out = (tokens.astype(jnp.float32) + summed).astype(jnp.bfloat16)
    received_high = lax.all_to_all(send_high, ("req", "core"), 0, 0, tiled=True)
    received_high, layer_out = lax.optimization_barrier((received_high, layer_out))
    half_rows = PAGE // 2
    pool = place_pages(from_req, from_rank, received_keys, slot_count, cores, 0, 0, PAGE)
    pool = place_pages(
        from_req, from_rank, received_low, slot_count, cores, 1, 0, half_rows, into=(pool,),
        paired=True,
    )
    pool = place_pages(
        from_req, from_rank, received_high, slot_count, cores, 1, 1, half_rows, into=(pool,)
    )
    return (layer_out, pool[:, None])


def solution(mesh):
    req_count, tp_count = mesh.devices.shape
    cores = tp_count // HG
    split_mesh = Mesh(mesh.devices.reshape(req_count, HG, cores), ("req", "y", "core"))
    tp = ("y", "core")
    placed = (
        P("req", tp),
        P(tp),
        P(None, tp),
        P(None, tp),
        P(None, tp),
        P(tp, None),
        P("req", tp),
        P("req", tp),
        P("req", None),
        P("req", None),
        P("req", None),
    )
    return jax.shard_map(
        shards,
        mesh=split_mesh,
        in_specs=placed,
        out_specs=(P("req", tp), P("req", tp, None, None)),
        check_vma=False,
    )
```

```python
import math

import jax
import jax.numpy as jnp
from jax import lax
from jax.experimental import pallas as pl
from jax.experimental.pallas import tpu as pltpu
from jax.sharding import Mesh
from jax.sharding import PartitionSpec as P

HD = 96
HG = 4
PAGE = 128
CAPACITY = 2


EPSILON = 1e-05
THETA = 10000.0


def rotate(values, positions, head_size):
    count = values.shape[0]
    half_size = head_size // 2
    shaped = values.reshape(count, -1, head_size)
    freqs = jnp.exp(-math.log(THETA) * 2.0 * jnp.arange(half_size, dtype=jnp.float32) / head_size)
    angles = positions.astype(jnp.float32)[:, None] * freqs[None, :]
    cosine = jnp.cos(angles)[:, None, :]
    sine = jnp.sin(angles)[:, None, :]
    first = shaped[:, :, :half_size]
    second = shaped[:, :, half_size:]
    turned = jnp.concatenate(
        [first * cosine - second * sine, second * cosine + first * sine], axis=2
    )
    return turned.reshape(count, -1)


def request_ids(lengths, count):
    ends = jnp.cumsum(lengths)
    row_index = jnp.arange(count, dtype=jnp.int32)
    return jnp.sum((row_index[:, None] >= ends[None, :]).astype(jnp.int32), axis=1)


def block_layout(earlier, fresh, count):
    owners = request_ids(fresh, count)
    starts = jnp.cumsum(fresh) - fresh
    onehot = (owners[:, None] == jnp.arange(fresh.shape[0], dtype=jnp.int32)[None, :]).astype(
        jnp.int32
    )
    first_row = jnp.sum(onehot * starts[None, :], axis=1)
    before = jnp.sum(onehot * earlier[None, :], axis=1)
    row_index = jnp.arange(count, dtype=jnp.int32)
    return (owners, before + row_index - first_row)


def visible(earlier, owners, prev_count, count):
    prev_owner = request_ids(earlier, prev_count)
    row_index = jnp.arange(count, dtype=jnp.int32)
    old_part = owners[:, None] == prev_owner[None, :]
    new_part = (owners[:, None] == owners[None, :]) & (row_index[None, :] <= row_index[:, None])
    return jnp.concatenate([old_part, new_part], axis=1)


def rank_in_dest(dests):
    same = (dests[..., :, None] == dests[..., None, :]).astype(jnp.int32)
    count = dests.shape[-1]
    order_index = jnp.arange(count, dtype=jnp.int32)
    earlier_mask = (order_index[None, :] < order_index[:, None]).astype(jnp.int32)
    return jnp.sum(same * earlier_mask, axis=-1)


def pack_pages(slots, sources, parts, slot_total, into=(), shapes=None, paired=()):
    page_total = sources[0].shape[0] // PAGE
    width = sources[0].shape[1]

    def body(slot_ref, *rest):
        blocks = rest[: len(sources)]
        outs = rest[len(rest) - len(parts) :]
        for out, (which, start, rows) in zip(outs, parts):
            out[0] = blocks[which][start : start + rows]

    in_specs = [pl.BlockSpec((PAGE, width), lambda page, slot_ref: (page, 0))] * len(sources)
    in_specs += [pl.BlockSpec(memory_space=pl.ANY)] * len(into)
    if shapes is None:
        shapes = [rows for _, _, rows in parts]
    out_shape = tuple(
        jax.ShapeDtypeStruct(
            (slot_total // CAPACITY if index in paired else slot_total, full, width),
            jnp.bfloat16,
        )
        for index, full in enumerate(shapes)
    )

    def out_map(index):
        if index in paired:
            return lambda page, slot_ref: (
                slot_ref[page] // CAPACITY,
                slot_ref[page] % CAPACITY,
                0,
            )
        return lambda page, slot_ref: (slot_ref[page], 0, 0)

    out_specs = tuple(
        pl.BlockSpec((1, rows, width), out_map(index)) for index, (_, _, rows) in enumerate(parts)
    )
    first_alias = 1 + len(sources)
    return pl.pallas_call(
        body,
        out_shape=out_shape,
        grid_spec=pltpu.PrefetchScalarGridSpec(
            num_scalar_prefetch=1,
            grid=(page_total,),
            in_specs=in_specs,
            out_specs=out_specs,
        ),
        input_output_aliases={first_alias + i: out for i, out in enumerate(into)},
    )(slots, *sources, *into.values())


def stamp_tags(tags, first_row):
    dest_total, tag_rows, width = tags.shape

    def body(tag_block, out):
        out[...] = tag_block[...]

    return pl.pallas_call(
        body,
        out_shape=jax.ShapeDtypeStruct((dest_total, first_row + tag_rows, width), jnp.bfloat16),
        grid=(1,),
        in_specs=[pl.BlockSpec((dest_total, tag_rows, width), lambda step: (0, 0, 0))],
        out_specs=pl.BlockSpec(
            (dest_total, tag_rows, width), lambda step: (0, first_row // tag_rows, 0)
        ),
    )(tags)


def place_pages(
    sources, ranks, received, slot_count, cores, part, row_block, rows, into=(), group=9,
    paired=False,
):
    stored, width = received.shape[-2:]
    if paired:
        shaped = received.reshape(-1, cores, stored, width)
        block = (1, cores, rows, width)
    else:
        shaped = received.reshape(-1, cores, CAPACITY, stored, width)
        block = (1, cores, 1, rows, width)

    def body(src_ref, rank_ref, *refs):
        out = refs[-1]
        for member in range(group):
            for core in range(cores):
                piece = refs[member][0, core] if paired else refs[member][0, core, 0]
                out[member, :, core * width : (core + 1) * width] = piece

    def source_map(member):
        if paired:
            return lambda step, src_ref, rank_ref: (
                src_ref[step * group + member],
                0,
                rank_ref[step * group + member],
                0,
            )
        return lambda step, src_ref, rank_ref: (
            src_ref[step * group + member],
            0,
            rank_ref[step * group + member],
            0,
            0,
        )

    in_specs = [
        pl.BlockSpec(block, source_map(member)) for member in range(group)
    ] + [pl.BlockSpec(memory_space=pl.ANY)] * len(into)
    return pl.pallas_call(
        body,
        out_shape=jax.ShapeDtypeStruct((slot_count, PAGE, 2 * cores * width), jnp.bfloat16),
        grid_spec=pltpu.PrefetchScalarGridSpec(
            num_scalar_prefetch=2,
            grid=(slot_count // group,),
            in_specs=in_specs,
            out_specs=pl.BlockSpec(
                (group, rows, cores * width),
                lambda step, src_ref, rank_ref: (step, row_block, part),
            ),
        ),
        input_output_aliases={2 + group + i: 0 for i in range(len(into))},
    )(sources, ranks, *([shaped] * group), *into)


def shards(
    tokens,
    norm_gain,
    w_query,
    w_key,
    w_value,
    w_out,
    prev_keys,
    prev_values,
    earlier_lengths,
    new_lengths,
    page_table,
):
    token_count, local_width = tokens.shape
    full_width = w_query.shape[0]
    prev_count = prev_keys.shape[0]
    req_count = lax.axis_size("req")
    cores = lax.axis_size("core")
    my_req = lax.axis_index("req")
    my_core = lax.axis_index("core")

    spare = 16
    riders = jnp.zeros((spare, local_width), tokens.dtype).at[0].set(norm_gain)
    gathered = lax.all_gather(
        jnp.concatenate([tokens, riders], axis=0), ("y", "core"), axis=1, tiled=True
    )
    full_tokens = gathered[:token_count]
    full_gain = gathered[token_count]
    widened = full_tokens.astype(jnp.float32)
    mean_square = jnp.mean(widened * widened, axis=1, keepdims=True)
    normed = (widened * lax.rsqrt(mean_square + EPSILON) * full_gain.astype(jnp.float32)[None, :]).astype(
        jnp.bfloat16
    )
    value_raw = jnp.dot(normed, w_value, preferred_element_type=jnp.float32)
    earlier = earlier_lengths[0]
    fresh = new_lengths[0]
    owners, positions = block_layout(earlier, fresh, token_count)
    new_values = value_raw.astype(jnp.bfloat16)

    page_total = (prev_count + token_count) // PAGE
    slot_count = page_total // cores
    dest_count = req_count * cores
    slot_total = dest_count * CAPACITY
    own_dests = page_table[0] // slot_count
    own_ranks = rank_in_dest(own_dests)
    send_slots = (own_dests * CAPACITY + own_ranks).astype(jnp.int32)
    prev_pages = prev_count // PAGE
    whole = ((0, 0, PAGE),)
    halves = ((0, 0, PAGE // 2), (0, PAGE // 2, PAGE // 2))
    both = ((0, 0, PAGE), (1, 0, PAGE // 2), (1, PAGE // 2, PAGE // 2))
    half_rows = PAGE // 2
    tag_rows = 16
    carried = (
        jnp.full((slot_total,), slot_count, jnp.int32)
        .at[send_slots]
        .set((page_table[0] % slot_count).astype(jnp.int32))
    )
    tags = jnp.zeros((dest_count, tag_rows, local_width), jnp.bfloat16)
    tags = tags.at[:, 0, :CAPACITY].set(
        carried.reshape(dest_count, CAPACITY).astype(jnp.bfloat16)
    )
    send_low = stamp_tags(tags, CAPACITY * half_rows)
    send_keys, send_low, send_high = pack_pages(
        send_slots[:prev_pages],
        (prev_keys, prev_values),
        both,
        slot_total,
        into={1: send_low},
        shapes=(PAGE, CAPACITY * half_rows + tag_rows, half_rows),
        paired=(1,),
    )
    send_low, send_high = pack_pages(
        send_slots[prev_pages:],
        (new_values,),
        halves,
        slot_total,
        into={0: send_low, 1: send_high},
        shapes=(CAPACITY * half_rows + tag_rows, half_rows),
        paired=(0,),
    )
    send_keys, send_low, send_high, normed, new_values = lax.optimization_barrier(
        (send_keys, send_low, send_high, normed, new_values)
    )
    received_low = lax.all_to_all(send_low, ("req", "core"), 0, 0, tiled=True)
    carried = received_low[:, CAPACITY * half_rows, :CAPACITY].astype(jnp.int32)
    carried = carried.reshape(req_count, cores, CAPACITY)[:, 0, :].reshape(-1)
    wanted = jnp.arange(slot_count, dtype=jnp.int32)
    found = jnp.argmax(carried[None, :] == wanted[:, None], axis=1).astype(jnp.int32)
    from_req = found // CAPACITY
    from_rank = found % CAPACITY
    key_raw = jnp.dot(normed, w_key, preferred_element_type=jnp.float32)
    new_keys = rotate(key_raw, positions, HD).astype(jnp.bfloat16)
    (send_keys,) = pack_pages(
        send_slots[prev_pages:], (new_keys,), whole, slot_total, into={0: send_keys}
    )
    keys_all = jnp.concatenate([prev_keys, new_keys], axis=0)
    values_all = jnp.concatenate([prev_values, new_values], axis=0)
    query_raw = jnp.dot(normed, w_query, preferred_element_type=jnp.float32)
    queries = rotate(query_raw, positions, HD).astype(jnp.bfloat16)
    received_keys = lax.all_to_all(send_keys, ("req", "core"), 0, 0, tiled=True)

    allowed = visible(earlier, owners, prev_count, token_count)
    heads_here = local_width // HD
    scores = jnp.einsum(
        "qhd,khd->hqk",
        queries.reshape(token_count, heads_here, HD),
        keys_all.reshape(-1, heads_here, HD),
        preferred_element_type=jnp.float32,
    ) * HD ** (-0.5)
    scores = jnp.where(allowed[None, :, :], scores, -1e30)
    row_peak = jnp.max(scores, axis=2, keepdims=True)
    weights = jnp.exp(scores - row_peak)
    totals = jnp.sum(weights, axis=2)
    prob_rows = weights.astype(jnp.bfloat16)
    mixture = jnp.einsum(
        "hqk,khd->qhd",
        prob_rows,
        values_all.reshape(-1, heads_here, HD),
        preferred_element_type=jnp.float32,
    )
    attended = (
        (mixture / totals.T[:, :, None]).astype(jnp.bfloat16).reshape(token_count, local_width)
    )
    projected = jnp.dot(attended, w_out, preferred_element_type=jnp.float32)
    received_keys, received_low, projected, send_high = lax.optimization_barrier(
        (received_keys, received_low, projected, send_high)
    )
    summed = lax.psum_scatter(projected, ("y", "core"), scatter_dimension=1, tiled=True)
    layer_out = (tokens.astype(jnp.float32) + summed).astype(jnp.bfloat16)
    received_high = lax.all_to_all(send_high, ("req", "core"), 0, 0, tiled=True)
    received_high, layer_out = lax.optimization_barrier((received_high, layer_out))
    half_rows = PAGE // 2
    pool = place_pages(from_req, from_rank, received_keys, slot_count, cores, 0, 0, PAGE)
    pool = place_pages(
        from_req, from_rank, received_low, slot_count, cores, 1, 0, half_rows, into=(pool,),
        paired=True,
    )
    pool = place_pages(
        from_req, from_rank, received_high, slot_count, cores, 1, 1, half_rows, into=(pool,),
        group=slot_count,
    )
    return (layer_out, pool[:, None])


def solution(mesh):
    req_count, tp_count = mesh.devices.shape
    cores = tp_count // HG
    split_mesh = Mesh(mesh.devices.reshape(req_count, HG, cores), ("req", "y", "core"))
    tp = ("y", "core")
    placed = (
        P("req", tp),
        P(tp),
        P(None, tp),
        P(None, tp),
        P(None, tp),
        P(tp, None),
        P("req", tp),
        P("req", tp),
        P("req", None),
        P("req", None),
        P("req", None),
    )
    return jax.shard_map(
        shards,
        mesh=split_mesh,
        in_specs=placed,
        out_specs=(P("req", tp), P("req", tp, None, None)),
        check_vma=False,
    )
```
